32 devices in a mesh: gx: 8 (over y, x, core), gy: 4 (over z).
Axes of the slice: x: 2, y: 2, z: 4, core: 2. Of those that a mesh axis runs over, the one named last changes fastest.
Arguments:
- positions: float32 [3, 65536], P(None, ('gx', 'gy')), may hold values from 0 to 8, as said below
- density: float32 [65536], P(('gx', 'gy')), may hold values from 0.5 to 4
- momentum: float32 [3, 65536], P(None, ('gx', 'gy')), may hold values from -3 to 3
- field: float32 [3, 65536], P(None, ('gx', 'gy')), may hold values from -3 to 3
- psi: float32 [65536], P(('gx', 'gy')), may hold values from -3 to 3
- ohmic: float32 [65536], P(('gx', 'gy')), may hold values from 0.05 to 20
- ambipolar: float32 [65536], P(('gx', 'gy')), may hold values from 0.02 to 0.3
- ghost_index: int32 [34816], P(('gx', 'gy')), may hold values from 0 to 2047, as said below
- tile_i: int32 [2048], P(('gx', 'gy')), may hold values from 0 to 15, as said below
- tile_j: int32 [2048], P(('gx', 'gy')), may hold values from 0 to 24, as said below
- tile_count: int32 [32], P(('gx', 'gy')), may hold values from 16 to 64, as said below
Outputs:
- density_new: float32 [65536], P(('gx', 'gy'))
- momentum_new: float32 [3, 65536], P(None, ('gx', 'gy'))
- field_new: float32 [3, 65536], P(None, ('gx', 'gy'))
- psi_new: float32 [65536], P(('gx', 'gy'))
The draws below stay inside these ranges and needn't reach their ends.
Inputs may be any that keep to these rules, and one draw needn't show every extreme that they name: `positions`: x lies in [ix, ix+1) and y in [iy, iy+1) for the owner (ix, iy); z lies in [0, 0.5). `ghost_index`: within one device the 1088 numbers are distinct. `tile_i`: a block of 128 local particles. `tile_j`: a block of 128 in the extended set; the pairs (tile_i, tile_j) of one device are distinct. `tile_count`: the devices of a dense region of three by three slabs use all 64 entries.
All inputs are finite; a program needn't handle non-finite values.
Results may differ from the reference program's by a relative error of at most 0.0003.
Values sent between devices are 32-bit elements; how exact they have to be, the bound alone decides.
No kernel may reach another device: no remote copies, remote signals or barrier semaphores. Data moves between devices by JAX's collectives and lax.ppermute only.
A program may use at most 64 MiB of HBM per device.

```python
import math
import jax
import jax.numpy as jnp
from jax import lax

PART_DEV = 2048
TILE = 128
SECTIONS = 4
GHOST_X = 320
GHOST_Y = 160
GHOST_C = 32
GSEND = 1088
EXT_BLOCKS = 25
TILE_MAX = 64
PARTICLES = 65536
N_GX = 8
N_GY = 4
DEVICES = 32


def ghost_plan(key):
    keys = jax.random.split(jax.random.fold_in(key, 7), DEVICES)
    return jax.vmap(lambda k: jax.random.permutation(k, PART_DEV))(keys).astype(jnp.int32)


def draw_ghost_index(key, part):
    perms = ghost_plan(key)
    return perms[:, :GSEND].reshape(-1).astype(jnp.int32)


def draw_positions(key, part):
    perms = ghost_plan(key)
    rank = jnp.argsort(perms, axis=1).astype(jnp.int32)
    sizes = [GHOST_C, GHOST_X, GHOST_C, GHOST_Y, GHOST_Y, GHOST_C, GHOST_X, GHOST_C]
    bounds = []
    total = 0
    for value in sizes:
        total = total + value
        bounds.append(total)
    which = jnp.zeros(rank.shape, jnp.int32)
    for k in range(7):
        which = which + (rank >= bounds[k]).astype(jnp.int32)
    inside = rank < GSEND
    table_x = jnp.array([-1, -1, -1, 0, 0, 1, 1, 1], jnp.int32)
    table_y = jnp.array([-1, 0, 1, -1, 1, -1, 0, 1], jnp.int32)
    side_x = jnp.where(inside, table_x[which], 0)
    side_y = jnp.where(inside, table_y[which], 0)
    unit = jax.random.uniform(jax.random.fold_in(key, 5), (3, DEVICES, PART_DEV), jnp.float32)

    def placed(value, side):
        return jnp.where(side < 0, 0.25 * value, jnp.where(side > 0, 0.75 + 0.25 * value, value))
    dev = jnp.arange(DEVICES, dtype=jnp.int32)[:, None]
    col_x = (dev // N_GY).astype(jnp.float32)
    col_y = (dev % N_GY).astype(jnp.float32)
    coord_x = col_x + placed(unit[0], side_x)
    coord_y = col_y + placed(unit[1], side_y)
    coord_z = 0.5 * unit[2]
    return jnp.stack([coord_x, coord_y, coord_z]).reshape(3, PARTICLES).astype(jnp.float32)


def tile_lists(key):
    ext_blocks = EXT_BLOCKS
    total = PART_DEV // TILE * ext_blocks
    scores = jax.random.randint(jax.random.fold_in(key, 11), (DEVICES, total), 0, 65536, dtype=jnp.int32)
    scores = scores * total + jnp.arange(total, dtype=jnp.int32)[None, :]
    order = jnp.argsort(scores, axis=1)[:, :TILE_MAX].astype(jnp.int32)
    return ((order // ext_blocks).reshape(-1), (order % ext_blocks).reshape(-1))


def draw_tile_i(key, part):
    return tile_lists(key)[0].astype(jnp.int32)


def draw_tile_j(key, part):
    return tile_lists(key)[1].astype(jnp.int32)


def draw_tile_count(key, part):
    centre_x = jax.random.randint(jax.random.fold_in(key, 23), (), 0, N_GX, dtype=jnp.int32)
    centre_y = jax.random.randint(jax.random.fold_in(key, 29), (), 0, N_GY, dtype=jnp.int32)
    dev = jnp.arange(DEVICES, dtype=jnp.int32)
    core = (jnp.abs(dev // N_GY - centre_x) <= 1) & (jnp.abs(dev % N_GY - centre_y) <= 1)
    lowest = max(1, TILE_MAX // 4)
    far_dev = (centre_x + N_GX // 2) % N_GX * N_GY + (centre_y + N_GY // 2) % N_GY
    base = jax.random.randint(jax.random.fold_in(key, 31), (DEVICES,), lowest, max(lowest, TILE_MAX // 2) + 1, dtype=jnp.int32)
    base = jnp.where(dev == far_dev, lowest, base)
    return jnp.where(core, TILE_MAX, base).astype(jnp.int32)


def levels(key, extent, shards, low, top_value):
    loudness = 1.0
    for axis_at, parts in shards:
        steps = jax.random.uniform(jax.random.fold_in(jax.random.fold_in(key, 6), axis_at), (parts,), jnp.float32, low / len(shards), top_value / len(shards))
        loudness = loudness * jnp.repeat(jnp.exp(steps), extent[axis_at] // parts).reshape((-1,) + (1,) * (len(extent) - 1 - axis_at))
    return loudness


def gaussian(key, shape, width, bound, shards=(), held_as=jnp.bfloat16):
    level = levels(key, shape, shards, -0.22, 0.18) if shards else 1.0
    entries = jax.random.normal(key, shape, jnp.float32) * width * level
    return jnp.minimum(jnp.maximum(entries, -bound), bound).astype(held_as)


def setup_inputs(seed: int = 0) -> dict:
    streams_of = jax.random.split(jax.random.key(seed), 12)
    positions = draw_positions(jax.random.fold_in(streams_of[11], 71), 0)
    density = jnp.clip(jnp.exp(math.log(4.0) - 2.0794415 * jax.random.uniform(streams_of[1], (PARTICLES,), jnp.float32) ** levels(streams_of[1], (PARTICLES,), ((0, 32),), -0.2, 0.2)), 0.5, 4.0)
    momentum = gaussian(streams_of[2], (3, PARTICLES), 0.5, 3.0, ((1, 32),), jnp.float32)
    field = gaussian(streams_of[3], (3, PARTICLES), 0.5, 3.0, ((1, 32),), jnp.float32)
    psi = gaussian(streams_of[4], (PARTICLES,), 0.5, 3.0, ((0, 32),), jnp.float32)
    ohmic = jnp.clip(jnp.exp(math.log(20.0) - 5.9914645 * jax.random.uniform(streams_of[5], (PARTICLES,), jnp.float32) ** levels(streams_of[5], (PARTICLES,), ((0, 32),), -0.2, 0.2)), 0.05, 20.0)
    ambipolar = jnp.clip(jnp.exp(math.log(0.3) - 2.7080503 * jax.random.uniform(streams_of[6], (PARTICLES,), jnp.float32) ** levels(streams_of[6], (PARTICLES,), ((0, 32),), -0.2, 0.2)), 0.02, 0.3)
    ghost_index = draw_ghost_index(jax.random.fold_in(streams_of[11], 71), 0)
    tile_i = draw_tile_i(jax.random.fold_in(streams_of[11], 71), 0)
    tile_j = draw_tile_j(jax.random.fold_in(streams_of[11], 71), 0)
    tile_count = draw_tile_count(jax.random.fold_in(streams_of[11], 71), 0)
    return {"positions": positions, "density": density, "momentum": momentum, "field": field, "psi": psi, "ohmic": ohmic, "ambipolar": ambipolar, "ghost_index": ghost_index, "tile_i": tile_i, "tile_j": tile_j, "tile_count": tile_count}


DIRECTIONS = [(-1, -1), (-1, 0), (-1, 1), (0, -1), (0, 1), (1, -1), (1, 0), (1, 1)]
courant = 0.3
damping = 0.5

def ghost_sizes():
    return [GHOST_C, GHOST_X, GHOST_C, GHOST_Y, GHOST_Y, GHOST_C, GHOST_X, GHOST_C]

def ghost_offsets():
    sizes = ghost_sizes()
    starts = [0]
    for value in sizes[:-1]:
        starts.append(starts[-1] + value)
    return starts

def rkl_table(sections):
    wfirst = 4.0 / (sections * sections + sections - 2)
    bvals = [1.0 / 3.0, 1.0 / 3.0, 1.0 / 3.0] + [(j * j + j - 2) / (2.0 * j * (j + 1)) for j in range(3, sections + 1)]
    first = bvals[1] * wfirst
    rows = []
    for j in range(2, sections + 1):
        mu_j = (2.0 * j - 1.0) / j * bvals[j] / bvals[j - 1]
        nu_j = -(j - 1.0) / j * bvals[j] / bvals[j - 2]
        mut_j = mu_j * wfirst
        rows.append((mu_j, nu_j, mut_j, -(1.0 - bvals[j - 1]) * mut_j))
    return (first, rows)

def kernel_tile(near, far):
    dist = (near[0][..., :, None] - far[0][..., None, :]) ** 2
    dist = dist + (near[1][..., :, None] - far[1][..., None, :]) ** 2
    dist = dist + (near[2][..., :, None] - far[2][..., None, :]) ** 2
    base = jnp.maximum(1.0 - 4.0 * dist, 0.0)
    return base * base

def flux_rows(ext, ch):
    posit = ext[0:3]
    live = ext[3]
    rho = ext[4]
    vel = ext[5:8]
    bfl = ext[8:11]
    cpsi = ext[11]
    speed = ext[12]
    mom = rho * vel
    ptot = rho + 0.5 * lax.optimization_barrier(jnp.sum(bfl * bfl, axis=0))
    fluxes = []
    for d in range(3):
        rows_d = [mom[d]]
        for k in range(3):
            term = mom[k] * vel[d] - bfl[k] * bfl[d]
            rows_d.append(term + ptot if k == d else term)
        for k in range(3):
            term = vel[d] * bfl[k] - bfl[d] * vel[k]
            rows_d.append(term + cpsi if k == d else term)
        rows_d.append(ch * ch * bfl[d])
        fluxes.append(jnp.stack(rows_d))
    flux = jnp.stack(fluxes)
    state = jnp.concatenate([rho[None], mom, bfl, cpsi[None]], axis=0)
    gsum = posit[0] * flux[0] + posit[1] * flux[1] + posit[2] * flux[2]
    return jnp.concatenate([live[None], posit, flux.reshape(24, -1), gsum, speed * state, speed[None], state], axis=0)

def add_tile(acc, weight, qblock, start):
    part = lax.dot_general(qblock, weight, (((1,), (1,)), ((), ())), precision=lax.Precision.HIGHEST, preferred_element_type=jnp.float32)
    cur = lax.dynamic_slice_in_dim(acc, start, TILE, 1)
    return lax.dynamic_update_slice_in_dim(acc, cur + part, start, 1)

def accumulate(qext, pos_ext, tiles_i, tiles_j, count, nlocal):

    def step(t, acc):
        start_i = (tiles_i[t] * TILE).astype(jnp.int32)
        start_j = (tiles_j[t] * TILE).astype(jnp.int32)
        near = lax.dynamic_slice_in_dim(pos_ext, start_i, TILE, 1)
        far = lax.dynamic_slice_in_dim(pos_ext, start_j, TILE, 1)
        weight = kernel_tile(near, far)
        qblock = lax.dynamic_slice_in_dim(qext, start_j, TILE, 1)
        return add_tile(acc, weight, qblock, start_i)
    acc = jnp.zeros((qext.shape[0], nlocal), jnp.float32)
    return lax.fori_loop(0, count, step, acc)

def hydro_rate(acc, local):
    count_n = acc[0]
    num = acc.shape[1]
    wflux = acc[4:28].reshape(3, 8, num)
    flux = local[4:28].reshape(3, 8, num)
    posit = local[1:4]
    speed = local[44]
    state = local[45:53]
    central = acc[28:36]
    for d in range(3):
        central = central + flux[d] * (acc[1 + d] - posit[d] * count_n) - posit[d] * wflux[d]
    dissip = speed * (acc[45:53] - state * count_n) + acc[36:44] - state * acc[44]
    return ((0.5 * dissip - 0.5 * central) / (1.0 + count_n), count_n)

def diffusion_rate(acc, bloc, etaloc, count_n):
    return 0.5 * (etaloc * (acc[0:3] - bloc * count_n) + acc[3:6] - bloc * acc[6]) / (1.0 + count_n)

def reference(positions, density, momentum, field, psi, ohmic, ambipolar, ghost_index, tile_i, tile_j, tile_count):
    ndev = N_GX * N_GY
    sizes = ghost_sizes()
    starts = ghost_offsets()

    def per_dev(rows):
        return rows.reshape(rows.shape[0], ndev, PART_DEV).transpose(1, 0, 2)

    def to_global(rows):
        return rows.transpose(1, 0, 2).reshape(rows.shape[1], ndev * PART_DEV)
    gidx = ghost_index.reshape(N_GX, N_GY, GSEND)

    def assemble(dev_rows):
        nrow = dev_rows.shape[1]
        grid = dev_rows.reshape(N_GX, N_GY, nrow, PART_DEV)
        pieces = []
        for p, q in DIRECTIONS:
            dsend = DIRECTIONS.index((-p, -q))
            segment = gidx[:, :, starts[dsend]:starts[dsend] + sizes[dsend]]
            idx = jnp.broadcast_to(segment[:, :, None, :], (N_GX, N_GY, nrow, sizes[dsend]))
            sent = jnp.take_along_axis(grid, idx, axis=3)
            padded = jnp.pad(sent, ((1, 1), (1, 1), (0, 0), (0, 0)))
            pieces.append(padded[1 + p:1 + p + N_GX, 1 + q:1 + q + N_GY])
        ghosts = jnp.concatenate(pieces, axis=3).reshape(ndev, nrow, GSEND)
        filler = jnp.zeros((ndev, nrow, EXT_BLOCKS * TILE - PART_DEV - GSEND), jnp.float32)
        return jnp.concatenate([dev_rows, ghosts, filler], axis=2)
    velocity = momentum / density
    speed = jnp.sqrt(1.0 + lax.optimization_barrier(jnp.sum(field * field, axis=0)) / density)
    ch = jnp.max(speed)
    dt = courant / ch
    fac = ambipolar / (density * jnp.sqrt(density))
    live = jnp.ones_like(density)
    payload = jnp.concatenate([positions, live[None], density[None], velocity, field, psi[None], speed[None], ohmic[None], fac[None]], axis=0)
    ext = assemble(per_dev(payload))
    tiles_i = tile_i.reshape(ndev, TILE_MAX)
    tiles_j = tile_j.reshape(ndev, TILE_MAX)

    def hydro_one(args):
        ext_d, ti_d, tj_d, cnt = args
        qext = flux_rows(ext_d, ch)
        acc = accumulate(qext, ext_d[0:3], ti_d, tj_d, cnt, PART_DEV)
        return hydro_rate(acc, qext[:, :PART_DEV])
    rates, counts = lax.map(hydro_one, (ext, tiles_i, tiles_j, tile_count))
    rate = to_global(rates)
    count_n = counts.reshape(ndev * PART_DEV)
    density_new = density + dt * rate[0]
    momentum_new = momentum + dt * rate[1:4]
    yzero = field + dt * rate[4:7]
    psi_new = (psi + dt * rate[7]) * jnp.exp(-damping * dt * ch)
    pos_ext = ext[:, 0:3]

    def operator(bfl):
        eta = ohmic + fac * lax.optimization_barrier(jnp.sum(bfl * bfl, axis=0))
        ext2 = assemble(per_dev(jnp.concatenate([bfl, eta[None]], axis=0)))

        def one(args):
            e2, pe, ti_d, tj_d, cnt = args
            qext = jnp.concatenate([e2[0:3], e2[3][None] * e2[0:3], e2[3][None]], axis=0)
            return accumulate(qext, pe, ti_d, tj_d, cnt, PART_DEV)
        acc = to_global(lax.map(one, (ext2, pos_ext, tiles_i, tiles_j, tile_count)))
        return diffusion_rate(acc, bfl, eta, count_n)
    first, rows = rkl_table(SECTIONS)
    lzero = operator(yzero)
    older = yzero
    prev = yzero + first * dt * lzero
    for mu_j, nu_j, mut_j, gam_j in rows:
        nxt = mu_j * prev + nu_j * older + (1.0 - mu_j - nu_j) * yzero + mut_j * dt * operator(prev) + gam_j * dt * lzero
        older = prev
        prev = nxt
    return (density_new, momentum_new, prev, psi_new)
```

```python
import math

import jax
import jax.numpy as jnp
from jax import lax
from jax.sharding import PartitionSpec as P

TILE = 128
SECTIONS = 4
GHOST_X = 320
GHOST_Y = 160
GHOST_C = 32
EXT_BLOCKS = 25


DIRECTIONS = [(-1, -1), (-1, 0), (-1, 1), (0, -1), (0, 1), (1, -1), (1, 0), (1, 1)]
courant = 0.3
damping = 0.5


def extended(array, sides, width):
    for axis, dim in sides:
        size, length = (lax.axis_size(axis), array.shape[dim])
        up = [(i, (i + 1) % size) for i in range(size - 1)]
        down = [(j, i) for i, j in up]
        last = lax.slice_in_dim(array, length - width, length, axis=dim)
        leading = lax.slice_in_dim(array, 0, width, axis=dim)
        before = lax.ppermute(last, axis, up)
        after = lax.ppermute(leading, axis, down)
        array = jnp.concatenate([before, array, after], axis=dim)
    return array


def mesh_max(value):
    for axis in ("gy", "gx"):
        size = lax.axis_size(axis)
        shift = 1
        while shift < size:
            pairs = [(i, (i + shift) % size) for i in range(size)]
            value = jnp.maximum(value, lax.ppermute(value, axis, pairs))
            shift = shift * 2
    return value


def ghost_sizes():
    return [GHOST_C, GHOST_X, GHOST_C, GHOST_Y, GHOST_Y, GHOST_C, GHOST_X, GHOST_C]


def ghost_offsets():
    sizes = ghost_sizes()
    starts = [0]
    for value in sizes[:-1]:
        starts.append(starts[-1] + value)
    return starts


def rkl_table(sections):
    wfirst = 4.0 / (sections * sections + sections - 2)
    bvals = [1.0 / 3.0, 1.0 / 3.0, 1.0 / 3.0] + [
        (j * j + j - 2) / (2.0 * j * (j + 1)) for j in range(3, sections + 1)
    ]
    first = bvals[1] * wfirst
    rows = []
    for j in range(2, sections + 1):
        mu_j = (2.0 * j - 1.0) / j * bvals[j] / bvals[j - 1]
        nu_j = -(j - 1.0) / j * bvals[j] / bvals[j - 2]
        mut_j = mu_j * wfirst
        rows.append((mu_j, nu_j, mut_j, -(1.0 - bvals[j - 1]) * mut_j))
    return (first, rows)


def kernel_tile(near, far):
    dist = (near[0][..., :, None] - far[0][..., None, :]) ** 2
    dist = dist + (near[1][..., :, None] - far[1][..., None, :]) ** 2
    dist = dist + (near[2][..., :, None] - far[2][..., None, :]) ** 2
    base = jnp.maximum(1.0 - 4.0 * dist, 0.0)
    return base * base


def flux_rows(ext):
    posit = ext[0:3]
    live = ext[3]
    rho = ext[4]
    vel = ext[5:8]
    bfl = ext[8:11]
    cpsi = ext[11]
    speed = ext[12]
    mom = rho * vel
    ptot = rho + 0.5 * jnp.sum(bfl * bfl, axis=0)
    fluxes = []
    for d in range(3):
        rows_d = [mom[d]]
        for k in range(3):
            term = mom[k] * vel[d] - bfl[k] * bfl[d]
            rows_d.append(term + ptot if k == d else term)
        for k in range(3):
            term = vel[d] * bfl[k] - bfl[d] * vel[k]
            rows_d.append(term + cpsi if k == d else term)
        rows_d.append(bfl[d])
        fluxes.append(jnp.stack(rows_d))
    flux = jnp.stack(fluxes)
    state = jnp.concatenate([rho[None], mom, bfl, cpsi[None]], axis=0)
    gsum = posit[0] * flux[0] + posit[1] * flux[1] + posit[2] * flux[2]
    return jnp.concatenate(
        [live[None], posit, flux.reshape(24, -1), gsum, speed * state, speed[None], state], axis=0
    )


def hydro_rate(acc, local, ch):
    count_n = acc[0]
    num = acc.shape[1]
    wflux = acc[4:28].reshape(3, 8, num)
    flux = local[4:28].reshape(3, 8, num)
    posit = local[1:4]
    speed = local[44]
    state = local[45:53]
    central = acc[28:36]
    for d in range(3):
        central = central + flux[d] * (acc[1 + d] - posit[d] * count_n) - posit[d] * wflux[d]
    central = jnp.concatenate([central[:7], (ch * ch) * central[7:8]], axis=0)
    dissip = speed * (acc[45:53] - state * count_n) + acc[36:44] - state * acc[44]
    return ((0.5 * dissip - 0.5 * central) / (1.0 + count_n), count_n)


def diffusion_rate(acc, bloc, etaloc, count_n):
    return 0.5 * (etaloc * (acc[0:3] - bloc * count_n) + acc[3:6] - bloc * acc[6]) / (1.0 + count_n)


def spread_ghosts(rows, ghost_index):
    sizes = ghost_sizes()
    starts = ghost_offsets()
    nx, ny = (lax.axis_size("gx"), lax.axis_size("gy"))
    sent = jnp.take(rows, ghost_index, axis=1)
    got = {}
    for d, (u, v) in enumerate(DIRECTIONS):
        pairs = [
            (ix * ny + iy, (ix + u) * ny + iy + v)
            for ix in range(nx)
            for iy in range(ny)
            if 0 <= ix + u < nx and 0 <= iy + v < ny
        ]
        segment = sent[:, starts[d] : starts[d] + sizes[d]]
        got[-u, -v] = lax.ppermute(segment, ("gx", "gy"), pairs)
    return jnp.concatenate([got[p, q] for p, q in DIRECTIONS], axis=1)


def extend(rows, extra):
    filler = jnp.zeros(
        (rows.shape[0], EXT_BLOCKS * TILE - rows.shape[1] - extra.shape[1]), jnp.float32
    )
    return jnp.concatenate([rows, extra, filler], axis=1)


def shards(
    positions,
    density,
    momentum,
    field,
    psi,
    ohmic,
    ambipolar,
    ghost_index,
    tile_i,
    tile_j,
    tile_count,
):
    nlocal = density.shape[0]
    nblocks = nlocal // TILE
    velocity = momentum / density
    speed = jnp.sqrt(1.0 + jnp.sum(field * field, axis=0) / density)
    fac = ambipolar / (density * jnp.sqrt(density))
    live = jnp.ones_like(density)
    core_rows = [positions, live[None], density[None], velocity, field, psi[None], speed[None]]
    payload = jnp.concatenate(core_rows + [ohmic[None], fac[None]], axis=0)
    ch = mesh_max(jnp.max(speed))
    dt = courant / ch
    ghosts = spread_ghosts(payload, ghost_index)
    ext = extend(payload, ghosts)
    pos_blocks = ext[0:3].reshape(3, EXT_BLOCKS, TILE)
    qext = flux_rows(ext)
    q_blocks = qext.reshape(qext.shape[0], EXT_BLOCKS, TILE)
    count = tile_count[0]
    tiles_total = tile_i.shape[0]
    batch = math.gcd(32, tiles_total)
    rounds = (count + batch - 1) // batch
    block_ids = jnp.arange(nblocks, dtype=jnp.int32)

    def batch_lists(offset):
        near_ids = lax.dynamic_slice_in_dim(tile_i, offset, batch, 0)
        far_ids = lax.dynamic_slice_in_dim(tile_j, offset, batch, 0)
        usable = offset + jnp.arange(batch, dtype=jnp.int32) < count
        onehot = ((near_ids[None, :] == block_ids[:, None]) & usable[None, :]).astype(jnp.float32)
        return (near_ids, far_ids, onehot)

    def fold_batch(acc, blocks, weight, far_ids, onehot):
        qsel = jnp.take(blocks, far_ids, axis=1)
        part = jnp.einsum(
            "rtb,tab->rta",
            qsel,
            weight,
            precision=lax.Precision.HIGHEST,
            preferred_element_type=jnp.float32,
        )
        return acc + jnp.einsum(
            "pt,rta->rpa",
            onehot,
            part,
            precision=lax.Precision.HIGHEST,
            preferred_element_type=jnp.float32,
        )

    def hydro_step(turn, carry):
        acc, stored = carry
        offset = (turn * batch).astype(jnp.int32)
        near_ids, far_ids, onehot = batch_lists(offset)
        near = jnp.take(pos_blocks, near_ids, axis=1)
        far = jnp.take(pos_blocks, far_ids, axis=1)
        weight = kernel_tile(near, far)
        stored = lax.dynamic_update_slice_in_dim(stored, weight, offset, 0)
        return (fold_batch(acc, q_blocks, weight, far_ids, onehot), stored)

    acc_start = jnp.zeros((qext.shape[0], nblocks, TILE), jnp.float32)
    stored_start = jnp.zeros((tiles_total, TILE, TILE), jnp.float32)
    acc, stored = lax.fori_loop(0, rounds, hydro_step, (acc_start, stored_start))
    acc = acc.reshape(qext.shape[0], nlocal)
    rate, count_n = hydro_rate(acc, qext[:, :nlocal], ch)
    density_new = density + dt * rate[0]
    momentum_new = momentum + dt * rate[1:4]
    yzero = field + dt * rate[4:7]
    psi_new = (psi + dt * rate[7]) * jnp.exp(-damping * dt * ch)

    def operator(bfl):
        eta = ohmic + fac * jnp.sum(bfl * bfl, axis=0)
        ghost_b = spread_ghosts(bfl, ghost_index)
        ghost_eta = ghosts[13] + ghosts[14] * jnp.sum(ghost_b * ghost_b, axis=0)
        b_ext = extend(bfl, ghost_b)
        eta_ext = extend(eta[None], ghost_eta[None])[0]
        qdiff = jnp.concatenate([b_ext, eta_ext[None] * b_ext, eta_ext[None]], axis=0)
        diff_blocks = qdiff.reshape(7, EXT_BLOCKS, TILE)

        def diff_step(turn, acc_diff):
            offset = (turn * batch).astype(jnp.int32)
            near_ids, far_ids, onehot = batch_lists(offset)
            weight = lax.dynamic_slice_in_dim(stored, offset, batch, 0)
            return fold_batch(acc_diff, diff_blocks, weight, far_ids, onehot)

        acc_diff = lax.fori_loop(0, rounds, diff_step, jnp.zeros((7, nblocks, TILE), jnp.float32))
        return diffusion_rate(acc_diff.reshape(7, nlocal), bfl, eta, count_n)

    first, rows = rkl_table(SECTIONS)
    lzero = operator(yzero)
    older = yzero
    prev = yzero + first * dt * lzero
    for mu_j, nu_j, mut_j, gam_j in rows:
        nxt = (
            mu_j * prev
            + nu_j * older
            + (1.0 - mu_j - nu_j) * yzero
            + mut_j * dt * operator(prev)
            + gam_j * dt * lzero
        )
        older = prev
        prev = nxt
    return (density_new, momentum_new, prev, psi_new)


def solution(mesh):
    placed = (
        P(None, ("gx", "gy")),
        P(("gx", "gy")),
        P(None, ("gx", "gy")),
        P(None, ("gx", "gy")),
        P(("gx", "gy")),
        P(("gx", "gy")),
        P(("gx", "gy")),
        P(("gx", "gy")),
        P(("gx", "gy")),
        P(("gx", "gy")),
        P(("gx", "gy")),
    )
    return jax.shard_map(
        shards,
        mesh=mesh,
        in_specs=placed,
        out_specs=(P(("gx", "gy")), P(None, ("gx", "gy")), P(None, ("gx", "gy")), P(("gx", "gy"))),
        check_vma=False,
    )
```

```python
import math

import jax
import jax.numpy as jnp
from jax import lax
from jax.sharding import PartitionSpec as P

TILE = 128
SECTIONS = 4
GHOST_X = 320
GHOST_Y = 160
GHOST_C = 32
EXT_BLOCKS = 25


DIRECTIONS = [(-1, -1), (-1, 0), (-1, 1), (0, -1), (0, 1), (1, -1), (1, 0), (1, 1)]
courant = 0.3
damping = 0.5


def extended(array, sides, width):
    for axis, dim in sides:
        size, length = (lax.axis_size(axis), array.shape[dim])
        up = [(i, (i + 1) % size) for i in range(size - 1)]
        down = [(j, i) for i, j in up]
        last = lax.slice_in_dim(array, length - width, length, axis=dim)
        leading = lax.slice_in_dim(array, 0, width, axis=dim)
        before = lax.ppermute(last, axis, up)
        after = lax.ppermute(leading, axis, down)
        array = jnp.concatenate([before, array, after], axis=dim)
    return array


def mesh_max(value):
    for axis in ("gy", "gx"):
        size = lax.axis_size(axis)
        shift = 1
        while shift < size:
            pairs = [(i, (i + shift) % size) for i in range(size)]
            value = jnp.maximum(value, lax.ppermute(value, axis, pairs))
            shift = shift * 2
    return value


def ghost_sizes():
    return [GHOST_C, GHOST_X, GHOST_C, GHOST_Y, GHOST_Y, GHOST_C, GHOST_X, GHOST_C]


def ghost_offsets():
    sizes = ghost_sizes()
    starts = [0]
    for value in sizes[:-1]:
        starts.append(starts[-1] + value)
    return starts


def rkl_table(sections):
    wfirst = 4.0 / (sections * sections + sections - 2)
    bvals = [1.0 / 3.0, 1.0 / 3.0, 1.0 / 3.0] + [
        (j * j + j - 2) / (2.0 * j * (j + 1)) for j in range(3, sections + 1)
    ]
    first = bvals[1] * wfirst
    rows = []
    for j in range(2, sections + 1):
        mu_j = (2.0 * j - 1.0) / j * bvals[j] / bvals[j - 1]
        nu_j = -(j - 1.0) / j * bvals[j] / bvals[j - 2]
        mut_j = mu_j * wfirst
        rows.append((mu_j, nu_j, mut_j, -(1.0 - bvals[j - 1]) * mut_j))
    return (first, rows)


def kernel_tile(near, far):
    dist = (near[0][..., :, None] - far[0][..., None, :]) ** 2
    dist = dist + (near[1][..., :, None] - far[1][..., None, :]) ** 2
    dist = dist + (near[2][..., :, None] - far[2][..., None, :]) ** 2
    base = jnp.maximum(1.0 - 4.0 * dist, 0.0)
    return base * base


def flux_rows(ext):
    posit = ext[0:3]
    live = ext[3]
    rho = ext[4]
    vel = ext[5:8]
    bfl = ext[8:11]
    cpsi = ext[11]
    speed = ext[12]
    mom = rho * vel
    ptot = rho + 0.5 * jnp.sum(bfl * bfl, axis=0)
    fluxes = []
    for d in range(3):
        rows_d = [mom[d]]
        for k in range(3):
            term = mom[k] * vel[d] - bfl[k] * bfl[d]
            rows_d.append(term + ptot if k == d else term)
        for k in range(3):
            term = vel[d] * bfl[k] - bfl[d] * vel[k]
            rows_d.append(term + cpsi if k == d else term)
        rows_d.append(bfl[d])
        fluxes.append(jnp.stack(rows_d))
    flux = jnp.stack(fluxes)
    state = jnp.concatenate([rho[None], mom, bfl, cpsi[None]], axis=0)
    gsum = posit[0] * flux[0] + posit[1] * flux[1] + posit[2] * flux[2]
    return jnp.concatenate(
        [live[None], posit, flux.reshape(24, -1), gsum, speed * state, speed[None], state], axis=0
    )


def hydro_rate(acc, local, ch):
    count_n = acc[0]
    num = acc.shape[1]
    wflux = acc[4:28].reshape(3, 8, num)
    flux = local[4:28].reshape(3, 8, num)
    posit = local[1:4]
    speed = local[44]
    state = local[45:53]
    central = acc[28:36]
    for d in range(3):
        central = central + flux[d] * (acc[1 + d] - posit[d] * count_n) - posit[d] * wflux[d]
    central = jnp.concatenate([central[:7], (ch * ch) * central[7:8]], axis=0)
    dissip = speed * (acc[45:53] - state * count_n) + acc[36:44] - state * acc[44]
    return ((0.5 * dissip - 0.5 * central) / (1.0 + count_n), count_n)


def diffusion_rate(acc, bloc, etaloc, count_n):
    return 0.5 * (etaloc * (acc[0:3] - bloc * count_n) + acc[3:6] - bloc * acc[6]) / (1.0 + count_n)


def spread_ghosts(rows, ghost_index):
    sizes = ghost_sizes()
    starts = ghost_offsets()
    sends = [
        jnp.take(rows, ghost_index[starts[d] : starts[d] + sizes[d]], axis=1) for d in range(8)
    ]

    def toward(p, q):
        return sends[DIRECTIONS.index((p, q))]

    got = {}
    face_x = GHOST_X
    corner = GHOST_C
    face_y = GHOST_Y
    toward_low = jnp.concatenate([toward(-1, 0), toward(-1, -1), toward(-1, 1)], axis=1)
    toward_high = jnp.concatenate([toward(1, 0), toward(1, -1), toward(1, 1)], axis=1)
    along_x = extended(jnp.stack([toward_low, toward_high]), (("gx", 0),), 1)
    from_low = along_x[0]
    from_high = along_x[3]
    downward = jnp.concatenate(
        [
            toward(0, -1),
            from_low[:, face_x : face_x + corner],
            from_high[:, face_x : face_x + corner],
        ],
        axis=1,
    )
    upward = jnp.concatenate(
        [toward(0, 1), from_low[:, face_x + corner :], from_high[:, face_x + corner :]], axis=1
    )
    along_y = extended(jnp.stack([downward, upward]), (("gy", 0),), 1)
    from_below = along_y[0]
    from_above = along_y[3]
    got[-1, 0] = from_low[:, :face_x]
    got[1, 0] = from_high[:, :face_x]
    got[0, -1] = from_below[:, :face_y]
    got[0, 1] = from_above[:, :face_y]
    got[-1, -1] = from_below[:, face_y : face_y + corner]
    got[1, -1] = from_below[:, face_y + corner :]
    got[-1, 1] = from_above[:, face_y : face_y + corner]
    got[1, 1] = from_above[:, face_y + corner :]
    return jnp.concatenate([got[p, q] for p, q in DIRECTIONS], axis=1)


def extend(rows, extra):
    filler = jnp.zeros(
        (rows.shape[0], EXT_BLOCKS * TILE - rows.shape[1] - extra.shape[1]), jnp.float32
    )
    return jnp.concatenate([rows, extra, filler], axis=1)


def shards(
    positions,
    density,
    momentum,
    field,
    psi,
    ohmic,
    ambipolar,
    ghost_index,
    tile_i,
    tile_j,
    tile_count,
):
    nlocal = density.shape[0]
    nblocks = nlocal // TILE
    velocity = momentum / density
    speed = jnp.sqrt(1.0 + jnp.sum(field * field, axis=0) / density)
    fac = ambipolar / (density * jnp.sqrt(density))
    live = jnp.ones_like(density)
    core_rows = [positions, live[None], density[None], velocity, field, psi[None], speed[None]]
    payload = jnp.concatenate(core_rows + [ohmic[None], fac[None]], axis=0)
    ch = mesh_max(jnp.max(speed))
    dt = courant / ch
    ghosts = spread_ghosts(payload, ghost_index)
    ext = extend(payload, ghosts)
    pos_blocks = ext[0:3].reshape(3, EXT_BLOCKS, TILE)
    qext = flux_rows(ext)
    q_blocks = qext.reshape(qext.shape[0], EXT_BLOCKS, TILE)
    count = tile_count[0]
    tiles_total = tile_i.shape[0]
    batch = math.gcd(32, tiles_total)
    rounds = (count + batch - 1) // batch
    block_ids = jnp.arange(nblocks, dtype=jnp.int32)

    def batch_lists(offset):
        near_ids = lax.dynamic_slice_in_dim(tile_i, offset, batch, 0)
        far_ids = lax.dynamic_slice_in_dim(tile_j, offset, batch, 0)
        usable = offset + jnp.arange(batch, dtype=jnp.int32) < count
        onehot = ((near_ids[None, :] == block_ids[:, None]) & usable[None, :]).astype(jnp.float32)
        return (near_ids, far_ids, onehot)

    def fold_batch(acc, blocks, weight, far_ids, onehot):
        qsel = jnp.take(blocks, far_ids, axis=1)
        part = jnp.einsum(
            "rtb,tab->rta",
            qsel,
            weight,
            precision=lax.Precision.HIGHEST,
            preferred_element_type=jnp.float32,
        )
        return acc + jnp.einsum(
            "pt,rta->rpa",
            onehot,
            part,
            precision=lax.Precision.HIGHEST,
            preferred_element_type=jnp.float32,
        )

    def hydro_step(turn, carry):
        acc, stored = carry
        offset = (turn * batch).astype(jnp.int32)
        near_ids, far_ids, onehot = batch_lists(offset)
        near = jnp.take(pos_blocks, near_ids, axis=1)
        far = jnp.take(pos_blocks, far_ids, axis=1)
        weight = kernel_tile(near, far)
        stored = lax.dynamic_update_slice_in_dim(stored, weight, offset, 0)
        return (fold_batch(acc, q_blocks, weight, far_ids, onehot), stored)

    acc_start = jnp.zeros((qext.shape[0], nblocks, TILE), jnp.float32)
    stored_start = jnp.zeros((tiles_total, TILE, TILE), jnp.float32)
    acc, stored = lax.fori_loop(0, rounds, hydro_step, (acc_start, stored_start))
    acc = acc.reshape(qext.shape[0], nlocal)
    rate, count_n = hydro_rate(acc, qext[:, :nlocal], ch)
    density_new = density + dt * rate[0]
    momentum_new = momentum + dt * rate[1:4]
    yzero = field + dt * rate[4:7]
    psi_new = (psi + dt * rate[7]) * jnp.exp(-damping * dt * ch)

    def operator(bfl):
        eta = ohmic + fac * jnp.sum(bfl * bfl, axis=0)
        ghost_b = spread_ghosts(bfl, ghost_index)
        ghost_eta = ghosts[13] + ghosts[14] * jnp.sum(ghost_b * ghost_b, axis=0)
        b_ext = extend(bfl, ghost_b)
        eta_ext = extend(eta[None], ghost_eta[None])[0]
        qdiff = jnp.concatenate([b_ext, eta_ext[None] * b_ext, eta_ext[None]], axis=0)
        diff_blocks = qdiff.reshape(7, EXT_BLOCKS, TILE)

        def diff_step(turn, acc_diff):
            offset = (turn * batch).astype(jnp.int32)
            near_ids, far_ids, onehot = batch_lists(offset)
            weight = lax.dynamic_slice_in_dim(stored, offset, batch, 0)
            return fold_batch(acc_diff, diff_blocks, weight, far_ids, onehot)

        acc_diff = lax.fori_loop(0, rounds, diff_step, jnp.zeros((7, nblocks, TILE), jnp.float32))
        return diffusion_rate(acc_diff.reshape(7, nlocal), bfl, eta, count_n)

    first, rows = rkl_table(SECTIONS)
    lzero = operator(yzero)
    older = yzero
    prev = yzero + first * dt * lzero
    for mu_j, nu_j, mut_j, gam_j in rows:
        nxt = (
            mu_j * prev
            + nu_j * older
            + (1.0 - mu_j - nu_j) * yzero
            + mut_j * dt * operator(prev)
            + gam_j * dt * lzero
        )
        older = prev
        prev = nxt
    return (density_new, momentum_new, prev, psi_new)


def solution(mesh):
    placed = (
        P(None, ("gx", "gy")),
        P(("gx", "gy")),
        P(None, ("gx", "gy")),
        P(None, ("gx", "gy")),
        P(("gx", "gy")),
        P(("gx", "gy")),
        P(("gx", "gy")),
        P(("gx", "gy")),
        P(("gx", "gy")),
        P(("gx", "gy")),
        P(("gx", "gy")),
    )
    return jax.shard_map(
        shards,
        mesh=mesh,
        in_specs=placed,
        out_specs=(P(("gx", "gy")), P(None, ("gx", "gy")), P(None, ("gx", "gy")), P(("gx", "gy"))),
        check_vma=False,
    )
```

```python
import math

import jax
import jax.numpy as jnp
from jax import lax
from jax.sharding import PartitionSpec as P

TILE = 128
SECTIONS = 4
GHOST_X = 320
GHOST_Y = 160
GHOST_C = 32
EXT_BLOCKS = 25


DIRECTIONS = [(-1, -1), (-1, 0), (-1, 1), (0, -1), (0, 1), (1, -1), (1, 0), (1, 1)]
courant = 0.3
damping = 0.5


def extended(array, sides, width):
    for axis, dim in sides:
        size, length = (lax.axis_size(axis), array.shape[dim])
        up = [(i, (i + 1) % size) for i in range(size - 1)]
        down = [(j, i) for i, j in up]
        last = lax.slice_in_dim(array, length - width, length, axis=dim)
        leading = lax.slice_in_dim(array, 0, width, axis=dim)
        before = lax.ppermute(last, axis, up)
        after = lax.ppermute(leading, axis, down)
        array = jnp.concatenate([before, array, after], axis=dim)
    return array


def mesh_max(value):
    for axis in ("gy", "gx"):
        size = lax.axis_size(axis)
        shift = 1
        while shift < size:
            pairs = [(i, (i + shift) % size) for i in range(size)]
            value = jnp.maximum(value, lax.ppermute(value, axis, pairs))
            shift = shift * 2
    return value


def ghost_sizes():
    return [GHOST_C, GHOST_X, GHOST_C, GHOST_Y, GHOST_Y, GHOST_C, GHOST_X, GHOST_C]


def ghost_offsets():
    sizes = ghost_sizes()
    starts = [0]
    for value in sizes[:-1]:
        starts.append(starts[-1] + value)
    return starts


def rkl_table(sections):
    wfirst = 4.0 / (sections * sections + sections - 2)
    bvals = [1.0 / 3.0, 1.0 / 3.0, 1.0 / 3.0] + [
        (j * j + j - 2) / (2.0 * j * (j + 1)) for j in range(3, sections + 1)
    ]
    first = bvals[1] * wfirst
    rows = []
    for j in range(2, sections + 1):
        mu_j = (2.0 * j - 1.0) / j * bvals[j] / bvals[j - 1]
        nu_j = -(j - 1.0) / j * bvals[j] / bvals[j - 2]
        mut_j = mu_j * wfirst
        rows.append((mu_j, nu_j, mut_j, -(1.0 - bvals[j - 1]) * mut_j))
    return (first, rows)


def kernel_tile(near, far):
    dist = (near[0][..., :, None] - far[0][..., None, :]) ** 2
    dist = dist + (near[1][..., :, None] - far[1][..., None, :]) ** 2
    dist = dist + (near[2][..., :, None] - far[2][..., None, :]) ** 2
    base = jnp.maximum(1.0 - 4.0 * dist, 0.0)
    return base * base


def flux_rows(ext):
    posit = ext[0:3]
    live = ext[3]
    rho = ext[4]
    vel = ext[5:8]
    bfl = ext[8:11]
    cpsi = ext[11]
    speed = ext[12]
    mom = rho * vel
    ptot = rho + 0.5 * jnp.sum(bfl * bfl, axis=0)
    fluxes = []
    for d in range(3):
        rows_d = [mom[d]]
        for k in range(3):
            term = mom[k] * vel[d] - bfl[k] * bfl[d]
            rows_d.append(term + ptot if k == d else term)
        for k in range(3):
            term = vel[d] * bfl[k] - bfl[d] * vel[k]
            rows_d.append(term + cpsi if k == d else term)
        rows_d.append(bfl[d])
        fluxes.append(jnp.stack(rows_d))
    flux = jnp.stack(fluxes)
    state = jnp.concatenate([rho[None], mom, bfl, cpsi[None]], axis=0)
    gsum = posit[0] * flux[0] + posit[1] * flux[1] + posit[2] * flux[2]
    return jnp.concatenate(
        [live[None], posit, flux.reshape(24, -1), gsum, speed * state, speed[None], state], axis=0
    )


def hydro_rate(acc, local, ch):
    count_n = acc[0]
    num = acc.shape[1]
    wflux = acc[4:28].reshape(3, 8, num)
    flux = local[4:28].reshape(3, 8, num)
    posit = local[1:4]
    speed = local[44]
    state = local[45:53]
    central = acc[28:36]
    for d in range(3):
        central = central + flux[d] * (acc[1 + d] - posit[d] * count_n) - posit[d] * wflux[d]
    central = jnp.concatenate([central[:7], (ch * ch) * central[7:8]], axis=0)
    dissip = speed * (acc[45:53] - state * count_n) + acc[36:44] - state * acc[44]
    return ((0.5 * dissip - 0.5 * central) / (1.0 + count_n), count_n)


def diffusion_rate(acc, bloc, etaloc, count_n):
    return 0.5 * (etaloc * (acc[0:3] - bloc * count_n) + acc[3:6] - bloc * acc[6]) / (1.0 + count_n)


def spread_ghosts(rows, ghost_index):
    sizes = ghost_sizes()
    starts = ghost_offsets()
    sends = [
        jnp.take(rows, ghost_index[starts[d] : starts[d] + sizes[d]], axis=1) for d in range(8)
    ]

    def toward(p, q):
        return sends[DIRECTIONS.index((p, q))]

    got = {}
    face_x = GHOST_X
    corner = GHOST_C
    face_y = GHOST_Y
    toward_low = jnp.concatenate([toward(-1, 0), toward(-1, -1), toward(-1, 1)], axis=1)
    toward_high = jnp.concatenate([toward(1, 0), toward(1, -1), toward(1, 1)], axis=1)
    along_x = extended(jnp.stack([toward_low, toward_high]), (("gx", 0),), 1)
    from_low = along_x[0]
    from_high = along_x[3]
    downward = jnp.concatenate(
        [
            toward(0, -1),
            from_low[:, face_x : face_x + corner],
            from_high[:, face_x : face_x + corner],
        ],
        axis=1,
    )
    upward = jnp.concatenate(
        [toward(0, 1), from_low[:, face_x + corner :], from_high[:, face_x + corner :]], axis=1
    )
    along_y = extended(jnp.stack([downward, upward]), (("gy", 0),), 1)
    from_below = along_y[0]
    from_above = along_y[3]
    got[-1, 0] = from_low[:, :face_x]
    got[1, 0] = from_high[:, :face_x]
    got[0, -1] = from_below[:, :face_y]
    got[0, 1] = from_above[:, :face_y]
    got[-1, -1] = from_below[:, face_y : face_y + corner]
    got[1, -1] = from_below[:, face_y + corner :]
    got[-1, 1] = from_above[:, face_y : face_y + corner]
    got[1, 1] = from_above[:, face_y + corner :]
    return jnp.concatenate([got[p, q] for p, q in DIRECTIONS], axis=1)


def extend(rows, extra):
    filler = jnp.zeros(
        (rows.shape[0], EXT_BLOCKS * TILE - rows.shape[1] - extra.shape[1]), jnp.float32
    )
    return jnp.concatenate([rows, extra, filler], axis=1)


def shards(
    positions,
    density,
    momentum,
    field,
    psi,
    ohmic,
    ambipolar,
    ghost_index,
    tile_i,
    tile_j,
    tile_count,
):
    nlocal = density.shape[0]
    nblocks = nlocal // TILE
    velocity = momentum / density
    speed = jnp.sqrt(1.0 + jnp.sum(field * field, axis=0) / density)
    fac = ambipolar / (density * jnp.sqrt(density))
    live = jnp.ones_like(density)
    core_rows = [positions, live[None], density[None], velocity, field, psi[None], speed[None]]
    payload = jnp.concatenate(core_rows + [ohmic[None], fac[None]], axis=0)
    ch = mesh_max(jnp.max(speed))
    dt = courant / ch
    ghosts = spread_ghosts(payload, ghost_index)
    ext = extend(payload, ghosts)
    pos_blocks = ext[0:3].reshape(3, EXT_BLOCKS, TILE)
    qext = flux_rows(ext)
    q_blocks = qext.reshape(qext.shape[0], EXT_BLOCKS, TILE)
    count = tile_count[0]
    tiles_total = tile_i.shape[0]
    batch = math.gcd(32, tiles_total)
    rounds = (count + batch - 1) // batch
    block_ids = jnp.arange(nblocks, dtype=jnp.int32)

    def batch_lists(offset):
        near_ids = lax.dynamic_slice_in_dim(tile_i, offset, batch, 0)
        far_ids = lax.dynamic_slice_in_dim(tile_j, offset, batch, 0)
        usable = offset + jnp.arange(batch, dtype=jnp.int32) < count
        onehot = ((near_ids[None, :] == block_ids[:, None]) & usable[None, :]).astype(jnp.float32)
        return (near_ids, far_ids, onehot)

    def fold_batch(acc, blocks, weight, far_ids, onehot):
        qsel = jnp.take(blocks, far_ids, axis=1)
        part = jnp.einsum(
            "rtb,tab->rta",
            qsel,
            weight,
            precision=lax.Precision.HIGH,
            preferred_element_type=jnp.float32,
        )
        return acc + jnp.einsum(
            "pt,rta->rpa",
            onehot,
            part,
            precision=lax.Precision.HIGHEST,
            preferred_element_type=jnp.float32,
        )

    def hydro_step(turn, carry):
        acc, stored = carry
        offset = (turn * batch).astype(jnp.int32)
        near_ids, far_ids, onehot = batch_lists(offset)
        near = jnp.take(pos_blocks, near_ids, axis=1)
        far = jnp.take(pos_blocks, far_ids, axis=1)
        weight = kernel_tile(near, far)
        stored = lax.dynamic_update_slice_in_dim(stored, weight, offset, 0)
        return (fold_batch(acc, q_blocks, weight, far_ids, onehot), stored)

    acc_start = jnp.zeros((qext.shape[0], nblocks, TILE), jnp.float32)
    stored_start = jnp.zeros((tiles_total, TILE, TILE), jnp.float32)
    acc, stored = lax.fori_loop(0, rounds, hydro_step, (acc_start, stored_start))
    acc = acc.reshape(qext.shape[0], nlocal)
    rate, count_n = hydro_rate(acc, qext[:, :nlocal], ch)
    density_new = density + dt * rate[0]
    momentum_new = momentum + dt * rate[1:4]
    yzero = field + dt * rate[4:7]
    psi_new = (psi + dt * rate[7]) * jnp.exp(-damping * dt * ch)

    def operator(bfl):
        eta = ohmic + fac * jnp.sum(bfl * bfl, axis=0)
        ghost_b = spread_ghosts(bfl, ghost_index)
        ghost_eta = ghosts[13] + ghosts[14] * jnp.sum(ghost_b * ghost_b, axis=0)
        b_ext = extend(bfl, ghost_b)
        eta_ext = extend(eta[None], ghost_eta[None])[0]
        qdiff = jnp.concatenate([b_ext, eta_ext[None] * b_ext, eta_ext[None]], axis=0)
        diff_blocks = qdiff.reshape(7, EXT_BLOCKS, TILE)

        def diff_step(turn, acc_diff):
            offset = (turn * batch).astype(jnp.int32)
            near_ids, far_ids, onehot = batch_lists(offset)
            weight = lax.dynamic_slice_in_dim(stored, offset, batch, 0)
            return fold_batch(acc_diff, diff_blocks, weight, far_ids, onehot)

        acc_diff = lax.fori_loop(0, rounds, diff_step, jnp.zeros((7, nblocks, TILE), jnp.float32))
        return diffusion_rate(acc_diff.reshape(7, nlocal), bfl, eta, count_n)

    first, rows = rkl_table(SECTIONS)
    lzero = operator(yzero)
    older = yzero
    prev = yzero + first * dt * lzero
    for mu_j, nu_j, mut_j, gam_j in rows:
        nxt = (
            mu_j * prev
            + nu_j * older
            + (1.0 - mu_j - nu_j) * yzero
            + mut_j * dt * operator(prev)
            + gam_j * dt * lzero
        )
        older = prev
        prev = nxt
    return (density_new, momentum_new, prev, psi_new)


def solution(mesh):
    placed = (
        P(None, ("gx", "gy")),
        P(("gx", "gy")),
        P(None, ("gx", "gy")),
        P(None, ("gx", "gy")),
        P(("gx", "gy")),
        P(("gx", "gy")),
        P(("gx", "gy")),
        P(("gx", "gy")),
        P(("gx", "gy")),
        P(("gx", "gy")),
        P(("gx", "gy")),
    )
    return jax.shard_map(
        shards,
        mesh=mesh,
        in_specs=placed,
        out_specs=(P(("gx", "gy")), P(None, ("gx", "gy")), P(None, ("gx", "gy")), P(("gx", "gy"))),
        check_vma=False,
    )
```

```python
import math

import jax
import jax.numpy as jnp
from jax import lax
from jax.sharding import PartitionSpec as P

TILE = 128
SECTIONS = 4
GHOST_X = 320
GHOST_Y = 160
GHOST_C = 32
EXT_BLOCKS = 25


DIRECTIONS = [(-1, -1), (-1, 0), (-1, 1), (0, -1), (0, 1), (1, -1), (1, 0), (1, 1)]
courant = 0.3
damping = 0.5


def extended(array, sides, width):
    for axis, dim in sides:
        size, length = (lax.axis_size(axis), array.shape[dim])
        up = [(i, (i + 1) % size) for i in range(size - 1)]
        down = [(j, i) for i, j in up]
        last = lax.slice_in_dim(array, length - width, length, axis=dim)
        leading = lax.slice_in_dim(array, 0, width, axis=dim)
        before = lax.ppermute(last, axis, up)
        after = lax.ppermute(leading, axis, down)
        array = jnp.concatenate([before, array, after], axis=dim)
    return array


def mesh_max(value):
    count = lax.axis_size("gx") * lax.axis_size("gy")
    spread = jnp.full((count, 1), value, jnp.float32)
    return jnp.max(lax.all_to_all(spread, ("gx", "gy"), 0, 0, tiled=True))


def ghost_sizes():
    return [GHOST_C, GHOST_X, GHOST_C, GHOST_Y, GHOST_Y, GHOST_C, GHOST_X, GHOST_C]


def ghost_offsets():
    sizes = ghost_sizes()
    starts = [0]
    for value in sizes[:-1]:
        starts.append(starts[-1] + value)
    return starts


def rkl_table(sections):
    wfirst = 4.0 / (sections * sections + sections - 2)
    bvals = [1.0 / 3.0, 1.0 / 3.0, 1.0 / 3.0] + [
        (j * j + j - 2) / (2.0 * j * (j + 1)) for j in range(3, sections + 1)
    ]
    first = bvals[1] * wfirst
    rows = []
    for j in range(2, sections + 1):
        mu_j = (2.0 * j - 1.0) / j * bvals[j] / bvals[j - 1]
        nu_j = -(j - 1.0) / j * bvals[j] / bvals[j - 2]
        mut_j = mu_j * wfirst
        rows.append((mu_j, nu_j, mut_j, -(1.0 - bvals[j - 1]) * mut_j))
    return (first, rows)


def kernel_tile(near, far):
    dist = (near[0][..., :, None] - far[0][..., None, :]) ** 2
    dist = dist + (near[1][..., :, None] - far[1][..., None, :]) ** 2
    dist = dist + (near[2][..., :, None] - far[2][..., None, :]) ** 2
    base = jnp.maximum(1.0 - 4.0 * dist, 0.0)
    return base * base


def flux_rows(ext):
    posit = ext[0:3]
    live = ext[3]
    rho = ext[4]
    vel = ext[5:8]
    bfl = ext[8:11]
    cpsi = ext[11]
    speed = ext[12]
    mom = rho * vel
    ptot = rho + 0.5 * jnp.sum(bfl * bfl, axis=0)
    fluxes = []
    for d in range(3):
        rows_d = [mom[d]]
        for k in range(3):
            term = mom[k] * vel[d] - bfl[k] * bfl[d]
            rows_d.append(term + ptot if k == d else term)
        for k in range(3):
            term = vel[d] * bfl[k] - bfl[d] * vel[k]
            rows_d.append(term + cpsi if k == d else term)
        rows_d.append(bfl[d])
        fluxes.append(jnp.stack(rows_d))
    flux = jnp.stack(fluxes)
    state = jnp.concatenate([rho[None], mom, bfl, cpsi[None]], axis=0)
    gsum = posit[0] * flux[0] + posit[1] * flux[1] + posit[2] * flux[2]
    return jnp.concatenate(
        [live[None], posit, flux.reshape(24, -1), gsum, speed * state, speed[None], state], axis=0
    )


def hydro_rate(acc, local, ch):
    count_n = acc[0]
    num = acc.shape[1]
    wflux = acc[4:28].reshape(3, 8, num)
    flux = local[4:28].reshape(3, 8, num)
    posit = local[1:4]
    speed = local[44]
    state = local[45:53]
    central = acc[28:36]
    for d in range(3):
        central = central + flux[d] * (acc[1 + d] - posit[d] * count_n) - posit[d] * wflux[d]
    central = jnp.concatenate([central[:7], (ch * ch) * central[7:8]], axis=0)
    dissip = speed * (acc[45:53] - state * count_n) + acc[36:44] - state * acc[44]
    return ((0.5 * dissip - 0.5 * central) / (1.0 + count_n), count_n)


def diffusion_rate(acc, bloc, etaloc, count_n):
    return 0.5 * (etaloc * (acc[0:3] - bloc * count_n) + acc[3:6] - bloc * acc[6]) / (1.0 + count_n)


def spread_ghosts(rows, ghost_index):
    sizes = ghost_sizes()
    starts = ghost_offsets()
    sends = [
        jnp.take(rows, ghost_index[starts[d] : starts[d] + sizes[d]], axis=1) for d in range(8)
    ]

    def toward(p, q):
        return sends[DIRECTIONS.index((p, q))]

    got = {}
    face_x = GHOST_X
    corner = GHOST_C
    face_y = GHOST_Y
    toward_low = jnp.concatenate([toward(-1, 0), toward(-1, -1), toward(-1, 1)], axis=1)
    toward_high = jnp.concatenate([toward(1, 0), toward(1, -1), toward(1, 1)], axis=1)
    along_x = extended(jnp.stack([toward_low, toward_high]), (("gx", 0),), 1)
    from_low = along_x[0]
    from_high = along_x[3]
    downward = jnp.concatenate(
        [
            toward(0, -1),
            from_low[:, face_x : face_x + corner],
            from_high[:, face_x : face_x + corner],
        ],
        axis=1,
    )
    upward = jnp.concatenate(
        [toward(0, 1), from_low[:, face_x + corner :], from_high[:, face_x + corner :]], axis=1
    )
    along_y = extended(jnp.stack([downward, upward]), (("gy", 0),), 1)
    from_below = along_y[0]
    from_above = along_y[3]
    got[-1, 0] = from_low[:, :face_x]
    got[1, 0] = from_high[:, :face_x]
    got[0, -1] = from_below[:, :face_y]
    got[0, 1] = from_above[:, :face_y]
    got[-1, -1] = from_below[:, face_y : face_y + corner]
    got[1, -1] = from_below[:, face_y + corner :]
    got[-1, 1] = from_above[:, face_y : face_y + corner]
    got[1, 1] = from_above[:, face_y + corner :]
    return jnp.concatenate([got[p, q] for p, q in DIRECTIONS], axis=1)


def extend(rows, extra):
    filler = jnp.zeros(
        (rows.shape[0], EXT_BLOCKS * TILE - rows.shape[1] - extra.shape[1]), jnp.float32
    )
    return jnp.concatenate([rows, extra, filler], axis=1)


def shards(
    positions,
    density,
    momentum,
    field,
    psi,
    ohmic,
    ambipolar,
    ghost_index,
    tile_i,
    tile_j,
    tile_count,
):
    nlocal = density.shape[0]
    nblocks = nlocal // TILE
    velocity = momentum / density
    speed = jnp.sqrt(1.0 + jnp.sum(field * field, axis=0) / density)
    fac = ambipolar / (density * jnp.sqrt(density))
    live = jnp.ones_like(density)
    core_rows = [positions, live[None], density[None], velocity, field, psi[None], speed[None]]
    payload = jnp.concatenate(core_rows + [ohmic[None], fac[None]], axis=0)
    ch = mesh_max(jnp.max(speed))
    dt = courant / ch
    ghosts = spread_ghosts(payload, ghost_index)
    ext = extend(payload, ghosts)
    pos_blocks = ext[0:3].reshape(3, EXT_BLOCKS, TILE)
    qext = flux_rows(ext)
    q_blocks = qext.reshape(qext.shape[0], EXT_BLOCKS, TILE)
    count = tile_count[0]
    tiles_total = tile_i.shape[0]
    batch = math.gcd(32, tiles_total)
    rounds = (count + batch - 1) // batch
    block_ids = jnp.arange(nblocks, dtype=jnp.int32)

    def batch_lists(offset):
        near_ids = lax.dynamic_slice_in_dim(tile_i, offset, batch, 0)
        far_ids = lax.dynamic_slice_in_dim(tile_j, offset, batch, 0)
        usable = offset + jnp.arange(batch, dtype=jnp.int32) < count
        onehot = ((near_ids[None, :] == block_ids[:, None]) & usable[None, :]).astype(jnp.float32)
        return (near_ids, far_ids, onehot)

    def fold_batch(acc, blocks, weight, far_ids, onehot):
        qsel = jnp.take(blocks, far_ids, axis=1)
        part = jnp.einsum(
            "rtb,tab->rta",
            qsel,
            weight,
            precision=lax.Precision.HIGH,
            preferred_element_type=jnp.float32,
        )
        return acc + jnp.einsum(
            "pt,rta->rpa",
            onehot,
            part,
            precision=lax.Precision.HIGHEST,
            preferred_element_type=jnp.float32,
        )

    def hydro_step(turn, carry):
        acc, stored = carry
        offset = (turn * batch).astype(jnp.int32)
        near_ids, far_ids, onehot = batch_lists(offset)
        near = jnp.take(pos_blocks, near_ids, axis=1)
        far = jnp.take(pos_blocks, far_ids, axis=1)
        weight = kernel_tile(near, far)
        stored = lax.dynamic_update_slice_in_dim(stored, weight, offset, 0)
        return (fold_batch(acc, q_blocks, weight, far_ids, onehot), stored)

    acc_start = jnp.zeros((qext.shape[0], nblocks, TILE), jnp.float32)
    stored_start = jnp.zeros((tiles_total, TILE, TILE), jnp.float32)
    acc, stored = lax.fori_loop(0, rounds, hydro_step, (acc_start, stored_start))
    acc = acc.reshape(qext.shape[0], nlocal)
    rate, count_n = hydro_rate(acc, qext[:, :nlocal], ch)
    density_new = density + dt * rate[0]
    momentum_new = momentum + dt * rate[1:4]
    yzero = field + dt * rate[4:7]
    psi_new = (psi + dt * rate[7]) * jnp.exp(-damping * dt * ch)

    def operator(bfl):
        eta = ohmic + fac * jnp.sum(bfl * bfl, axis=0)
        ghost_b = spread_ghosts(bfl, ghost_index)
        ghost_eta = ghosts[13] + ghosts[14] * jnp.sum(ghost_b * ghost_b, axis=0)
        b_ext = extend(bfl, ghost_b)
        eta_ext = extend(eta[None], ghost_eta[None])[0]
        qdiff = jnp.concatenate([b_ext, eta_ext[None] * b_ext, eta_ext[None]], axis=0)
        diff_blocks = qdiff.reshape(7, EXT_BLOCKS, TILE)

        def diff_step(turn, acc_diff):
            offset = (turn * batch).astype(jnp.int32)
            near_ids, far_ids, onehot = batch_lists(offset)
            weight = lax.dynamic_slice_in_dim(stored, offset, batch, 0)
            return fold_batch(acc_diff, diff_blocks, weight, far_ids, onehot)

        acc_diff = lax.fori_loop(0, rounds, diff_step, jnp.zeros((7, nblocks, TILE), jnp.float32))
        return diffusion_rate(acc_diff.reshape(7, nlocal), bfl, eta, count_n)

    first, rows = rkl_table(SECTIONS)
    lzero = operator(yzero)
    older = yzero
    prev = yzero + first * dt * lzero
    for mu_j, nu_j, mut_j, gam_j in rows:
        nxt = (
            mu_j * prev
            + nu_j * older
            + (1.0 - mu_j - nu_j) * yzero
            + mut_j * dt * operator(prev)
            + gam_j * dt * lzero
        )
        older = prev
        prev = nxt
    return (density_new, momentum_new, prev, psi_new)


def solution(mesh):
    placed = (
        P(None, ("gx", "gy")),
        P(("gx", "gy")),
        P(None, ("gx", "gy")),
        P(None, ("gx", "gy")),
        P(("gx", "gy")),
        P(("gx", "gy")),
        P(("gx", "gy")),
        P(("gx", "gy")),
        P(("gx", "gy")),
        P(("gx", "gy")),
        P(("gx", "gy")),
    )
    return jax.shard_map(
        shards,
        mesh=mesh,
        in_specs=placed,
        out_specs=(P(("gx", "gy")), P(None, ("gx", "gy")), P(None, ("gx", "gy")), P(("gx", "gy"))),
        check_vma=False,
    )
```

```python
import math

import jax
import jax.numpy as jnp
from jax import lax
from jax.sharding import PartitionSpec as P

TILE = 128
SECTIONS = 4
GHOST_X = 320
GHOST_Y = 160
GHOST_C = 32
EXT_BLOCKS = 25


DIRECTIONS = [(-1, -1), (-1, 0), (-1, 1), (0, -1), (0, 1), (1, -1), (1, 0), (1, 1)]
courant = 0.3
damping = 0.5


def extended(array, sides, width):
    for axis, dim in sides:
        size, length = (lax.axis_size(axis), array.shape[dim])
        up = [(i, (i + 1) % size) for i in range(size - 1)]
        down = [(j, i) for i, j in up]
        last = lax.slice_in_dim(array, length - width, length, axis=dim)
        leading = lax.slice_in_dim(array, 0, width, axis=dim)
        before = lax.ppermute(last, axis, up)
        after = lax.ppermute(leading, axis, down)
        array = jnp.concatenate([before, array, after], axis=dim)
    return array


def mesh_max(value):
    count = lax.axis_size("gx") * lax.axis_size("gy")
    spread = jnp.full((count, 1), value, jnp.float32)
    return jnp.max(lax.all_to_all(spread, ("gx", "gy"), 0, 0, tiled=True))


def ghost_sizes():
    return [GHOST_C, GHOST_X, GHOST_C, GHOST_Y, GHOST_Y, GHOST_C, GHOST_X, GHOST_C]


def ghost_offsets():
    sizes = ghost_sizes()
    starts = [0]
    for value in sizes[:-1]:
        starts.append(starts[-1] + value)
    return starts


def rkl_table(sections):
    wfirst = 4.0 / (sections * sections + sections - 2)
    bvals = [1.0 / 3.0, 1.0 / 3.0, 1.0 / 3.0] + [
        (j * j + j - 2) / (2.0 * j * (j + 1)) for j in range(3, sections + 1)
    ]
    first = bvals[1] * wfirst
    rows = []
    for j in range(2, sections + 1):
        mu_j = (2.0 * j - 1.0) / j * bvals[j] / bvals[j - 1]
        nu_j = -(j - 1.0) / j * bvals[j] / bvals[j - 2]
        mut_j = mu_j * wfirst
        rows.append((mu_j, nu_j, mut_j, -(1.0 - bvals[j - 1]) * mut_j))
    return (first, rows)


def kernel_tile(near, far):
    dist = (near[0][..., :, None] - far[0][..., None, :]) ** 2
    dist = dist + (near[1][..., :, None] - far[1][..., None, :]) ** 2
    dist = dist + (near[2][..., :, None] - far[2][..., None, :]) ** 2
    base = jnp.maximum(1.0 - 4.0 * dist, 0.0)
    return base * base


def flux_rows(ext):
    posit = ext[0:3]
    live = ext[3]
    rho = ext[4]
    vel = ext[5:8]
    bfl = ext[8:11]
    cpsi = ext[11]
    speed = ext[12]
    mom = rho * vel
    ptot = rho + 0.5 * jnp.sum(bfl * bfl, axis=0)
    fluxes = []
    for d in range(3):
        rows_d = [mom[d]]
        for k in range(3):
            term = mom[k] * vel[d] - bfl[k] * bfl[d]
            rows_d.append(term + ptot if k == d else term)
        for k in range(3):
            term = vel[d] * bfl[k] - bfl[d] * vel[k]
            rows_d.append(term + cpsi if k == d else term)
        rows_d.append(bfl[d])
        fluxes.append(jnp.stack(rows_d))
    flux = jnp.stack(fluxes)
    state = jnp.concatenate([rho[None], mom, bfl, cpsi[None]], axis=0)
    gsum = posit[0] * flux[0] + posit[1] * flux[1] + posit[2] * flux[2]
    return jnp.concatenate(
        [live[None], posit, flux.reshape(24, -1), gsum, speed * state, speed[None], state], axis=0
    )


def hydro_rate(acc, local, ch):
    count_n = acc[0]
    num = acc.shape[1]
    wflux = acc[4:28].reshape(3, 8, num)
    flux = local[4:28].reshape(3, 8, num)
    posit = local[1:4]
    speed = local[44]
    state = local[45:53]
    central = acc[28:36]
    for d in range(3):
        central = central + flux[d] * (acc[1 + d] - posit[d] * count_n) - posit[d] * wflux[d]
    central = jnp.concatenate([central[:7], (ch * ch) * central[7:8]], axis=0)
    dissip = speed * (acc[45:53] - state * count_n) + acc[36:44] - state * acc[44]
    return ((0.5 * dissip - 0.5 * central) / (1.0 + count_n), count_n)


def diffusion_rate(acc, bloc, etaloc, count_n):
    return 0.5 * (etaloc * (acc[0:3] - bloc * count_n) + acc[3:6] - bloc * acc[6]) / (1.0 + count_n)


def spread_ghosts(rows, ghost_index):
    sizes = ghost_sizes()
    starts = ghost_offsets()
    order = [(-1, 0), (-1, -1), (-1, 1), (1, 0), (1, -1), (1, 1), (0, -1), (0, 1)]
    picks = []
    for p, q in order:
        d = DIRECTIONS.index((p, q))
        picks.append(ghost_index[starts[d] : starts[d] + sizes[d]])
    sent = jnp.take(rows, jnp.concatenate(picks), axis=1)
    bounds = [0]
    for p, q in order:
        bounds.append(bounds[-1] + sizes[DIRECTIONS.index((p, q))])

    def toward(p, q):
        k = order.index((p, q))
        return sent[:, bounds[k] : bounds[k + 1]]

    got = {}
    face_x = GHOST_X
    corner = GHOST_C
    face_y = GHOST_Y
    toward_low = sent[:, bounds[0] : bounds[3]]
    toward_high = sent[:, bounds[3] : bounds[6]]
    along_x = extended(jnp.stack([toward_low, toward_high]), (("gx", 0),), 1)
    from_low = along_x[0]
    from_high = along_x[3]
    downward = jnp.concatenate(
        [
            toward(0, -1),
            from_low[:, face_x : face_x + corner],
            from_high[:, face_x : face_x + corner],
        ],
        axis=1,
    )
    upward = jnp.concatenate(
        [toward(0, 1), from_low[:, face_x + corner :], from_high[:, face_x + corner :]], axis=1
    )
    along_y = extended(jnp.stack([downward, upward]), (("gy", 0),), 1)
    from_below = along_y[0]
    from_above = along_y[3]
    got[-1, 0] = from_low[:, :face_x]
    got[1, 0] = from_high[:, :face_x]
    got[0, -1] = from_below[:, :face_y]
    got[0, 1] = from_above[:, :face_y]
    got[-1, -1] = from_below[:, face_y : face_y + corner]
    got[1, -1] = from_below[:, face_y + corner :]
    got[-1, 1] = from_above[:, face_y : face_y + corner]
    got[1, 1] = from_above[:, face_y + corner :]
    return jnp.concatenate([got[p, q] for p, q in DIRECTIONS], axis=1)


def extend(rows, extra):
    filler = jnp.zeros(
        (rows.shape[0], EXT_BLOCKS * TILE - rows.shape[1] - extra.shape[1]), jnp.float32
    )
    return jnp.concatenate([rows, extra, filler], axis=1)


def shards(
    positions,
    density,
    momentum,
    field,
    psi,
    ohmic,
    ambipolar,
    ghost_index,
    tile_i,
    tile_j,
    tile_count,
):
    nlocal = density.shape[0]
    nblocks = nlocal // TILE
    velocity = momentum / density
    speed = jnp.sqrt(1.0 + jnp.sum(field * field, axis=0) / density)
    fac = ambipolar / (density * jnp.sqrt(density))
    live = jnp.ones_like(density)
    core_rows = [positions, live[None], density[None], velocity, field, psi[None], speed[None]]
    payload = jnp.concatenate(core_rows + [ohmic[None], fac[None]], axis=0)
    ch = mesh_max(jnp.max(speed))
    dt = courant / ch
    ghosts = spread_ghosts(payload, ghost_index)
    ext = extend(payload, ghosts)
    pos_blocks = ext[0:3].reshape(3, EXT_BLOCKS, TILE)
    qext = flux_rows(ext)
    q_blocks = qext.reshape(qext.shape[0], EXT_BLOCKS, TILE)
    count = tile_count[0]
    tiles_total = tile_i.shape[0]
    batch = math.gcd(32, tiles_total)
    rounds = (count + batch - 1) // batch
    block_ids = jnp.arange(nblocks, dtype=jnp.int32)

    def batch_lists(offset):
        near_ids = lax.dynamic_slice_in_dim(tile_i, offset, batch, 0)
        far_ids = lax.dynamic_slice_in_dim(tile_j, offset, batch, 0)
        usable = offset + jnp.arange(batch, dtype=jnp.int32) < count
        onehot = ((near_ids[None, :] == block_ids[:, None]) & usable[None, :]).astype(jnp.float32)
        return (near_ids, far_ids, onehot)

    def fold_batch(acc, blocks, weight, far_ids, onehot):
        qsel = jnp.take(blocks, far_ids, axis=1)
        part = jnp.einsum(
            "rtb,tab->rta",
            qsel,
            weight,
            precision=lax.Precision.HIGH,
            preferred_element_type=jnp.float32,
        )
        return acc + jnp.einsum(
            "pt,rta->rpa",
            onehot,
            part,
            precision=lax.Precision.HIGHEST,
            preferred_element_type=jnp.float32,
        )

    def hydro_step(turn, carry):
        acc, stored = carry
        offset = (turn * batch).astype(jnp.int32)
        near_ids, far_ids, onehot = batch_lists(offset)
        near = jnp.take(pos_blocks, near_ids, axis=1)
        far = jnp.take(pos_blocks, far_ids, axis=1)
        weight = kernel_tile(near, far)
        stored = lax.dynamic_update_slice_in_dim(stored, weight, offset, 0)
        return (fold_batch(acc, q_blocks, weight, far_ids, onehot), stored)

    acc_start = jnp.zeros((qext.shape[0], nblocks, TILE), jnp.float32)
    stored_start = jnp.zeros((tiles_total, TILE, TILE), jnp.float32)
    acc, stored = lax.fori_loop(0, rounds, hydro_step, (acc_start, stored_start))
    acc = acc.reshape(qext.shape[0], nlocal)
    rate, count_n = hydro_rate(acc, qext[:, :nlocal], ch)
    density_new = density + dt * rate[0]
    momentum_new = momentum + dt * rate[1:4]
    yzero = field + dt * rate[4:7]
    psi_new = (psi + dt * rate[7]) * jnp.exp(-damping * dt * ch)

    def operator(bfl):
        eta = ohmic + fac * jnp.sum(bfl * bfl, axis=0)
        ghost_b = spread_ghosts(bfl, ghost_index)
        ghost_eta = ghosts[13] + ghosts[14] * jnp.sum(ghost_b * ghost_b, axis=0)
        b_ext = extend(bfl, ghost_b)
        eta_ext = extend(eta[None], ghost_eta[None])[0]
        qdiff = jnp.concatenate([b_ext, eta_ext[None] * b_ext, eta_ext[None]], axis=0)
        diff_blocks = qdiff.reshape(7, EXT_BLOCKS, TILE)

        def diff_step(turn, acc_diff):
            offset = (turn * batch).astype(jnp.int32)
            near_ids, far_ids, onehot = batch_lists(offset)
            weight = lax.dynamic_slice_in_dim(stored, offset, batch, 0)
            return fold_batch(acc_diff, diff_blocks, weight, far_ids, onehot)

        acc_diff = lax.fori_loop(0, rounds, diff_step, jnp.zeros((7, nblocks, TILE), jnp.float32))
        return diffusion_rate(acc_diff.reshape(7, nlocal), bfl, eta, count_n)

    first, rows = rkl_table(SECTIONS)
    lzero = operator(yzero)
    older = yzero
    prev = yzero + first * dt * lzero
    for mu_j, nu_j, mut_j, gam_j in rows:
        nxt = (
            mu_j * prev
            + nu_j * older
            + (1.0 - mu_j - nu_j) * yzero
            + mut_j * dt * operator(prev)
            + gam_j * dt * lzero
        )
        older = prev
        prev = nxt
    return (density_new, momentum_new, prev, psi_new)


def solution(mesh):
    placed = (
        P(None, ("gx", "gy")),
        P(("gx", "gy")),
        P(None, ("gx", "gy")),
        P(None, ("gx", "gy")),
        P(("gx", "gy")),
        P(("gx", "gy")),
        P(("gx", "gy")),
        P(("gx", "gy")),
        P(("gx", "gy")),
        P(("gx", "gy")),
        P(("gx", "gy")),
    )
    return jax.shard_map(
        shards,
        mesh=mesh,
        in_specs=placed,
        out_specs=(P(("gx", "gy")), P(None, ("gx", "gy")), P(None, ("gx", "gy")), P(("gx", "gy"))),
        check_vma=False,
    )
```

```python
import math

import jax
import jax.numpy as jnp
from jax import lax
from jax.sharding import PartitionSpec as P

TILE = 128
SECTIONS = 4
GHOST_X = 320
GHOST_Y = 160
GHOST_C = 32
EXT_BLOCKS = 25


DIRECTIONS = [(-1, -1), (-1, 0), (-1, 1), (0, -1), (0, 1), (1, -1), (1, 0), (1, 1)]
courant = 0.3
damping = 0.5


def extended(array, sides, width):
    for axis, dim in sides:
        size, length = (lax.axis_size(axis), array.shape[dim])
        up = [(i, (i + 1) % size) for i in range(size - 1)]
        down = [(j, i) for i, j in up]
        last = lax.slice_in_dim(array, length - width, length, axis=dim)
        leading = lax.slice_in_dim(array, 0, width, axis=dim)
        before = lax.ppermute(last, axis, up)
        after = lax.ppermute(leading, axis, down)
        array = jnp.concatenate([before, array, after], axis=dim)
    return array


def mesh_max(value):
    count = lax.axis_size("gx") * lax.axis_size("gy")
    spread = jnp.full((count, 1), value, jnp.float32)
    return jnp.max(lax.all_to_all(spread, ("gx", "gy"), 0, 0, tiled=True))


def ghost_sizes():
    return [GHOST_C, GHOST_X, GHOST_C, GHOST_Y, GHOST_Y, GHOST_C, GHOST_X, GHOST_C]


def ghost_offsets():
    sizes = ghost_sizes()
    starts = [0]
    for value in sizes[:-1]:
        starts.append(starts[-1] + value)
    return starts


def rkl_table(sections):
    wfirst = 4.0 / (sections * sections + sections - 2)
    bvals = [1.0 / 3.0, 1.0 / 3.0, 1.0 / 3.0] + [
        (j * j + j - 2) / (2.0 * j * (j + 1)) for j in range(3, sections + 1)
    ]
    first = bvals[1] * wfirst
    rows = []
    for j in range(2, sections + 1):
        mu_j = (2.0 * j - 1.0) / j * bvals[j] / bvals[j - 1]
        nu_j = -(j - 1.0) / j * bvals[j] / bvals[j - 2]
        mut_j = mu_j * wfirst
        rows.append((mu_j, nu_j, mut_j, -(1.0 - bvals[j - 1]) * mut_j))
    return (first, rows)


def kernel_tile(near, far):
    dist = (near[0][..., :, None] - far[0][..., None, :]) ** 2
    dist = dist + (near[1][..., :, None] - far[1][..., None, :]) ** 2
    dist = dist + (near[2][..., :, None] - far[2][..., None, :]) ** 2
    base = jnp.maximum(1.0 - 4.0 * dist, 0.0)
    return base * base


def flux_rows(ext):
    posit = ext[0:3]
    live = ext[3]
    rho = ext[4]
    vel = ext[5:8]
    bfl = ext[8:11]
    cpsi = ext[11]
    speed = ext[12]
    mom = rho * vel
    ptot = rho + 0.5 * jnp.sum(bfl * bfl, axis=0)
    fluxes = []
    for d in range(3):
        rows_d = [mom[d]]
        for k in range(3):
            term = mom[k] * vel[d] - bfl[k] * bfl[d]
            rows_d.append(term + ptot if k == d else term)
        for k in range(3):
            term = vel[d] * bfl[k] - bfl[d] * vel[k]
            rows_d.append(term + cpsi if k == d else term)
        rows_d.append(bfl[d])
        fluxes.append(jnp.stack(rows_d))
    flux = jnp.stack(fluxes)
    state = jnp.concatenate([rho[None], mom, bfl, cpsi[None]], axis=0)
    gsum = posit[0] * flux[0] + posit[1] * flux[1] + posit[2] * flux[2]
    return jnp.concatenate(
        [live[None], posit, flux.reshape(24, -1), gsum, speed * state, speed[None], state], axis=0
    )


def hydro_rate(acc, local, ch):
    count_n = acc[0]
    num = acc.shape[1]
    wflux = acc[4:28].reshape(3, 8, num)
    flux = local[4:28].reshape(3, 8, num)
    posit = local[1:4]
    speed = local[44]
    state = local[45:53]
    central = acc[28:36]
    for d in range(3):
        central = central + flux[d] * (acc[1 + d] - posit[d] * count_n) - posit[d] * wflux[d]
    central = jnp.concatenate([central[:7], (ch * ch) * central[7:8]], axis=0)
    dissip = speed * (acc[45:53] - state * count_n) + acc[36:44] - state * acc[44]
    return ((0.5 * dissip - 0.5 * central) / (1.0 + count_n), count_n)


def diffusion_rate(acc, bloc, etaloc, count_n):
    return 0.5 * (etaloc * (acc[0:3] - bloc * count_n) + acc[3:6] - bloc * acc[6]) / (1.0 + count_n)


def spread_ghosts(rows, ghost_index):
    sizes = ghost_sizes()
    starts = ghost_offsets()
    width = max(sizes)
    nx, ny = (lax.axis_size("gx"), lax.axis_size("gy"))
    ix, iy = (lax.axis_index("gx"), lax.axis_index("gy"))
    sent = jnp.take(rows, ghost_index, axis=1)
    segments = []
    for d in range(8):
        part = sent[:, starts[d] : starts[d] + sizes[d]]
        segments.append(jnp.pad(part, ((0, 0), (0, width - sizes[d]))))
    segments.append(jnp.zeros_like(segments[0]))
    segments = jnp.stack(segments)
    table = [8] * 9
    for d, (p, q) in enumerate(DIRECTIONS):
        table[(p + 1) * 3 + q + 1] = d
    peer = jnp.arange(nx * ny, dtype=jnp.int32)
    du = peer // ny - ix
    dv = peer % ny - iy
    near = (jnp.abs(du) <= 1) & (jnp.abs(dv) <= 1)
    code = jnp.clip((du + 1) * 3 + dv + 1, 0, 8)
    pick = jnp.where(near, jnp.array(table, jnp.int32)[code], 8)
    outgoing = jnp.take(segments, pick, axis=0)
    incoming = lax.all_to_all(outgoing, ("gx", "gy"), 0, 0, tiled=True)
    pieces = []
    for d, (p, q) in enumerate(DIRECTIONS):
        sx, sy = (ix + p, iy + q)
        inside = (sx >= 0) & (sx < nx) & (sy >= 0) & (sy < ny)
        source = jnp.clip(sx, 0, nx - 1) * ny + jnp.clip(sy, 0, ny - 1)
        block = lax.dynamic_index_in_dim(incoming, source, 0, keepdims=False)
        pieces.append(jnp.where(inside, block[:, : sizes[d]], 0.0))
    return jnp.concatenate(pieces, axis=1)


def extend(rows, extra):
    filler = jnp.zeros(
        (rows.shape[0], EXT_BLOCKS * TILE - rows.shape[1] - extra.shape[1]), jnp.float32
    )
    return jnp.concatenate([rows, extra, filler], axis=1)


def shards(
    positions,
    density,
    momentum,
    field,
    psi,
    ohmic,
    ambipolar,
    ghost_index,
    tile_i,
    tile_j,
    tile_count,
):
    nlocal = density.shape[0]
    nblocks = nlocal // TILE
    velocity = momentum / density
    speed = jnp.sqrt(1.0 + jnp.sum(field * field, axis=0) / density)
    fac = ambipolar / (density * jnp.sqrt(density))
    live = jnp.ones_like(density)
    core_rows = [positions, live[None], density[None], velocity, field, psi[None], speed[None]]
    payload = jnp.concatenate(core_rows + [ohmic[None], fac[None]], axis=0)
    ch = mesh_max(jnp.max(speed))
    dt = courant / ch
    ghosts = spread_ghosts(payload, ghost_index)
    ext = extend(payload, ghosts)
    pos_blocks = ext[0:3].reshape(3, EXT_BLOCKS, TILE)
    qext = flux_rows(ext)
    q_blocks = qext.reshape(qext.shape[0], EXT_BLOCKS, TILE)
    count = tile_count[0]
    tiles_total = tile_i.shape[0]
    batch = math.gcd(32, tiles_total)
    rounds = (count + batch - 1) // batch
    block_ids = jnp.arange(nblocks, dtype=jnp.int32)

    def batch_lists(offset):
        near_ids = lax.dynamic_slice_in_dim(tile_i, offset, batch, 0)
        far_ids = lax.dynamic_slice_in_dim(tile_j, offset, batch, 0)
        usable = offset + jnp.arange(batch, dtype=jnp.int32) < count
        onehot = ((near_ids[None, :] == block_ids[:, None]) & usable[None, :]).astype(jnp.float32)
        return (near_ids, far_ids, onehot)

    def fold_batch(acc, blocks, weight, far_ids, onehot):
        qsel = jnp.take(blocks, far_ids, axis=1)
        part = jnp.einsum(
            "rtb,tab->rta",
            qsel,
            weight,
            precision=lax.Precision.HIGH,
            preferred_element_type=jnp.float32,
        )
        return acc + jnp.einsum(
            "pt,rta->rpa",
            onehot,
            part,
            precision=lax.Precision.HIGHEST,
            preferred_element_type=jnp.float32,
        )

    def hydro_step(turn, carry):
        acc, stored = carry
        offset = (turn * batch).astype(jnp.int32)
        near_ids, far_ids, onehot = batch_lists(offset)
        near = jnp.take(pos_blocks, near_ids, axis=1)
        far = jnp.take(pos_blocks, far_ids, axis=1)
        weight = kernel_tile(near, far)
        stored = lax.dynamic_update_slice_in_dim(stored, weight, offset, 0)
        return (fold_batch(acc, q_blocks, weight, far_ids, onehot), stored)

    acc_start = jnp.zeros((qext.shape[0], nblocks, TILE), jnp.float32)
    stored_start = jnp.zeros((tiles_total, TILE, TILE), jnp.float32)
    acc, stored = lax.fori_loop(0, rounds, hydro_step, (acc_start, stored_start))
    acc = acc.reshape(qext.shape[0], nlocal)
    rate, count_n = hydro_rate(acc, qext[:, :nlocal], ch)
    density_new = density + dt * rate[0]
    momentum_new = momentum + dt * rate[1:4]
    yzero = field + dt * rate[4:7]
    psi_new = (psi + dt * rate[7]) * jnp.exp(-damping * dt * ch)

    def operator(bfl):
        eta = ohmic + fac * jnp.sum(bfl * bfl, axis=0)
        ghost_b = spread_ghosts(bfl, ghost_index)
        ghost_eta = ghosts[13] + ghosts[14] * jnp.sum(ghost_b * ghost_b, axis=0)
        b_ext = extend(bfl, ghost_b)
        eta_ext = extend(eta[None], ghost_eta[None])[0]
        qdiff = jnp.concatenate([b_ext, eta_ext[None] * b_ext, eta_ext[None]], axis=0)
        diff_blocks = qdiff.reshape(7, EXT_BLOCKS, TILE)

        def diff_step(turn, acc_diff):
            offset = (turn * batch).astype(jnp.int32)
            near_ids, far_ids, onehot = batch_lists(offset)
            weight = lax.dynamic_slice_in_dim(stored, offset, batch, 0)
            return fold_batch(acc_diff, diff_blocks, weight, far_ids, onehot)

        acc_diff = lax.fori_loop(0, rounds, diff_step, jnp.zeros((7, nblocks, TILE), jnp.float32))
        return diffusion_rate(acc_diff.reshape(7, nlocal), bfl, eta, count_n)

    first, rows = rkl_table(SECTIONS)
    lzero = operator(yzero)
    older = yzero
    prev = yzero + first * dt * lzero
    for mu_j, nu_j, mut_j, gam_j in rows:
        nxt = (
            mu_j * prev
            + nu_j * older
            + (1.0 - mu_j - nu_j) * yzero
            + mut_j * dt * operator(prev)
            + gam_j * dt * lzero
        )
        older = prev
        prev = nxt
    return (density_new, momentum_new, prev, psi_new)


def solution(mesh):
    placed = (
        P(None, ("gx", "gy")),
        P(("gx", "gy")),
        P(None, ("gx", "gy")),
        P(None, ("gx", "gy")),
        P(("gx", "gy")),
        P(("gx", "gy")),
        P(("gx", "gy")),
        P(("gx", "gy")),
        P(("gx", "gy")),
        P(("gx", "gy")),
        P(("gx", "gy")),
    )
    return jax.shard_map(
        shards,
        mesh=mesh,
        in_specs=placed,
        out_specs=(P(("gx", "gy")), P(None, ("gx", "gy")), P(None, ("gx", "gy")), P(("gx", "gy"))),
        check_vma=False,
    )
```

```python
import math

import jax
import jax.numpy as jnp
from jax import lax
from jax.sharding import PartitionSpec as P

TILE = 128
SECTIONS = 4
GHOST_X = 320
GHOST_Y = 160
GHOST_C = 32
EXT_BLOCKS = 25


DIRECTIONS = [(-1, -1), (-1, 0), (-1, 1), (0, -1), (0, 1), (1, -1), (1, 0), (1, 1)]
courant = 0.3
damping = 0.5


def extended(array, sides, width):
    for axis, dim in sides:
        size, length = (lax.axis_size(axis), array.shape[dim])
        up = [(i, (i + 1) % size) for i in range(size - 1)]
        down = [(j, i) for i, j in up]
        last = lax.slice_in_dim(array, length - width, length, axis=dim)
        leading = lax.slice_in_dim(array, 0, width, axis=dim)
        before = lax.ppermute(last, axis, up)
        after = lax.ppermute(leading, axis, down)
        array = jnp.concatenate([before, array, after], axis=dim)
    return array


def ghost_sizes():
    return [GHOST_C, GHOST_X, GHOST_C, GHOST_Y, GHOST_Y, GHOST_C, GHOST_X, GHOST_C]


def ghost_offsets():
    sizes = ghost_sizes()
    starts = [0]
    for value in sizes[:-1]:
        starts.append(starts[-1] + value)
    return starts


def rkl_table(sections):
    wfirst = 4.0 / (sections * sections + sections - 2)
    bvals = [1.0 / 3.0, 1.0 / 3.0, 1.0 / 3.0] + [
        (j * j + j - 2) / (2.0 * j * (j + 1)) for j in range(3, sections + 1)
    ]
    first = bvals[1] * wfirst
    rows = []
    for j in range(2, sections + 1):
        mu_j = (2.0 * j - 1.0) / j * bvals[j] / bvals[j - 1]
        nu_j = -(j - 1.0) / j * bvals[j] / bvals[j - 2]
        mut_j = mu_j * wfirst
        rows.append((mu_j, nu_j, mut_j, -(1.0 - bvals[j - 1]) * mut_j))
    return (first, rows)


def kernel_tile(near, far):
    dist = (near[0][..., :, None] - far[0][..., None, :]) ** 2
    dist = dist + (near[1][..., :, None] - far[1][..., None, :]) ** 2
    dist = dist + (near[2][..., :, None] - far[2][..., None, :]) ** 2
    base = jnp.maximum(1.0 - 4.0 * dist, 0.0)
    return base * base


def flux_rows(ext):
    posit = ext[0:3]
    live = ext[3]
    rho = ext[4]
    vel = ext[5:8]
    bfl = ext[8:11]
    cpsi = ext[11]
    speed = ext[12]
    mom = rho * vel
    ptot = rho + 0.5 * jnp.sum(bfl * bfl, axis=0)
    fluxes = []
    for d in range(3):
        rows_d = [mom[d]]
        for k in range(3):
            term = mom[k] * vel[d] - bfl[k] * bfl[d]
            rows_d.append(term + ptot if k == d else term)
        for k in range(3):
            term = vel[d] * bfl[k] - bfl[d] * vel[k]
            rows_d.append(term + cpsi if k == d else term)
        rows_d.append(bfl[d])
        fluxes.append(jnp.stack(rows_d))
    flux = jnp.stack(fluxes)
    state = jnp.concatenate([rho[None], mom, bfl, cpsi[None]], axis=0)
    gsum = posit[0] * flux[0] + posit[1] * flux[1] + posit[2] * flux[2]
    return jnp.concatenate(
        [live[None], posit, flux.reshape(24, -1), gsum, speed * state, speed[None], state], axis=0
    )


def hydro_rate(acc, local, ch):
    count_n = acc[0]
    num = acc.shape[1]
    wflux = acc[4:28].reshape(3, 8, num)
    flux = local[4:28].reshape(3, 8, num)
    posit = local[1:4]
    speed = local[44]
    state = local[45:53]
    central = acc[28:36]
    for d in range(3):
        central = central + flux[d] * (acc[1 + d] - posit[d] * count_n) - posit[d] * wflux[d]
    central = jnp.concatenate([central[:7], (ch * ch) * central[7:8]], axis=0)
    dissip = speed * (acc[45:53] - state * count_n) + acc[36:44] - state * acc[44]
    return ((0.5 * dissip - 0.5 * central) / (1.0 + count_n), count_n)


def diffusion_rate(acc, bloc, etaloc, count_n):
    return 0.5 * (etaloc * (acc[0:3] - bloc * count_n) + acc[3:6] - bloc * acc[6]) / (1.0 + count_n)


def spread_ghosts(rows, ghost_index, extra=None):
    sizes = ghost_sizes()
    starts = ghost_offsets()
    width = max(sizes)
    nx, ny = (lax.axis_size("gx"), lax.axis_size("gy"))
    ix, iy = (lax.axis_index("gx"), lax.axis_index("gy"))
    sent = jnp.take(rows, ghost_index, axis=1)
    segments = []
    for d in range(8):
        part = sent[:, starts[d] : starts[d] + sizes[d]]
        segments.append(jnp.pad(part, ((0, 0), (0, width - sizes[d]))))
    segments.append(jnp.zeros_like(segments[0]))
    segments = jnp.stack(segments)
    table = [8] * 9
    for d, (p, q) in enumerate(DIRECTIONS):
        table[(p + 1) * 3 + q + 1] = d
    peer = jnp.arange(nx * ny, dtype=jnp.int32)
    du = peer // ny - ix
    dv = peer % ny - iy
    near = (jnp.abs(du) <= 1) & (jnp.abs(dv) <= 1)
    code = jnp.clip((du + 1) * 3 + dv + 1, 0, 8)
    pick = jnp.where(near, jnp.array(table, jnp.int32)[code], 8)
    outgoing = jnp.take(segments, pick, axis=0)
    nrows = rows.shape[0]
    if extra is not None:
        tag = jnp.full((nx * ny, 1, width), extra, jnp.float32)
        outgoing = jnp.concatenate([outgoing, tag], axis=1)
    incoming = lax.all_to_all(outgoing, ("gx", "gy"), 0, 0, tiled=True)
    pieces = []
    for d, (p, q) in enumerate(DIRECTIONS):
        sx, sy = (ix + p, iy + q)
        inside = (sx >= 0) & (sx < nx) & (sy >= 0) & (sy < ny)
        source = jnp.clip(sx, 0, nx - 1) * ny + jnp.clip(sy, 0, ny - 1)
        block = lax.dynamic_index_in_dim(incoming, source, 0, keepdims=False)
        pieces.append(jnp.where(inside, block[:nrows, : sizes[d]], 0.0))
    ghosts = jnp.concatenate(pieces, axis=1)
    if extra is None:
        return ghosts
    return (ghosts, jnp.max(incoming[:, nrows, 0]))


def extend(rows, extra):
    filler = jnp.zeros(
        (rows.shape[0], EXT_BLOCKS * TILE - rows.shape[1] - extra.shape[1]), jnp.float32
    )
    return jnp.concatenate([rows, extra, filler], axis=1)


def shards(
    positions,
    density,
    momentum,
    field,
    psi,
    ohmic,
    ambipolar,
    ghost_index,
    tile_i,
    tile_j,
    tile_count,
):
    nlocal = density.shape[0]
    nblocks = nlocal // TILE
    velocity = momentum / density
    speed = jnp.sqrt(1.0 + jnp.sum(field * field, axis=0) / density)
    fac = ambipolar / (density * jnp.sqrt(density))
    live = jnp.ones_like(density)
    core_rows = [positions, live[None], density[None], velocity, field, psi[None], speed[None]]
    payload = jnp.concatenate(core_rows + [ohmic[None], fac[None]], axis=0)
    ghosts, ch = spread_ghosts(payload, ghost_index, jnp.max(speed))
    dt = courant / ch
    ext = extend(payload, ghosts)
    pos_blocks = ext[0:3].reshape(3, EXT_BLOCKS, TILE)
    qext = flux_rows(ext)
    q_blocks = qext.reshape(qext.shape[0], EXT_BLOCKS, TILE)
    count = tile_count[0]
    tiles_total = tile_i.shape[0]
    batch = math.gcd(32, tiles_total)
    rounds = (count + batch - 1) // batch
    block_ids = jnp.arange(nblocks, dtype=jnp.int32)

    def batch_lists(offset):
        near_ids = lax.dynamic_slice_in_dim(tile_i, offset, batch, 0)
        far_ids = lax.dynamic_slice_in_dim(tile_j, offset, batch, 0)
        usable = offset + jnp.arange(batch, dtype=jnp.int32) < count
        onehot = ((near_ids[None, :] == block_ids[:, None]) & usable[None, :]).astype(jnp.float32)
        return (near_ids, far_ids, onehot)

    def fold_batch(acc, blocks, weight, far_ids, onehot):
        qsel = jnp.take(blocks, far_ids, axis=1)
        part = jnp.einsum(
            "rtb,tab->rta",
            qsel,
            weight,
            precision=lax.Precision.HIGH,
            preferred_element_type=jnp.float32,
        )
        return acc + jnp.einsum(
            "pt,rta->rpa",
            onehot,
            part,
            precision=lax.Precision.HIGHEST,
            preferred_element_type=jnp.float32,
        )

    def hydro_step(turn, carry):
        acc, stored = carry
        offset = (turn * batch).astype(jnp.int32)
        near_ids, far_ids, onehot = batch_lists(offset)
        near = jnp.take(pos_blocks, near_ids, axis=1)
        far = jnp.take(pos_blocks, far_ids, axis=1)
        weight = kernel_tile(near, far)
        stored = lax.dynamic_update_slice_in_dim(stored, weight, offset, 0)
        return (fold_batch(acc, q_blocks, weight, far_ids, onehot), stored)

    acc_start = jnp.zeros((qext.shape[0], nblocks, TILE), jnp.float32)
    stored_start = jnp.zeros((tiles_total, TILE, TILE), jnp.float32)
    acc, stored = lax.fori_loop(0, rounds, hydro_step, (acc_start, stored_start))
    acc = acc.reshape(qext.shape[0], nlocal)
    rate, count_n = hydro_rate(acc, qext[:, :nlocal], ch)
    density_new = density + dt * rate[0]
    momentum_new = momentum + dt * rate[1:4]
    yzero = field + dt * rate[4:7]
    psi_new = (psi + dt * rate[7]) * jnp.exp(-damping * dt * ch)

    def operator(bfl):
        eta = ohmic + fac * jnp.sum(bfl * bfl, axis=0)
        ghost_b = spread_ghosts(bfl, ghost_index)
        ghost_eta = ghosts[13] + ghosts[14] * jnp.sum(ghost_b * ghost_b, axis=0)
        b_ext = extend(bfl, ghost_b)
        eta_ext = extend(eta[None], ghost_eta[None])[0]
        qdiff = jnp.concatenate([b_ext, eta_ext[None] * b_ext, eta_ext[None]], axis=0)
        diff_blocks = qdiff.reshape(7, EXT_BLOCKS, TILE)

        def diff_step(turn, acc_diff):
            offset = (turn * batch).astype(jnp.int32)
            near_ids, far_ids, onehot = batch_lists(offset)
            weight = lax.dynamic_slice_in_dim(stored, offset, batch, 0)
            return fold_batch(acc_diff, diff_blocks, weight, far_ids, onehot)

        acc_diff = lax.fori_loop(0, rounds, diff_step, jnp.zeros((7, nblocks, TILE), jnp.float32))
        return diffusion_rate(acc_diff.reshape(7, nlocal), bfl, eta, count_n)

    first, rows = rkl_table(SECTIONS)
    lzero = operator(yzero)
    older = yzero
    prev = yzero + first * dt * lzero
    for mu_j, nu_j, mut_j, gam_j in rows:
        nxt = (
            mu_j * prev
            + nu_j * older
            + (1.0 - mu_j - nu_j) * yzero
            + mut_j * dt * operator(prev)
            + gam_j * dt * lzero
        )
        older = prev
        prev = nxt
    return (density_new, momentum_new, prev, psi_new)


def solution(mesh):
    placed = (
        P(None, ("gx", "gy")),
        P(("gx", "gy")),
        P(None, ("gx", "gy")),
        P(None, ("gx", "gy")),
        P(("gx", "gy")),
        P(("gx", "gy")),
        P(("gx", "gy")),
        P(("gx", "gy")),
        P(("gx", "gy")),
        P(("gx", "gy")),
        P(("gx", "gy")),
    )
    return jax.shard_map(
        shards,
        mesh=mesh,
        in_specs=placed,
        out_specs=(P(("gx", "gy")), P(None, ("gx", "gy")), P(None, ("gx", "gy")), P(("gx", "gy"))),
        check_vma=False,
    )
```

```python
import math

import jax
import jax.numpy as jnp
from jax import lax
from jax.sharding import PartitionSpec as P

TILE = 128
SECTIONS = 4
GHOST_X = 320
GHOST_Y = 160
GHOST_C = 32
EXT_BLOCKS = 25


DIRECTIONS = [(-1, -1), (-1, 0), (-1, 1), (0, -1), (0, 1), (1, -1), (1, 0), (1, 1)]
courant = 0.3
damping = 0.5


def extended(array, sides, width):
    for axis, dim in sides:
        size, length = (lax.axis_size(axis), array.shape[dim])
        up = [(i, (i + 1) % size) for i in range(size - 1)]
        down = [(j, i) for i, j in up]
        last = lax.slice_in_dim(array, length - width, length, axis=dim)
        leading = lax.slice_in_dim(array, 0, width, axis=dim)
        before = lax.ppermute(last, axis, up)
        after = lax.ppermute(leading, axis, down)
        array = jnp.concatenate([before, array, after], axis=dim)
    return array


def ghost_sizes():
    return [GHOST_C, GHOST_X, GHOST_C, GHOST_Y, GHOST_Y, GHOST_C, GHOST_X, GHOST_C]


def ghost_offsets():
    sizes = ghost_sizes()
    starts = [0]
    for value in sizes[:-1]:
        starts.append(starts[-1] + value)
    return starts


def rkl_table(sections):
    wfirst = 4.0 / (sections * sections + sections - 2)
    bvals = [1.0 / 3.0, 1.0 / 3.0, 1.0 / 3.0] + [
        (j * j + j - 2) / (2.0 * j * (j + 1)) for j in range(3, sections + 1)
    ]
    first = bvals[1] * wfirst
    rows = []
    for j in range(2, sections + 1):
        mu_j = (2.0 * j - 1.0) / j * bvals[j] / bvals[j - 1]
        nu_j = -(j - 1.0) / j * bvals[j] / bvals[j - 2]
        mut_j = mu_j * wfirst
        rows.append((mu_j, nu_j, mut_j, -(1.0 - bvals[j - 1]) * mut_j))
    return (first, rows)


def kernel_tile(near, far):
    dist = (near[0][..., :, None] - far[0][..., None, :]) ** 2
    dist = dist + (near[1][..., :, None] - far[1][..., None, :]) ** 2
    dist = dist + (near[2][..., :, None] - far[2][..., None, :]) ** 2
    base = jnp.maximum(1.0 - 4.0 * dist, 0.0)
    return base * base


def flux_rows(ext):
    posit = ext[0:3]
    live = ext[3]
    rho = ext[4]
    vel = ext[5:8]
    bfl = ext[8:11]
    cpsi = ext[11]
    speed = ext[12]
    mom = rho * vel
    ptot = rho + 0.5 * jnp.sum(bfl * bfl, axis=0)
    fluxes = []
    for d in range(3):
        rows_d = [mom[d]]
        for k in range(3):
            term = mom[k] * vel[d] - bfl[k] * bfl[d]
            rows_d.append(term + ptot if k == d else term)
        for k in range(3):
            term = vel[d] * bfl[k] - bfl[d] * vel[k]
            rows_d.append(term + cpsi if k == d else term)
        rows_d.append(bfl[d])
        fluxes.append(jnp.stack(rows_d))
    flux = jnp.stack(fluxes)
    state = jnp.concatenate([rho[None], mom, bfl, cpsi[None]], axis=0)
    gsum = posit[0] * flux[0] + posit[1] * flux[1] + posit[2] * flux[2]
    return jnp.concatenate(
        [live[None], posit, flux.reshape(24, -1), gsum, speed * state, speed[None], state], axis=0
    )


def hydro_rate(acc, local, ch):
    count_n = acc[0]
    num = acc.shape[1]
    wflux = acc[4:28].reshape(3, 8, num)
    flux = local[4:28].reshape(3, 8, num)
    posit = local[1:4]
    speed = local[44]
    state = local[45:53]
    central = acc[28:36]
    for d in range(3):
        central = central + flux[d] * (acc[1 + d] - posit[d] * count_n) - posit[d] * wflux[d]
    central = jnp.concatenate([central[:7], (ch * ch) * central[7:8]], axis=0)
    dissip = speed * (acc[45:53] - state * count_n) + acc[36:44] - state * acc[44]
    return ((0.5 * dissip - 0.5 * central) / (1.0 + count_n), count_n)


def diffusion_rate(acc, bloc, etaloc, count_n):
    return 0.5 * (etaloc * (acc[0:3] - bloc * count_n) + acc[3:6] - bloc * acc[6]) / (1.0 + count_n)


def spread_ghosts(rows, ghost_index, extra=None):
    sizes = ghost_sizes()
    starts = ghost_offsets()
    width = max(sizes)
    nx, ny = (lax.axis_size("gx"), lax.axis_size("gy"))
    ix, iy = (lax.axis_index("gx"), lax.axis_index("gy"))
    sent = jnp.take(rows, ghost_index, axis=1)
    segments = []
    for d in range(8):
        part = sent[:, starts[d] : starts[d] + sizes[d]]
        segments.append(jnp.pad(part, ((0, 0), (0, width - sizes[d]))))
    segments.append(jnp.zeros_like(segments[0]))
    segments = jnp.stack(segments)
    table = [8] * 9
    for d, (p, q) in enumerate(DIRECTIONS):
        table[(p + 1) * 3 + q + 1] = d
    peer = jnp.arange(nx * ny, dtype=jnp.int32)
    du = peer // ny - ix
    dv = peer % ny - iy
    near = (jnp.abs(du) <= 1) & (jnp.abs(dv) <= 1)
    code = jnp.clip((du + 1) * 3 + dv + 1, 0, 8)
    pick = jnp.where(near, jnp.array(table, jnp.int32)[code], 8)
    outgoing = jnp.take(segments, pick, axis=0)
    nrows = rows.shape[0]
    if extra is not None:
        tag = jnp.full((nx * ny, 1, width), extra, jnp.float32)
        outgoing = jnp.concatenate([outgoing, tag], axis=1)
    incoming = lax.all_to_all(outgoing, ("gx", "gy"), 0, 0, tiled=True)
    pieces = []
    for d, (p, q) in enumerate(DIRECTIONS):
        sx, sy = (ix + p, iy + q)
        inside = (sx >= 0) & (sx < nx) & (sy >= 0) & (sy < ny)
        source = jnp.clip(sx, 0, nx - 1) * ny + jnp.clip(sy, 0, ny - 1)
        block = lax.dynamic_index_in_dim(incoming, source, 0, keepdims=False)
        pieces.append(jnp.where(inside, block[:nrows, : sizes[d]], 0.0))
    ghosts = jnp.concatenate(pieces, axis=1)
    if extra is None:
        return ghosts
    return (ghosts, jnp.max(incoming[:, nrows, 0]))


def extend(rows, extra):
    filler = jnp.zeros(
        (rows.shape[0], EXT_BLOCKS * TILE - rows.shape[1] - extra.shape[1]), jnp.float32
    )
    return jnp.concatenate([rows, extra, filler], axis=1)


def shards(
    positions,
    density,
    momentum,
    field,
    psi,
    ohmic,
    ambipolar,
    ghost_index,
    tile_i,
    tile_j,
    tile_count,
):
    nlocal = density.shape[0]
    nblocks = nlocal // TILE
    velocity = momentum / density
    speed = jnp.sqrt(1.0 + jnp.sum(field * field, axis=0) / density)
    fac = ambipolar / (density * jnp.sqrt(density))
    live = jnp.ones_like(density)
    core_rows = [positions, live[None], density[None], velocity, field, psi[None], speed[None]]
    payload = jnp.concatenate(core_rows + [ohmic[None], fac[None]], axis=0)
    qlocal = flux_rows(payload)
    ghosts, ch = spread_ghosts(payload, ghost_index, jnp.max(speed))
    dt = courant / ch
    ext = extend(payload, ghosts)
    pos_blocks = ext[0:3].reshape(3, EXT_BLOCKS, TILE)
    pos_local = positions.reshape(3, nblocks, TILE)
    qext = jnp.concatenate([qlocal, flux_rows(ext[:, nlocal:])], axis=1)
    nrow = qext.shape[0]
    q_blocks = qext.reshape(nrow, EXT_BLOCKS, TILE)
    q_local_blocks = qlocal.reshape(nrow, nblocks, TILE)
    count = tile_count[0]
    tiles_total = tile_i.shape[0]
    batch = math.gcd(32, tiles_total)
    block_ids = jnp.arange(nblocks, dtype=jnp.int32)
    slots = jnp.arange(tiles_total, dtype=jnp.int32)
    key = jnp.where(slots < count, (tile_j >= nblocks).astype(jnp.int32), 2)
    first_n = jnp.sum((key == 0).astype(jnp.int32))
    second_n = jnp.sum((key == 1).astype(jnp.int32))
    rank = [jnp.cumsum((key == c).astype(jnp.int32)) - 1 for c in range(3)]
    dest = jnp.where(
        key == 0, rank[0], jnp.where(key == 1, first_n + rank[1], first_n + second_n + rank[2])
    )
    place = dest[None, :] == slots[:, None]
    pad = jnp.zeros((batch,), jnp.int32)
    list_i = jnp.concatenate([jnp.sum(jnp.where(place, tile_i[None, :], 0), axis=1), pad])
    list_j = jnp.concatenate([jnp.sum(jnp.where(place, tile_j[None, :], 0), axis=1), pad])

    def batch_lists(offset, stop, clip):
        near_ids = lax.dynamic_slice_in_dim(list_i, offset, batch, 0)
        far_ids = lax.dynamic_slice_in_dim(list_j, offset, batch, 0)
        if clip:
            far_ids = jnp.minimum(far_ids, nblocks - 1)
        usable = offset + jnp.arange(batch, dtype=jnp.int32) < stop
        onehot = ((near_ids[None, :] == block_ids[:, None]) & usable[None, :]).astype(jnp.float32)
        return (near_ids, far_ids, onehot)

    def fold_batch(acc, blocks, weight, far_ids, onehot):
        qsel = jnp.take(blocks, far_ids, axis=1)
        part = jnp.einsum(
            "rtb,tab->rta",
            qsel,
            weight,
            precision=lax.Precision.HIGH,
            preferred_element_type=jnp.float32,
        )
        return acc + jnp.einsum(
            "pt,rta->rpa",
            onehot,
            part,
            precision=lax.Precision.HIGHEST,
            preferred_element_type=jnp.float32,
        )

    def hydro_pass(start, stop, pos_far, blocks, carry, clip):
        def step(turn, carry):
            acc, stored = carry
            offset = start + turn * batch
            near_ids, far_ids, onehot = batch_lists(offset, stop, clip)
            near = jnp.take(pos_local, near_ids, axis=1)
            far = jnp.take(pos_far, far_ids, axis=1)
            weight = kernel_tile(near, far)
            stored = lax.dynamic_update_slice_in_dim(stored, weight, offset, 0)
            return (fold_batch(acc, blocks, weight, far_ids, onehot), stored)

        return lax.fori_loop(0, (stop - start + batch - 1) // batch, step, carry)

    acc_start = jnp.zeros((nrow, nblocks, TILE), jnp.float32)
    stored_start = jnp.zeros((tiles_total + batch, TILE, TILE), jnp.float32)
    carry = hydro_pass(0, first_n, pos_local, q_local_blocks, (acc_start, stored_start), True)
    acc, stored = hydro_pass(first_n, count, pos_blocks, q_blocks, carry, False)
    acc = acc.reshape(nrow, nlocal)
    rate, count_n = hydro_rate(acc, qlocal, ch)
    density_new = density + dt * rate[0]
    momentum_new = momentum + dt * rate[1:4]
    yzero = field + dt * rate[4:7]
    psi_new = (psi + dt * rate[7]) * jnp.exp(-damping * dt * ch)

    def diff_pass(start, stop, blocks, acc, clip):
        def step(turn, acc_diff):
            offset = start + turn * batch
            near_ids, far_ids, onehot = batch_lists(offset, stop, clip)
            weight = lax.dynamic_slice_in_dim(stored, offset, batch, 0)
            return fold_batch(acc_diff, blocks, weight, far_ids, onehot)

        return lax.fori_loop(0, (stop - start + batch - 1) // batch, step, acc)

    def operator(bfl):
        eta = ohmic + fac * jnp.sum(bfl * bfl, axis=0)
        q_near = jnp.concatenate([bfl, eta[None] * bfl, eta[None]], axis=0)
        acc_diff = diff_pass(
            0, first_n, q_near.reshape(7, nblocks, TILE), jnp.zeros((7, nblocks, TILE), jnp.float32), True
        )
        ghost_b = spread_ghosts(bfl, ghost_index)
        ghost_eta = ghosts[13] + ghosts[14] * jnp.sum(ghost_b * ghost_b, axis=0)
        b_ext = extend(bfl, ghost_b)
        eta_ext = extend(eta[None], ghost_eta[None])[0]
        qdiff = jnp.concatenate([b_ext, eta_ext[None] * b_ext, eta_ext[None]], axis=0)
        diff_blocks = qdiff.reshape(7, EXT_BLOCKS, TILE)
        acc_diff = diff_pass(first_n, count, diff_blocks, acc_diff, False)
        return diffusion_rate(acc_diff.reshape(7, nlocal), bfl, eta, count_n)

    first, rows = rkl_table(SECTIONS)
    lzero = operator(yzero)
    older = yzero
    prev = yzero + first * dt * lzero
    for mu_j, nu_j, mut_j, gam_j in rows:
        nxt = (
            mu_j * prev
            + nu_j * older
            + (1.0 - mu_j - nu_j) * yzero
            + mut_j * dt * operator(prev)
            + gam_j * dt * lzero
        )
        older = prev
        prev = nxt
    return (density_new, momentum_new, prev, psi_new)


def solution(mesh):
    placed = (
        P(None, ("gx", "gy")),
        P(("gx", "gy")),
        P(None, ("gx", "gy")),
        P(None, ("gx", "gy")),
        P(("gx", "gy")),
        P(("gx", "gy")),
        P(("gx", "gy")),
        P(("gx", "gy")),
        P(("gx", "gy")),
        P(("gx", "gy")),
        P(("gx", "gy")),
    )
    return jax.shard_map(
        shards,
        mesh=mesh,
        in_specs=placed,
        out_specs=(P(("gx", "gy")), P(None, ("gx", "gy")), P(None, ("gx", "gy")), P(("gx", "gy"))),
        check_vma=False,
    )
```

```python
import math

import jax
import jax.numpy as jnp
from jax import lax
from jax.sharding import PartitionSpec as P

TILE = 128
SECTIONS = 4
GHOST_X = 320
GHOST_Y = 160
GHOST_C = 32
EXT_BLOCKS = 25


DIRECTIONS = [(-1, -1), (-1, 0), (-1, 1), (0, -1), (0, 1), (1, -1), (1, 0), (1, 1)]
courant = 0.3
damping = 0.5


def extended(array, sides, width):
    for axis, dim in sides:
        size, length = (lax.axis_size(axis), array.shape[dim])
        up = [(i, (i + 1) % size) for i in range(size - 1)]
        down = [(j, i) for i, j in up]
        last = lax.slice_in_dim(array, length - width, length, axis=dim)
        leading = lax.slice_in_dim(array, 0, width, axis=dim)
        before = lax.ppermute(last, axis, up)
        after = lax.ppermute(leading, axis, down)
        array = jnp.concatenate([before, array, after], axis=dim)
    return array


def ghost_sizes():
    return [GHOST_C, GHOST_X, GHOST_C, GHOST_Y, GHOST_Y, GHOST_C, GHOST_X, GHOST_C]


def ghost_offsets():
    sizes = ghost_sizes()
    starts = [0]
    for value in sizes[:-1]:
        starts.append(starts[-1] + value)
    return starts


def rkl_table(sections):
    wfirst = 4.0 / (sections * sections + sections - 2)
    bvals = [1.0 / 3.0, 1.0 / 3.0, 1.0 / 3.0] + [
        (j * j + j - 2) / (2.0 * j * (j + 1)) for j in range(3, sections + 1)
    ]
    first = bvals[1] * wfirst
    rows = []
    for j in range(2, sections + 1):
        mu_j = (2.0 * j - 1.0) / j * bvals[j] / bvals[j - 1]
        nu_j = -(j - 1.0) / j * bvals[j] / bvals[j - 2]
        mut_j = mu_j * wfirst
        rows.append((mu_j, nu_j, mut_j, -(1.0 - bvals[j - 1]) * mut_j))
    return (first, rows)


def kernel_tile(near, far):
    dist = (near[0][..., :, None] - far[0][..., None, :]) ** 2
    dist = dist + (near[1][..., :, None] - far[1][..., None, :]) ** 2
    dist = dist + (near[2][..., :, None] - far[2][..., None, :]) ** 2
    base = jnp.maximum(1.0 - 4.0 * dist, 0.0)
    return base * base


def flux_rows(ext):
    posit = ext[0:3]
    live = ext[3]
    rho = ext[4]
    vel = ext[5:8]
    bfl = ext[8:11]
    cpsi = ext[11]
    speed = ext[12]
    mom = rho * vel
    ptot = rho + 0.5 * jnp.sum(bfl * bfl, axis=0)
    fluxes = []
    for d in range(3):
        rows_d = [mom[d]]
        for k in range(3):
            term = mom[k] * vel[d] - bfl[k] * bfl[d]
            rows_d.append(term + ptot if k == d else term)
        for k in range(3):
            term = vel[d] * bfl[k] - bfl[d] * vel[k]
            rows_d.append(term + cpsi if k == d else term)
        rows_d.append(bfl[d])
        fluxes.append(jnp.stack(rows_d))
    flux = jnp.stack(fluxes)
    state = jnp.concatenate([rho[None], mom, bfl, cpsi[None]], axis=0)
    gsum = posit[0] * flux[0] + posit[1] * flux[1] + posit[2] * flux[2]
    return jnp.concatenate(
        [live[None], posit, flux.reshape(24, -1), gsum, speed * state, speed[None], state], axis=0
    )


def hydro_rate(acc, local, ch):
    count_n = acc[0]
    num = acc.shape[1]
    wflux = acc[4:28].reshape(3, 8, num)
    flux = local[4:28].reshape(3, 8, num)
    posit = local[1:4]
    speed = local[44]
    state = local[45:53]
    central = acc[28:36]
    for d in range(3):
        central = central + flux[d] * (acc[1 + d] - posit[d] * count_n) - posit[d] * wflux[d]
    central = jnp.concatenate([central[:7], (ch * ch) * central[7:8]], axis=0)
    dissip = speed * (acc[45:53] - state * count_n) + acc[36:44] - state * acc[44]
    return ((0.5 * dissip - 0.5 * central) / (1.0 + count_n), count_n)


def diffusion_rate(acc, bloc, etaloc, count_n):
    return 0.5 * (etaloc * (acc[0:3] - bloc * count_n) + acc[3:6] - bloc * acc[6]) / (1.0 + count_n)


def spread_ghosts(rows, ghost_index, extra=None):
    sizes = ghost_sizes()
    starts = ghost_offsets()
    width = max(sizes)
    nx, ny = (lax.axis_size("gx"), lax.axis_size("gy"))
    ix, iy = (lax.axis_index("gx"), lax.axis_index("gy"))
    sent = jnp.take(rows, ghost_index, axis=1)
    segments = []
    for d in range(8):
        part = sent[:, starts[d] : starts[d] + sizes[d]]
        segments.append(jnp.pad(part, ((0, 0), (0, width - sizes[d]))))
    segments.append(jnp.zeros_like(segments[0]))
    segments = jnp.stack(segments)
    table = [8] * 9
    for d, (p, q) in enumerate(DIRECTIONS):
        table[(p + 1) * 3 + q + 1] = d
    peer = jnp.arange(nx * ny, dtype=jnp.int32)
    du = peer // ny - ix
    dv = peer % ny - iy
    near = (jnp.abs(du) <= 1) & (jnp.abs(dv) <= 1)
    code = jnp.clip((du + 1) * 3 + dv + 1, 0, 8)
    pick = jnp.where(near, jnp.array(table, jnp.int32)[code], 8)
    outgoing = jnp.take(segments, pick, axis=0)
    nrows = rows.shape[0]
    if extra is not None:
        tag = jnp.full((nx * ny, 1, width), extra, jnp.float32)
        outgoing = jnp.concatenate([outgoing, tag], axis=1)
    incoming = lax.all_to_all(outgoing, ("gx", "gy"), 0, 0, tiled=True)
    pieces = []
    for d, (p, q) in enumerate(DIRECTIONS):
        sx, sy = (ix + p, iy + q)
        inside = (sx >= 0) & (sx < nx) & (sy >= 0) & (sy < ny)
        source = jnp.clip(sx, 0, nx - 1) * ny + jnp.clip(sy, 0, ny - 1)
        block = lax.dynamic_index_in_dim(incoming, source, 0, keepdims=False)
        pieces.append(jnp.where(inside, block[:nrows, : sizes[d]], 0.0))
    ghosts = jnp.concatenate(pieces, axis=1)
    if extra is None:
        return ghosts
    return (ghosts, jnp.max(incoming[:, nrows, 0]))


def extend(rows, extra):
    filler = jnp.zeros(
        (rows.shape[0], EXT_BLOCKS * TILE - rows.shape[1] - extra.shape[1]), jnp.float32
    )
    return jnp.concatenate([rows, extra, filler], axis=1)


def shards(
    positions,
    density,
    momentum,
    field,
    psi,
    ohmic,
    ambipolar,
    ghost_index,
    tile_i,
    tile_j,
    tile_count,
):
    nlocal = density.shape[0]
    nblocks = nlocal // TILE
    velocity = momentum / density
    speed = jnp.sqrt(1.0 + jnp.sum(field * field, axis=0) / density)
    fac = ambipolar / (density * jnp.sqrt(density))
    live = jnp.ones_like(density)
    core_rows = [positions, live[None], density[None], velocity, field, psi[None], speed[None]]
    payload = jnp.concatenate(core_rows + [ohmic[None], fac[None]], axis=0)
    qlocal = flux_rows(payload)
    ghosts, ch = spread_ghosts(payload, ghost_index, jnp.max(speed))
    dt = courant / ch
    ext = extend(payload, ghosts)
    pos_blocks = ext[0:3].reshape(3, EXT_BLOCKS, TILE)
    pos_local = positions.reshape(3, nblocks, TILE)
    qext = jnp.concatenate([qlocal, flux_rows(ext[:, nlocal:])], axis=1)
    nrow = qext.shape[0]
    q_blocks = qext.reshape(nrow, EXT_BLOCKS, TILE)
    q_local_blocks = qlocal.reshape(nrow, nblocks, TILE)
    count = tile_count[0]
    tiles_total = tile_i.shape[0]
    batch = math.gcd(16, tiles_total)
    block_ids = jnp.arange(nblocks, dtype=jnp.int32)
    slots = jnp.arange(tiles_total, dtype=jnp.int32)
    key = jnp.where(slots < count, (tile_j >= nblocks).astype(jnp.int32), 2)
    first_n = jnp.sum((key == 0).astype(jnp.int32))
    second_n = jnp.sum((key == 1).astype(jnp.int32))
    rank = [jnp.cumsum((key == c).astype(jnp.int32)) - 1 for c in range(3)]
    dest = jnp.where(
        key == 0, rank[0], jnp.where(key == 1, first_n + rank[1], first_n + second_n + rank[2])
    )
    place = dest[None, :] == slots[:, None]
    pad = jnp.zeros((batch,), jnp.int32)
    list_i = jnp.concatenate([jnp.sum(jnp.where(place, tile_i[None, :], 0), axis=1), pad])
    list_j = jnp.concatenate([jnp.sum(jnp.where(place, tile_j[None, :], 0), axis=1), pad])

    def batch_lists(offset, stop, clip):
        near_ids = lax.dynamic_slice_in_dim(list_i, offset, batch, 0)
        far_ids = lax.dynamic_slice_in_dim(list_j, offset, batch, 0)
        if clip:
            far_ids = jnp.minimum(far_ids, nblocks - 1)
        usable = offset + jnp.arange(batch, dtype=jnp.int32) < stop
        onehot = ((near_ids[None, :] == block_ids[:, None]) & usable[None, :]).astype(jnp.float32)
        return (near_ids, far_ids, onehot)

    def fold_batch(acc, blocks, weight, far_ids, onehot):
        qsel = jnp.take(blocks, far_ids, axis=1)
        part = jnp.einsum(
            "rtb,tab->rta",
            qsel,
            weight,
            precision=lax.Precision.HIGH,
            preferred_element_type=jnp.float32,
        )
        return acc + jnp.einsum(
            "pt,rta->rpa",
            onehot,
            part,
            precision=lax.Precision.HIGHEST,
            preferred_element_type=jnp.float32,
        )

    def hydro_pass(start, stop, pos_far, blocks, carry, clip):
        def step(turn, carry):
            acc, stored = carry
            offset = start + turn * batch
            near_ids, far_ids, onehot = batch_lists(offset, stop, clip)
            near = jnp.take(pos_local, near_ids, axis=1)
            far = jnp.take(pos_far, far_ids, axis=1)
            weight = kernel_tile(near, far)
            stored = lax.dynamic_update_slice_in_dim(stored, weight, offset, 0)
            return (fold_batch(acc, blocks, weight, far_ids, onehot), stored)

        return lax.fori_loop(0, (stop - start + batch - 1) // batch, step, carry)

    acc_start = jnp.zeros((nrow, nblocks, TILE), jnp.float32)
    stored_start = jnp.zeros((tiles_total + batch, TILE, TILE), jnp.float32)
    carry = hydro_pass(0, first_n, pos_local, q_local_blocks, (acc_start, stored_start), True)
    acc, stored = hydro_pass(first_n, count, pos_blocks, q_blocks, carry, False)
    acc = acc.reshape(nrow, nlocal)
    rate, count_n = hydro_rate(acc, qlocal, ch)
    density_new = density + dt * rate[0]
    momentum_new = momentum + dt * rate[1:4]
    yzero = field + dt * rate[4:7]
    psi_new = (psi + dt * rate[7]) * jnp.exp(-damping * dt * ch)

    def diff_pass(start, stop, blocks, acc, clip):
        def step(turn, acc_diff):
            offset = start + turn * batch
            near_ids, far_ids, onehot = batch_lists(offset, stop, clip)
            weight = lax.dynamic_slice_in_dim(stored, offset, batch, 0)
            return fold_batch(acc_diff, blocks, weight, far_ids, onehot)

        return lax.fori_loop(0, (stop - start + batch - 1) // batch, step, acc)

    def operator(bfl):
        eta = ohmic + fac * jnp.sum(bfl * bfl, axis=0)
        q_near = jnp.concatenate([bfl, eta[None] * bfl, eta[None]], axis=0)
        acc_diff = diff_pass(
            0, first_n, q_near.reshape(7, nblocks, TILE), jnp.zeros((7, nblocks, TILE), jnp.float32), True
        )
        ghost_b = spread_ghosts(bfl, ghost_index)
        ghost_eta = ghosts[13] + ghosts[14] * jnp.sum(ghost_b * ghost_b, axis=0)
        b_ext = extend(bfl, ghost_b)
        eta_ext = extend(eta[None], ghost_eta[None])[0]
        qdiff = jnp.concatenate([b_ext, eta_ext[None] * b_ext, eta_ext[None]], axis=0)
        diff_blocks = qdiff.reshape(7, EXT_BLOCKS, TILE)
        acc_diff = diff_pass(first_n, count, diff_blocks, acc_diff, False)
        return diffusion_rate(acc_diff.reshape(7, nlocal), bfl, eta, count_n)

    first, rows = rkl_table(SECTIONS)
    lzero = operator(yzero)
    older = yzero
    prev = yzero + first * dt * lzero
    for mu_j, nu_j, mut_j, gam_j in rows:
        nxt = (
            mu_j * prev
            + nu_j * older
            + (1.0 - mu_j - nu_j) * yzero
            + mut_j * dt * operator(prev)
            + gam_j * dt * lzero
        )
        older = prev
        prev = nxt
    return (density_new, momentum_new, prev, psi_new)


def solution(mesh):
    placed = (
        P(None, ("gx", "gy")),
        P(("gx", "gy")),
        P(None, ("gx", "gy")),
        P(None, ("gx", "gy")),
        P(("gx", "gy")),
        P(("gx", "gy")),
        P(("gx", "gy")),
        P(("gx", "gy")),
        P(("gx", "gy")),
        P(("gx", "gy")),
        P(("gx", "gy")),
    )
    return jax.shard_map(
        shards,
        mesh=mesh,
        in_specs=placed,
        out_specs=(P(("gx", "gy")), P(None, ("gx", "gy")), P(None, ("gx", "gy")), P(("gx", "gy"))),
        check_vma=False,
    )
```

```python
import math

import jax
import jax.numpy as jnp
from jax import lax
from jax.sharding import PartitionSpec as P

TILE = 128
SECTIONS = 4
GHOST_X = 320
GHOST_Y = 160
GHOST_C = 32
EXT_BLOCKS = 25


DIRECTIONS = [(-1, -1), (-1, 0), (-1, 1), (0, -1), (0, 1), (1, -1), (1, 0), (1, 1)]
courant = 0.3
damping = 0.5


def extended(array, sides, width):
    for axis, dim in sides:
        size, length = (lax.axis_size(axis), array.shape[dim])
        up = [(i, (i + 1) % size) for i in range(size - 1)]
        down = [(j, i) for i, j in up]
        last = lax.slice_in_dim(array, length - width, length, axis=dim)
        leading = lax.slice_in_dim(array, 0, width, axis=dim)
        before = lax.ppermute(last, axis, up)
        after = lax.ppermute(leading, axis, down)
        array = jnp.concatenate([before, array, after], axis=dim)
    return array


def ghost_sizes():
    return [GHOST_C, GHOST_X, GHOST_C, GHOST_Y, GHOST_Y, GHOST_C, GHOST_X, GHOST_C]


def ghost_offsets():
    sizes = ghost_sizes()
    starts = [0]
    for value in sizes[:-1]:
        starts.append(starts[-1] + value)
    return starts


def rkl_table(sections):
    wfirst = 4.0 / (sections * sections + sections - 2)
    bvals = [1.0 / 3.0, 1.0 / 3.0, 1.0 / 3.0] + [
        (j * j + j - 2) / (2.0 * j * (j + 1)) for j in range(3, sections + 1)
    ]
    first = bvals[1] * wfirst
    rows = []
    for j in range(2, sections + 1):
        mu_j = (2.0 * j - 1.0) / j * bvals[j] / bvals[j - 1]
        nu_j = -(j - 1.0) / j * bvals[j] / bvals[j - 2]
        mut_j = mu_j * wfirst
        rows.append((mu_j, nu_j, mut_j, -(1.0 - bvals[j - 1]) * mut_j))
    return (first, rows)


def kernel_tile(near, far):
    dist = (near[0][..., :, None] - far[0][..., None, :]) ** 2
    dist = dist + (near[1][..., :, None] - far[1][..., None, :]) ** 2
    dist = dist + (near[2][..., :, None] - far[2][..., None, :]) ** 2
    base = jnp.maximum(1.0 - 4.0 * dist, 0.0)
    return base * base


def flux_rows(ext):
    posit = ext[0:3]
    live = ext[3]
    rho = ext[4]
    vel = ext[5:8]
    bfl = ext[8:11]
    cpsi = ext[11]
    speed = ext[12]
    mom = rho * vel
    ptot = rho + 0.5 * jnp.sum(bfl * bfl, axis=0)
    fluxes = []
    for d in range(3):
        rows_d = [mom[d]]
        for k in range(3):
            term = mom[k] * vel[d] - bfl[k] * bfl[d]
            rows_d.append(term + ptot if k == d else term)
        for k in range(3):
            term = vel[d] * bfl[k] - bfl[d] * vel[k]
            rows_d.append(term + cpsi if k == d else term)
        rows_d.append(bfl[d])
        fluxes.append(jnp.stack(rows_d))
    flux = jnp.stack(fluxes)
    state = jnp.concatenate([rho[None], mom, bfl, cpsi[None]], axis=0)
    gsum = posit[0] * flux[0] + posit[1] * flux[1] + posit[2] * flux[2]
    return jnp.concatenate(
        [live[None], posit, flux.reshape(24, -1), gsum, speed * state, speed[None], state], axis=0
    )


def hydro_rate(acc, local, ch):
    count_n = acc[0]
    num = acc.shape[1]
    wflux = acc[4:28].reshape(3, 8, num)
    flux = local[4:28].reshape(3, 8, num)
    posit = local[1:4]
    speed = local[44]
    state = local[45:53]
    central = acc[28:36]
    for d in range(3):
        central = central + flux[d] * (acc[1 + d] - posit[d] * count_n) - posit[d] * wflux[d]
    central = jnp.concatenate([central[:7], (ch * ch) * central[7:8]], axis=0)
    dissip = speed * (acc[45:53] - state * count_n) + acc[36:44] - state * acc[44]
    return ((0.5 * dissip - 0.5 * central) / (1.0 + count_n), count_n)


def diffusion_rate(acc, bloc, etaloc, count_n):
    return 0.5 * (etaloc * (acc[0:3] - bloc * count_n) + acc[3:6] - bloc * acc[6]) / (1.0 + count_n)


def spread_ghosts(rows, ghost_index, extra=None):
    sizes = ghost_sizes()
    starts = ghost_offsets()
    width = max(sizes)
    nx, ny = (lax.axis_size("gx"), lax.axis_size("gy"))
    ix, iy = (lax.axis_index("gx"), lax.axis_index("gy"))
    sent = jnp.take(rows, ghost_index, axis=1)
    segments = []
    for d in range(8):
        part = sent[:, starts[d] : starts[d] + sizes[d]]
        segments.append(jnp.pad(part, ((0, 0), (0, width - sizes[d]))).reshape(-1))
    segments.append(jnp.zeros_like(segments[0]))
    segments = jnp.stack(segments)
    table = [8] * 9
    for d, (p, q) in enumerate(DIRECTIONS):
        table[(p + 1) * 3 + q + 1] = d
    peer = jnp.arange(nx * ny, dtype=jnp.int32)
    du = peer // ny - ix
    dv = peer % ny - iy
    near = (jnp.abs(du) <= 1) & (jnp.abs(dv) <= 1)
    code = jnp.clip((du + 1) * 3 + dv + 1, 0, 8)
    pick = jnp.where(near, jnp.array(table, jnp.int32)[code], 8)
    outgoing = jnp.take(segments, pick, axis=0)
    nrows = rows.shape[0]
    if extra is not None:
        tag = jnp.full((nx * ny, width), extra, jnp.float32)
        outgoing = jnp.concatenate([outgoing, tag], axis=1)
    incoming = lax.all_to_all(outgoing, ("gx", "gy"), 0, 0, tiled=True)
    pieces = []
    for d, (p, q) in enumerate(DIRECTIONS):
        sx, sy = (ix + p, iy + q)
        inside = (sx >= 0) & (sx < nx) & (sy >= 0) & (sy < ny)
        source = jnp.clip(sx, 0, nx - 1) * ny + jnp.clip(sy, 0, ny - 1)
        block = lax.dynamic_index_in_dim(incoming, source, 0, keepdims=False)
        block = block[: nrows * width].reshape(nrows, width)
        pieces.append(jnp.where(inside, block[:, : sizes[d]], 0.0))
    ghosts = jnp.concatenate(pieces, axis=1)
    if extra is None:
        return ghosts
    return (ghosts, jnp.max(incoming[:, nrows * width]))


def extend(rows, extra):
    filler = jnp.zeros(
        (rows.shape[0], EXT_BLOCKS * TILE - rows.shape[1] - extra.shape[1]), jnp.float32
    )
    return jnp.concatenate([rows, extra, filler], axis=1)


def shards(
    positions,
    density,
    momentum,
    field,
    psi,
    ohmic,
    ambipolar,
    ghost_index,
    tile_i,
    tile_j,
    tile_count,
):
    nlocal = density.shape[0]
    nblocks = nlocal // TILE
    velocity = momentum / density
    speed = jnp.sqrt(1.0 + jnp.sum(field * field, axis=0) / density)
    fac = ambipolar / (density * jnp.sqrt(density))
    live = jnp.ones_like(density)
    core_rows = [positions, live[None], density[None], velocity, field, psi[None], speed[None]]
    payload = jnp.concatenate(core_rows + [ohmic[None], fac[None]], axis=0)
    qlocal = flux_rows(payload)
    ghosts, ch = spread_ghosts(payload, ghost_index, jnp.max(speed))
    dt = courant / ch
    ext = extend(payload, ghosts)
    pos_blocks = ext[0:3].reshape(3, EXT_BLOCKS, TILE)
    pos_local = positions.reshape(3, nblocks, TILE)
    qext = jnp.concatenate([qlocal, flux_rows(ext[:, nlocal:])], axis=1)
    nrow = qext.shape[0]
    q_blocks = qext.reshape(nrow, EXT_BLOCKS, TILE)
    q_local_blocks = qlocal.reshape(nrow, nblocks, TILE)
    count = tile_count[0]
    tiles_total = tile_i.shape[0]
    batch = math.gcd(32, tiles_total)
    block_ids = jnp.arange(nblocks, dtype=jnp.int32)
    slots = jnp.arange(tiles_total, dtype=jnp.int32)
    key = jnp.where(slots < count, (tile_j >= nblocks).astype(jnp.int32), 2)
    first_n = jnp.sum((key == 0).astype(jnp.int32))
    second_n = jnp.sum((key == 1).astype(jnp.int32))
    rank = [jnp.cumsum((key == c).astype(jnp.int32)) - 1 for c in range(3)]
    dest = jnp.where(
        key == 0, rank[0], jnp.where(key == 1, first_n + rank[1], first_n + second_n + rank[2])
    )
    place = dest[None, :] == slots[:, None]
    pad = jnp.zeros((batch,), jnp.int32)
    list_i = jnp.concatenate([jnp.sum(jnp.where(place, tile_i[None, :], 0), axis=1), pad])
    list_j = jnp.concatenate([jnp.sum(jnp.where(place, tile_j[None, :], 0), axis=1), pad])

    def batch_lists(offset, stop, clip):
        near_ids = lax.dynamic_slice_in_dim(list_i, offset, batch, 0)
        far_ids = lax.dynamic_slice_in_dim(list_j, offset, batch, 0)
        if clip:
            far_ids = jnp.minimum(far_ids, nblocks - 1)
        usable = offset + jnp.arange(batch, dtype=jnp.int32) < stop
        onehot = ((near_ids[None, :] == block_ids[:, None]) & usable[None, :]).astype(jnp.float32)
        return (near_ids, far_ids, onehot)

    def fold_batch(acc, blocks, weight, far_ids, onehot):
        qsel = jnp.take(blocks, far_ids, axis=1)
        part = jnp.einsum(
            "rtb,tab->rta",
            qsel,
            weight,
            precision=lax.Precision.HIGH,
            preferred_element_type=jnp.float32,
        )
        return acc + jnp.einsum(
            "pt,rta->rpa",
            onehot,
            part,
            precision=lax.Precision.HIGHEST,
            preferred_element_type=jnp.float32,
        )

    def hydro_pass(start, stop, pos_far, blocks, carry, clip):
        def step(turn, carry):
            acc, stored = carry
            offset = start + turn * batch
            near_ids, far_ids, onehot = batch_lists(offset, stop, clip)
            near = jnp.take(pos_local, near_ids, axis=1)
            far = jnp.take(pos_far, far_ids, axis=1)
            weight = kernel_tile(near, far)
            stored = lax.dynamic_update_slice_in_dim(stored, weight, offset, 0)
            return (fold_batch(acc, blocks, weight, far_ids, onehot), stored)

        return lax.fori_loop(0, (stop - start + batch - 1) // batch, step, carry)

    acc_start = jnp.zeros((nrow, nblocks, TILE), jnp.float32)
    stored_start = jnp.zeros((tiles_total + batch, TILE, TILE), jnp.float32)
    carry = hydro_pass(0, first_n, pos_local, q_local_blocks, (acc_start, stored_start), True)
    acc, stored = hydro_pass(first_n, count, pos_blocks, q_blocks, carry, False)
    acc = acc.reshape(nrow, nlocal)
    rate, count_n = hydro_rate(acc, qlocal, ch)
    density_new = density + dt * rate[0]
    momentum_new = momentum + dt * rate[1:4]
    yzero = field + dt * rate[4:7]
    psi_new = (psi + dt * rate[7]) * jnp.exp(-damping * dt * ch)

    def diff_pass(start, stop, blocks, acc, clip):
        def step(turn, acc_diff):
            offset = start + turn * batch
            near_ids, far_ids, onehot = batch_lists(offset, stop, clip)
            weight = lax.dynamic_slice_in_dim(stored, offset, batch, 0)
            return fold_batch(acc_diff, blocks, weight, far_ids, onehot)

        return lax.fori_loop(0, (stop - start + batch - 1) // batch, step, acc)

    def operator(bfl):
        eta = ohmic + fac * jnp.sum(bfl * bfl, axis=0)
        q_near = jnp.concatenate([bfl, eta[None] * bfl, eta[None]], axis=0)
        acc_diff = diff_pass(
            0, first_n, q_near.reshape(7, nblocks, TILE), jnp.zeros((7, nblocks, TILE), jnp.float32), True
        )
        ghost_b = spread_ghosts(bfl, ghost_index)
        ghost_eta = ghosts[13] + ghosts[14] * jnp.sum(ghost_b * ghost_b, axis=0)
        b_ext = extend(bfl, ghost_b)
        eta_ext = extend(eta[None], ghost_eta[None])[0]
        qdiff = jnp.concatenate([b_ext, eta_ext[None] * b_ext, eta_ext[None]], axis=0)
        diff_blocks = qdiff.reshape(7, EXT_BLOCKS, TILE)
        acc_diff = diff_pass(first_n, count, diff_blocks, acc_diff, False)
        return diffusion_rate(acc_diff.reshape(7, nlocal), bfl, eta, count_n)

    first, rows = rkl_table(SECTIONS)
    lzero = operator(yzero)
    older = yzero
    prev = yzero + first * dt * lzero
    coef = jnp.array(
        [[mu_j, nu_j, 1.0 - mu_j - nu_j, mut_j, gam_j] for mu_j, nu_j, mut_j, gam_j in rows],
        jnp.float32,
    )

    def stage(k, carry):
        prev, older = carry
        c = coef[k]
        nxt = (
            c[0] * prev
            + c[1] * older
            + c[2] * yzero
            + c[3] * dt * operator(prev)
            + c[4] * dt * lzero
        )
        return (nxt, prev)

    prev, older = lax.fori_loop(0, len(rows), stage, (prev, older))
    return (density_new, momentum_new, prev, psi_new)


def solution(mesh):
    placed = (
        P(None, ("gx", "gy")),
        P(("gx", "gy")),
        P(None, ("gx", "gy")),
        P(None, ("gx", "gy")),
        P(("gx", "gy")),
        P(("gx", "gy")),
        P(("gx", "gy")),
        P(("gx", "gy")),
        P(("gx", "gy")),
        P(("gx", "gy")),
        P(("gx", "gy")),
    )
    return jax.shard_map(
        shards,
        mesh=mesh,
        in_specs=placed,
        out_specs=(P(("gx", "gy")), P(None, ("gx", "gy")), P(None, ("gx", "gy")), P(("gx", "gy"))),
        check_vma=False,
    )
```

```python
import math

import jax
import jax.numpy as jnp
from jax import lax
from jax.sharding import PartitionSpec as P

TILE = 128
SECTIONS = 4
GHOST_X = 320
GHOST_Y = 160
GHOST_C = 32
EXT_BLOCKS = 25


DIRECTIONS = [(-1, -1), (-1, 0), (-1, 1), (0, -1), (0, 1), (1, -1), (1, 0), (1, 1)]
courant = 0.3
damping = 0.5


def extended(array, sides, width):
    for axis, dim in sides:
        size, length = (lax.axis_size(axis), array.shape[dim])
        up = [(i, (i + 1) % size) for i in range(size - 1)]
        down = [(j, i) for i, j in up]
        last = lax.slice_in_dim(array, length - width, length, axis=dim)
        leading = lax.slice_in_dim(array, 0, width, axis=dim)
        before = lax.ppermute(last, axis, up)
        after = lax.ppermute(leading, axis, down)
        array = jnp.concatenate([before, array, after], axis=dim)
    return array


def ghost_sizes():
    return [GHOST_C, GHOST_X, GHOST_C, GHOST_Y, GHOST_Y, GHOST_C, GHOST_X, GHOST_C]


def ghost_offsets():
    sizes = ghost_sizes()
    starts = [0]
    for value in sizes[:-1]:
        starts.append(starts[-1] + value)
    return starts


def rkl_table(sections):
    wfirst = 4.0 / (sections * sections + sections - 2)
    bvals = [1.0 / 3.0, 1.0 / 3.0, 1.0 / 3.0] + [
        (j * j + j - 2) / (2.0 * j * (j + 1)) for j in range(3, sections + 1)
    ]
    first = bvals[1] * wfirst
    rows = []
    for j in range(2, sections + 1):
        mu_j = (2.0 * j - 1.0) / j * bvals[j] / bvals[j - 1]
        nu_j = -(j - 1.0) / j * bvals[j] / bvals[j - 2]
        mut_j = mu_j * wfirst
        rows.append((mu_j, nu_j, mut_j, -(1.0 - bvals[j - 1]) * mut_j))
    return (first, rows)


def kernel_tile(near, far):
    dist = (near[0][..., :, None] - far[0][..., None, :]) ** 2
    dist = dist + (near[1][..., :, None] - far[1][..., None, :]) ** 2
    dist = dist + (near[2][..., :, None] - far[2][..., None, :]) ** 2
    base = jnp.maximum(1.0 - 4.0 * dist, 0.0)
    return base * base


def flux_rows(ext):
    posit = ext[0:3]
    live = ext[3]
    rho = ext[4]
    vel = ext[5:8]
    bfl = ext[8:11]
    cpsi = ext[11]
    speed = ext[12]
    mom = rho * vel
    ptot = rho + 0.5 * jnp.sum(bfl * bfl, axis=0)
    fluxes = []
    for d in range(3):
        rows_d = [mom[d]]
        for k in range(3):
            term = mom[k] * vel[d] - bfl[k] * bfl[d]
            rows_d.append(term + ptot if k == d else term)
        for k in range(3):
            term = vel[d] * bfl[k] - bfl[d] * vel[k]
            rows_d.append(term + cpsi if k == d else term)
        rows_d.append(bfl[d])
        fluxes.append(jnp.stack(rows_d))
    flux = jnp.stack(fluxes)
    state = jnp.concatenate([rho[None], mom, bfl, cpsi[None]], axis=0)
    gsum = posit[0] * flux[0] + posit[1] * flux[1] + posit[2] * flux[2]
    return jnp.concatenate(
        [live[None], posit, flux.reshape(24, -1), gsum, speed * state, speed[None], state], axis=0
    )


def hydro_rate(acc, local, ch):
    count_n = acc[0]
    num = acc.shape[1]
    wflux = acc[4:28].reshape(3, 8, num)
    flux = local[4:28].reshape(3, 8, num)
    posit = local[1:4]
    speed = local[44]
    state = local[45:53]
    central = acc[28:36]
    for d in range(3):
        central = central + flux[d] * (acc[1 + d] - posit[d] * count_n) - posit[d] * wflux[d]
    central = jnp.concatenate([central[:7], (ch * ch) * central[7:8]], axis=0)
    dissip = speed * (acc[45:53] - state * count_n) + acc[36:44] - state * acc[44]
    return ((0.5 * dissip - 0.5 * central) / (1.0 + count_n), count_n)


def diffusion_rate(acc, bloc, etaloc, count_n):
    return 0.5 * (etaloc * (acc[0:3] - bloc * count_n) + acc[3:6] - bloc * acc[6]) / (1.0 + count_n)


def spread_ghosts(rows, ghost_index, extra=None):
    sizes = ghost_sizes()
    starts = ghost_offsets()
    width = max(sizes)
    nx, ny = (lax.axis_size("gx"), lax.axis_size("gy"))
    ix, iy = (lax.axis_index("gx"), lax.axis_index("gy"))
    sent = jnp.take(rows, ghost_index, axis=1)
    segments = []
    for d in range(8):
        part = sent[:, starts[d] : starts[d] + sizes[d]]
        segments.append(jnp.pad(part, ((0, 0), (0, width - sizes[d]))).reshape(-1))
    segments.append(jnp.zeros_like(segments[0]))
    segments = jnp.stack(segments)
    table = [8] * 9
    for d, (p, q) in enumerate(DIRECTIONS):
        table[(p + 1) * 3 + q + 1] = d
    peer = jnp.arange(nx * ny, dtype=jnp.int32)
    du = peer // ny - ix
    dv = peer % ny - iy
    near = (jnp.abs(du) <= 1) & (jnp.abs(dv) <= 1)
    code = jnp.clip((du + 1) * 3 + dv + 1, 0, 8)
    pick = jnp.where(near, jnp.array(table, jnp.int32)[code], 8)
    outgoing = jnp.take(segments, pick, axis=0)
    nrows = rows.shape[0]
    if extra is not None:
        tag = jnp.full((nx * ny, width), extra, jnp.float32)
        outgoing = jnp.concatenate([outgoing, tag], axis=1)
    incoming = lax.all_to_all(outgoing, ("gx", "gy"), 0, 0, tiled=True)
    pieces = []
    for d, (p, q) in enumerate(DIRECTIONS):
        sx, sy = (ix + p, iy + q)
        inside = (sx >= 0) & (sx < nx) & (sy >= 0) & (sy < ny)
        source = jnp.clip(sx, 0, nx - 1) * ny + jnp.clip(sy, 0, ny - 1)
        block = lax.dynamic_index_in_dim(incoming, source, 0, keepdims=False)
        block = block[: nrows * width].reshape(nrows, width)
        pieces.append(jnp.where(inside, block[:, : sizes[d]], 0.0))
    ghosts = jnp.concatenate(pieces, axis=1)
    if extra is None:
        return ghosts
    return (ghosts, jnp.max(incoming[:, nrows * width]))


def extend(rows, extra):
    filler = jnp.zeros(
        (rows.shape[0], EXT_BLOCKS * TILE - rows.shape[1] - extra.shape[1]), jnp.float32
    )
    return jnp.concatenate([rows, extra, filler], axis=1)


def shards(
    positions,
    density,
    momentum,
    field,
    psi,
    ohmic,
    ambipolar,
    ghost_index,
    tile_i,
    tile_j,
    tile_count,
):
    nlocal = density.shape[0]
    nblocks = nlocal // TILE
    velocity = momentum / density
    speed = jnp.sqrt(1.0 + jnp.sum(field * field, axis=0) / density)
    fac = ambipolar / (density * jnp.sqrt(density))
    live = jnp.ones_like(density)
    core_rows = [positions, live[None], density[None], velocity, field, psi[None], speed[None]]
    payload = jnp.concatenate(core_rows + [ohmic[None], fac[None]], axis=0)
    qlocal = flux_rows(payload)
    ghosts, ch = spread_ghosts(payload, ghost_index, jnp.max(speed))
    dt = courant / ch
    ext = extend(payload, ghosts)
    pos_blocks = ext[0:3].reshape(3, EXT_BLOCKS, TILE)
    pos_local = positions.reshape(3, nblocks, TILE)
    qext = jnp.concatenate([qlocal, flux_rows(ext[:, nlocal:])], axis=1)
    nrow = qext.shape[0]
    q_blocks = qext.reshape(nrow, EXT_BLOCKS, TILE)
    q_local_blocks = qlocal.reshape(nrow, nblocks, TILE)
    count = tile_count[0]
    tiles_total = tile_i.shape[0]
    batch = math.gcd(32, tiles_total)
    block_ids = jnp.arange(nblocks, dtype=jnp.int32)
    slots = jnp.arange(tiles_total, dtype=jnp.int32)
    key = jnp.where(slots < count, (tile_j >= nblocks).astype(jnp.int32), 2)
    first_n = jnp.sum((key == 0).astype(jnp.int32))
    second_n = jnp.sum((key == 1).astype(jnp.int32))
    rank = [jnp.cumsum((key == c).astype(jnp.int32)) - 1 for c in range(3)]
    dest = jnp.where(
        key == 0, rank[0], jnp.where(key == 1, first_n + rank[1], first_n + second_n + rank[2])
    )
    place = dest[None, :] == slots[:, None]
    pad = jnp.zeros((batch,), jnp.int32)
    list_i = jnp.concatenate([jnp.sum(jnp.where(place, tile_i[None, :], 0), axis=1), pad])
    list_j = jnp.concatenate([jnp.sum(jnp.where(place, tile_j[None, :], 0), axis=1), pad])

    def batch_lists(offset, stop, clip):
        near_ids = lax.dynamic_slice_in_dim(list_i, offset, batch, 0)
        far_ids = lax.dynamic_slice_in_dim(list_j, offset, batch, 0)
        if clip:
            far_ids = jnp.minimum(far_ids, nblocks - 1)
        usable = offset + jnp.arange(batch, dtype=jnp.int32) < stop
        onehot = ((near_ids[None, :] == block_ids[:, None]) & usable[None, :]).astype(jnp.float32)
        return (near_ids, far_ids, onehot)

    def fold_batch(acc, blocks, weight, far_ids, onehot):
        qsel = jnp.take(blocks, far_ids, axis=1)
        part = jnp.einsum(
            "rtb,tab->rta",
            qsel,
            weight,
            precision=lax.Precision.HIGH,
            preferred_element_type=jnp.float32,
        )
        return acc + jnp.einsum(
            "pt,rta->rpa",
            onehot,
            part,
            precision=lax.Precision.HIGHEST,
            preferred_element_type=jnp.float32,
        )

    def hydro_pass(start, stop, pos_far, blocks, carry, clip):
        def step(turn, carry):
            acc, stored = carry
            offset = start + turn * batch
            near_ids, far_ids, onehot = batch_lists(offset, stop, clip)
            near = jnp.take(pos_local, near_ids, axis=1)
            far = jnp.take(pos_far, far_ids, axis=1)
            weight = kernel_tile(near, far)
            stored = lax.dynamic_update_slice_in_dim(stored, weight, offset, 0)
            return (fold_batch(acc, blocks, weight, far_ids, onehot), stored)

        return lax.fori_loop(0, (stop - start + batch - 1) // batch, step, carry)

    acc_start = jnp.zeros((nrow, nblocks, TILE), jnp.float32)
    stored_start = jnp.zeros((tiles_total + batch, TILE, TILE), jnp.float32)
    carry = hydro_pass(0, first_n, pos_local, q_local_blocks, (acc_start, stored_start), True)
    acc, stored = hydro_pass(first_n, count, pos_blocks, q_blocks, carry, False)
    acc = acc.reshape(nrow, nlocal)
    rate, count_n = hydro_rate(acc, qlocal, ch)
    density_new = density + dt * rate[0]
    momentum_new = momentum + dt * rate[1:4]
    yzero = field + dt * rate[4:7]
    psi_new = (psi + dt * rate[7]) * jnp.exp(-damping * dt * ch)

    def diff_pass(start, stop, blocks, acc, clip):
        def step(turn, acc_diff):
            offset = start + turn * batch
            near_ids, far_ids, onehot = batch_lists(offset, stop, clip)
            weight = lax.dynamic_slice_in_dim(stored, offset, batch, 0)
            return fold_batch(acc_diff, blocks, weight, far_ids, onehot)

        return lax.fori_loop(0, (stop - start + batch - 1) // batch, step, acc)

    def operator(bfl):
        eta = ohmic + fac * jnp.sum(bfl * bfl, axis=0)
        q_near = jnp.concatenate([bfl, eta[None] * bfl, eta[None]], axis=0)
        acc_diff = diff_pass(
            0, first_n, q_near.reshape(7, nblocks, TILE), jnp.zeros((7, nblocks, TILE), jnp.float32), True
        )
        ghost_b = spread_ghosts(bfl, ghost_index)
        ghost_eta = ghosts[13] + ghosts[14] * jnp.sum(ghost_b * ghost_b, axis=0)
        b_ext = extend(bfl, ghost_b)
        eta_ext = extend(eta[None], ghost_eta[None])[0]
        qdiff = jnp.concatenate([b_ext, eta_ext[None] * b_ext, eta_ext[None]], axis=0)
        diff_blocks = qdiff.reshape(7, EXT_BLOCKS, TILE)
        acc_diff = diff_pass(first_n, count, diff_blocks, acc_diff, False)
        return diffusion_rate(acc_diff.reshape(7, nlocal), bfl, eta, count_n)

    first, rows = rkl_table(SECTIONS)
    lzero = operator(yzero)
    older = yzero
    prev = yzero + first * dt * lzero
    for mu_j, nu_j, mut_j, gam_j in rows:
        nxt = (
            mu_j * prev
            + nu_j * older
            + (1.0 - mu_j - nu_j) * yzero
            + mut_j * dt * operator(prev)
            + gam_j * dt * lzero
        )
        older = prev
        prev = nxt
    return (density_new, momentum_new, prev, psi_new)


def solution(mesh):
    placed = (
        P(None, ("gx", "gy")),
        P(("gx", "gy")),
        P(None, ("gx", "gy")),
        P(None, ("gx", "gy")),
        P(("gx", "gy")),
        P(("gx", "gy")),
        P(("gx", "gy")),
        P(("gx", "gy")),
        P(("gx", "gy")),
        P(("gx", "gy")),
        P(("gx", "gy")),
    )
    return jax.shard_map(
        shards,
        mesh=mesh,
        in_specs=placed,
        out_specs=(P(("gx", "gy")), P(None, ("gx", "gy")), P(None, ("gx", "gy")), P(("gx", "gy"))),
        check_vma=False,
    )
```

```python
import math

import jax
import jax.numpy as jnp
from jax import lax
from jax.sharding import PartitionSpec as P

TILE = 128
SECTIONS = 4
GHOST_X = 320
GHOST_Y = 160
GHOST_C = 32
EXT_BLOCKS = 25


DIRECTIONS = [(-1, -1), (-1, 0), (-1, 1), (0, -1), (0, 1), (1, -1), (1, 0), (1, 1)]
courant = 0.3
damping = 0.5


def extended(array, sides, width):
    for axis, dim in sides:
        size, length = (lax.axis_size(axis), array.shape[dim])
        up = [(i, (i + 1) % size) for i in range(size - 1)]
        down = [(j, i) for i, j in up]
        last = lax.slice_in_dim(array, length - width, length, axis=dim)
        leading = lax.slice_in_dim(array, 0, width, axis=dim)
        before = lax.ppermute(last, axis, up)
        after = lax.ppermute(leading, axis, down)
        array = jnp.concatenate([before, array, after], axis=dim)
    return array


def ghost_sizes():
    return [GHOST_C, GHOST_X, GHOST_C, GHOST_Y, GHOST_Y, GHOST_C, GHOST_X, GHOST_C]


def ghost_offsets():
    sizes = ghost_sizes()
    starts = [0]
    for value in sizes[:-1]:
        starts.append(starts[-1] + value)
    return starts


def rkl_table(sections):
    wfirst = 4.0 / (sections * sections + sections - 2)
    bvals = [1.0 / 3.0, 1.0 / 3.0, 1.0 / 3.0] + [
        (j * j + j - 2) / (2.0 * j * (j + 1)) for j in range(3, sections + 1)
    ]
    first = bvals[1] * wfirst
    rows = []
    for j in range(2, sections + 1):
        mu_j = (2.0 * j - 1.0) / j * bvals[j] / bvals[j - 1]
        nu_j = -(j - 1.0) / j * bvals[j] / bvals[j - 2]
        mut_j = mu_j * wfirst
        rows.append((mu_j, nu_j, mut_j, -(1.0 - bvals[j - 1]) * mut_j))
    return (first, rows)


def kernel_tile(near, far):
    dist = (near[0][..., :, None] - far[0][..., None, :]) ** 2
    dist = dist + (near[1][..., :, None] - far[1][..., None, :]) ** 2
    dist = dist + (near[2][..., :, None] - far[2][..., None, :]) ** 2
    base = jnp.maximum(1.0 - 4.0 * dist, 0.0)
    return base * base


def flux_rows(ext):
    posit = ext[0:3]
    live = ext[3]
    rho = ext[4]
    vel = ext[5:8]
    bfl = ext[8:11]
    cpsi = ext[11]
    speed = ext[12]
    mom = rho * vel
    ptot = rho + 0.5 * jnp.sum(bfl * bfl, axis=0)
    fluxes = []
    for d in range(3):
        rows_d = [mom[d]]
        for k in range(3):
            term = mom[k] * vel[d] - bfl[k] * bfl[d]
            rows_d.append(term + ptot if k == d else term)
        for k in range(3):
            term = vel[d] * bfl[k] - bfl[d] * vel[k]
            rows_d.append(term + cpsi if k == d else term)
        rows_d.append(bfl[d])
        fluxes.append(jnp.stack(rows_d))
    flux = jnp.stack(fluxes)
    state = jnp.concatenate([rho[None], mom, bfl, cpsi[None]], axis=0)
    gsum = posit[0] * flux[0] + posit[1] * flux[1] + posit[2] * flux[2]
    return jnp.concatenate(
        [live[None], posit, flux.reshape(24, -1), gsum, speed * state, speed[None], state], axis=0
    )


def hydro_rate(acc, local, ch):
    count_n = acc[0]
    num = acc.shape[1]
    wflux = acc[4:28].reshape(3, 8, num)
    flux = local[4:28].reshape(3, 8, num)
    posit = local[1:4]
    speed = local[44]
    state = local[45:53]
    central = acc[28:36]
    for d in range(3):
        central = central + flux[d] * (acc[1 + d] - posit[d] * count_n) - posit[d] * wflux[d]
    central = jnp.concatenate([central[:7], (ch * ch) * central[7:8]], axis=0)
    dissip = speed * (acc[45:53] - state * count_n) + acc[36:44] - state * acc[44]
    return ((0.5 * dissip - 0.5 * central) / (1.0 + count_n), count_n)


def diffusion_rate(acc, bloc, etaloc, count_n):
    return 0.5 * (etaloc * (acc[0:3] - bloc * count_n) + acc[3:6] - bloc * acc[6]) / (1.0 + count_n)


def spread_ghosts(rows, ghost_index, extra=None):
    sizes = ghost_sizes()
    starts = ghost_offsets()
    width = max(sizes)
    nx, ny = (lax.axis_size("gx"), lax.axis_size("gy"))
    ix, iy = (lax.axis_index("gx"), lax.axis_index("gy"))
    sent = jnp.take(rows, ghost_index, axis=1)
    segments = []
    for d in range(8):
        part = sent[:, starts[d] : starts[d] + sizes[d]]
        segments.append(jnp.pad(part, ((0, 0), (0, width - sizes[d]))))
    segments.append(jnp.zeros_like(segments[0]))
    segments = jnp.stack(segments)
    table = [8] * 9
    for d, (p, q) in enumerate(DIRECTIONS):
        table[(p + 1) * 3 + q + 1] = d
    peer = jnp.arange(nx * ny, dtype=jnp.int32)
    du = peer // ny - ix
    dv = peer % ny - iy
    near = (jnp.abs(du) <= 1) & (jnp.abs(dv) <= 1)
    code = jnp.clip((du + 1) * 3 + dv + 1, 0, 8)
    pick = jnp.where(near, jnp.array(table, jnp.int32)[code], 8)
    outgoing = jnp.take(segments, pick, axis=0)
    nrows = rows.shape[0]
    if extra is not None:
        tag = jnp.full((nx * ny, 1, width), extra, jnp.float32)
        outgoing = jnp.concatenate([outgoing, tag], axis=1)
    incoming = lax.all_to_all(outgoing, ("gx", "gy"), 0, 0, tiled=True)
    pieces = []
    for d, (p, q) in enumerate(DIRECTIONS):
        sx, sy = (ix + p, iy + q)
        inside = (sx >= 0) & (sx < nx) & (sy >= 0) & (sy < ny)
        source = jnp.clip(sx, 0, nx - 1) * ny + jnp.clip(sy, 0, ny - 1)
        block = lax.dynamic_index_in_dim(incoming, source, 0, keepdims=False)
        pieces.append(jnp.where(inside, block[:nrows, : sizes[d]], 0.0))
    ghosts = jnp.concatenate(pieces, axis=1)
    if extra is None:
        return ghosts
    return (ghosts, jnp.max(incoming[:, nrows, 0]))


def extend(rows, extra):
    filler = jnp.zeros(
        (rows.shape[0], EXT_BLOCKS * TILE - rows.shape[1] - extra.shape[1]), jnp.float32
    )
    return jnp.concatenate([rows, extra, filler], axis=1)


def shards(
    positions,
    density,
    momentum,
    field,
    psi,
    ohmic,
    ambipolar,
    ghost_index,
    tile_i,
    tile_j,
    tile_count,
):
    nlocal = density.shape[0]
    nblocks = nlocal // TILE
    velocity = momentum / density
    speed = jnp.sqrt(1.0 + jnp.sum(field * field, axis=0) / density)
    fac = ambipolar / (density * jnp.sqrt(density))
    live = jnp.ones_like(density)
    core_rows = [positions, live[None], density[None], velocity, field, psi[None], speed[None]]
    payload = jnp.concatenate(core_rows + [ohmic[None], fac[None]], axis=0)
    qlocal = flux_rows(payload)
    ghosts, ch = spread_ghosts(payload, ghost_index, jnp.max(speed))
    dt = courant / ch
    ext = extend(payload, ghosts)
    pos_blocks = ext[0:3].reshape(3, EXT_BLOCKS, TILE)
    pos_local = positions.reshape(3, nblocks, TILE)
    qext = jnp.concatenate([qlocal, flux_rows(ext[:, nlocal:])], axis=1)
    nrow = qext.shape[0]
    q_blocks = qext.reshape(nrow, EXT_BLOCKS, TILE)
    q_local_blocks = qlocal.reshape(nrow, nblocks, TILE)
    count = tile_count[0]
    tiles_total = tile_i.shape[0]
    batch = math.gcd(32, tiles_total)
    block_ids = jnp.arange(nblocks, dtype=jnp.int32)
    slots = jnp.arange(tiles_total, dtype=jnp.int32)
    key = jnp.where(slots < count, (tile_j >= nblocks).astype(jnp.int32), 2)
    first_n = jnp.sum((key == 0).astype(jnp.int32))
    second_n = jnp.sum((key == 1).astype(jnp.int32))
    rank = [jnp.cumsum((key == c).astype(jnp.int32)) - 1 for c in range(3)]
    dest = jnp.where(
        key == 0, rank[0], jnp.where(key == 1, first_n + rank[1], first_n + second_n + rank[2])
    )
    place = dest[None, :] == slots[:, None]
    pad = jnp.zeros((batch,), jnp.int32)
    list_i = jnp.concatenate([jnp.sum(jnp.where(place, tile_i[None, :], 0), axis=1), pad])
    list_j = jnp.concatenate([jnp.sum(jnp.where(place, tile_j[None, :], 0), axis=1), pad])
    split = first_n // batch * batch

    def batch_lists(offset, stop, clip):
        near_ids = lax.dynamic_slice_in_dim(list_i, offset, batch, 0)
        far_ids = lax.dynamic_slice_in_dim(list_j, offset, batch, 0)
        if clip:
            far_ids = jnp.minimum(far_ids, nblocks - 1)
        usable = offset + jnp.arange(batch, dtype=jnp.int32) < stop
        onehot = ((near_ids[None, :] == block_ids[:, None]) & usable[None, :]).astype(jnp.float32)
        return (near_ids, far_ids, onehot)

    def fold_batch(acc, blocks, weight, far_ids, onehot):
        qsel = jnp.take(blocks, far_ids, axis=1)
        part = jnp.einsum(
            "rtb,tab->rta",
            qsel,
            weight,
            precision=lax.Precision.HIGH,
            preferred_element_type=jnp.float32,
        )
        return acc + jnp.einsum(
            "pt,rta->rpa",
            onehot,
            part,
            precision=lax.Precision.HIGHEST,
            preferred_element_type=jnp.float32,
        )

    def hydro_pass(start, stop, pos_far, blocks, carry, clip):
        def step(turn, carry):
            acc, stored = carry
            offset = start + turn * batch
            near_ids, far_ids, onehot = batch_lists(offset, stop, clip)
            near = jnp.take(pos_local, near_ids, axis=1)
            far = jnp.take(pos_far, far_ids, axis=1)
            weight = kernel_tile(near, far)
            stored = lax.dynamic_update_slice_in_dim(stored, weight, offset, 0)
            return (fold_batch(acc, blocks, weight, far_ids, onehot), stored)

        return lax.fori_loop(0, (stop - start + batch - 1) // batch, step, carry)

    acc_start = jnp.zeros((nrow, nblocks, TILE), jnp.float32)
    stored_start = jnp.zeros((tiles_total, TILE, TILE), jnp.float32)
    carry = hydro_pass(0, split, pos_local, q_local_blocks, (acc_start, stored_start), True)
    acc, stored = hydro_pass(split, count, pos_blocks, q_blocks, carry, False)
    acc = acc.reshape(nrow, nlocal)
    rate, count_n = hydro_rate(acc, qlocal, ch)
    density_new = density + dt * rate[0]
    momentum_new = momentum + dt * rate[1:4]
    yzero = field + dt * rate[4:7]
    psi_new = (psi + dt * rate[7]) * jnp.exp(-damping * dt * ch)

    def diff_pass(start, stop, blocks, acc, clip):
        def step(turn, acc_diff):
            offset = start + turn * batch
            near_ids, far_ids, onehot = batch_lists(offset, stop, clip)
            weight = lax.dynamic_slice_in_dim(stored, offset, batch, 0)
            return fold_batch(acc_diff, blocks, weight, far_ids, onehot)

        return lax.fori_loop(0, (stop - start + batch - 1) // batch, step, acc)

    def operator(bfl):
        eta = ohmic + fac * jnp.sum(bfl * bfl, axis=0)
        q_near = jnp.concatenate([bfl, eta[None] * bfl, eta[None]], axis=0)
        acc_diff = diff_pass(
            0, split, q_near.reshape(7, nblocks, TILE), jnp.zeros((7, nblocks, TILE), jnp.float32), True
        )
        ghost_b = spread_ghosts(bfl, ghost_index)
        ghost_eta = ghosts[13] + ghosts[14] * jnp.sum(ghost_b * ghost_b, axis=0)
        b_ext = extend(bfl, ghost_b)
        eta_ext = extend(eta[None], ghost_eta[None])[0]
        qdiff = jnp.concatenate([b_ext, eta_ext[None] * b_ext, eta_ext[None]], axis=0)
        diff_blocks = qdiff.reshape(7, EXT_BLOCKS, TILE)
        acc_diff = diff_pass(split, count, diff_blocks, acc_diff, False)
        return diffusion_rate(acc_diff.reshape(7, nlocal), bfl, eta, count_n)

    first, rows = rkl_table(SECTIONS)
    lzero = operator(yzero)
    older = yzero
    prev = yzero + first * dt * lzero
    for mu_j, nu_j, mut_j, gam_j in rows:
        nxt = (
            mu_j * prev
            + nu_j * older
            + (1.0 - mu_j - nu_j) * yzero
            + mut_j * dt * operator(prev)
            + gam_j * dt * lzero
        )
        older = prev
        prev = nxt
    return (density_new, momentum_new, prev, psi_new)


def solution(mesh):
    placed = (
        P(None, ("gx", "gy")),
        P(("gx", "gy")),
        P(None, ("gx", "gy")),
        P(None, ("gx", "gy")),
        P(("gx", "gy")),
        P(("gx", "gy")),
        P(("gx", "gy")),
        P(("gx", "gy")),
        P(("gx", "gy")),
        P(("gx", "gy")),
        P(("gx", "gy")),
    )
    return jax.shard_map(
        shards,
        mesh=mesh,
        in_specs=placed,
        out_specs=(P(("gx", "gy")), P(None, ("gx", "gy")), P(None, ("gx", "gy")), P(("gx", "gy"))),
        check_vma=False,
    )
```

```python
import math

import jax
import jax.numpy as jnp
from jax import lax
from jax.sharding import PartitionSpec as P

TILE = 128
SECTIONS = 4
GHOST_X = 320
GHOST_Y = 160
GHOST_C = 32
EXT_BLOCKS = 25


DIRECTIONS = [(-1, -1), (-1, 0), (-1, 1), (0, -1), (0, 1), (1, -1), (1, 0), (1, 1)]
courant = 0.3
damping = 0.5


def extended(array, sides, width):
    for axis, dim in sides:
        size, length = (lax.axis_size(axis), array.shape[dim])
        up = [(i, (i + 1) % size) for i in range(size - 1)]
        down = [(j, i) for i, j in up]
        last = lax.slice_in_dim(array, length - width, length, axis=dim)
        leading = lax.slice_in_dim(array, 0, width, axis=dim)
        before = lax.ppermute(last, axis, up)
        after = lax.ppermute(leading, axis, down)
        array = jnp.concatenate([before, array, after], axis=dim)
    return array


def ghost_sizes():
    return [GHOST_C, GHOST_X, GHOST_C, GHOST_Y, GHOST_Y, GHOST_C, GHOST_X, GHOST_C]


def ghost_offsets():
    sizes = ghost_sizes()
    starts = [0]
    for value in sizes[:-1]:
        starts.append(starts[-1] + value)
    return starts


def rkl_table(sections):
    wfirst = 4.0 / (sections * sections + sections - 2)
    bvals = [1.0 / 3.0, 1.0 / 3.0, 1.0 / 3.0] + [
        (j * j + j - 2) / (2.0 * j * (j + 1)) for j in range(3, sections + 1)
    ]
    first = bvals[1] * wfirst
    rows = []
    for j in range(2, sections + 1):
        mu_j = (2.0 * j - 1.0) / j * bvals[j] / bvals[j - 1]
        nu_j = -(j - 1.0) / j * bvals[j] / bvals[j - 2]
        mut_j = mu_j * wfirst
        rows.append((mu_j, nu_j, mut_j, -(1.0 - bvals[j - 1]) * mut_j))
    return (first, rows)


def kernel_tile(near, far):
    dist = (near[0][..., :, None] - far[0][..., None, :]) ** 2
    dist = dist + (near[1][..., :, None] - far[1][..., None, :]) ** 2
    dist = dist + (near[2][..., :, None] - far[2][..., None, :]) ** 2
    base = jnp.maximum(1.0 - 4.0 * dist, 0.0)
    return base * base


def flux_rows(ext):
    posit = ext[0:3]
    live = ext[3]
    rho = ext[4]
    vel = ext[5:8]
    bfl = ext[8:11]
    cpsi = ext[11]
    speed = ext[12]
    mom = rho * vel
    ptot = rho + 0.5 * jnp.sum(bfl * bfl, axis=0)
    fluxes = []
    for d in range(3):
        rows_d = [mom[d]]
        for k in range(3):
            term = mom[k] * vel[d] - bfl[k] * bfl[d]
            rows_d.append(term + ptot if k == d else term)
        for k in range(3):
            term = vel[d] * bfl[k] - bfl[d] * vel[k]
            rows_d.append(term + cpsi if k == d else term)
        rows_d.append(bfl[d])
        fluxes.append(jnp.stack(rows_d))
    flux = jnp.stack(fluxes)
    state = jnp.concatenate([rho[None], mom, bfl, cpsi[None]], axis=0)
    gsum = posit[0] * flux[0] + posit[1] * flux[1] + posit[2] * flux[2]
    return jnp.concatenate(
        [live[None], posit, flux.reshape(24, -1), gsum, speed * state, speed[None], state], axis=0
    )


def hydro_rate(acc, local, ch):
    count_n = acc[0]
    num = acc.shape[1]
    wflux = acc[4:28].reshape(3, 8, num)
    flux = local[4:28].reshape(3, 8, num)
    posit = local[1:4]
    speed = local[44]
    state = local[45:53]
    central = acc[28:36]
    for d in range(3):
        central = central + flux[d] * (acc[1 + d] - posit[d] * count_n) - posit[d] * wflux[d]
    central = jnp.concatenate([central[:7], (ch * ch) * central[7:8]], axis=0)
    dissip = speed * (acc[45:53] - state * count_n) + acc[36:44] - state * acc[44]
    return ((0.5 * dissip - 0.5 * central) / (1.0 + count_n), count_n)


def diffusion_rate(acc, bloc, etaloc, count_n):
    return 0.5 * (etaloc * (acc[0:3] - bloc * count_n) + acc[3:6] - bloc * acc[6]) / (1.0 + count_n)


def spread_ghosts(rows, ghost_index, extra=None):
    sizes = ghost_sizes()
    starts = ghost_offsets()
    width = max(sizes)
    nx, ny = (lax.axis_size("gx"), lax.axis_size("gy"))
    ix, iy = (lax.axis_index("gx"), lax.axis_index("gy"))
    sent = jnp.take(rows, ghost_index, axis=1)
    segments = []
    for d in range(8):
        part = sent[:, starts[d] : starts[d] + sizes[d]]
        segments.append(jnp.pad(part, ((0, 0), (0, width - sizes[d]))))
    segments.append(jnp.zeros_like(segments[0]))
    segments = jnp.stack(segments)
    table = [8] * 9
    for d, (p, q) in enumerate(DIRECTIONS):
        table[(p + 1) * 3 + q + 1] = d
    peer = jnp.arange(nx * ny, dtype=jnp.int32)
    du = peer // ny - ix
    dv = peer % ny - iy
    near = (jnp.abs(du) <= 1) & (jnp.abs(dv) <= 1)
    code = jnp.clip((du + 1) * 3 + dv + 1, 0, 8)
    pick = jnp.where(near, jnp.array(table, jnp.int32)[code], 8)
    outgoing = jnp.take(segments, pick, axis=0)
    nrows = rows.shape[0]
    if extra is not None:
        tag = jnp.full((nx * ny, 1, width), extra, jnp.float32)
        outgoing = jnp.concatenate([outgoing, tag], axis=1)
    incoming = lax.all_to_all(outgoing, ("gx", "gy"), 0, 0, tiled=True)
    pieces = []
    for d, (p, q) in enumerate(DIRECTIONS):
        sx, sy = (ix + p, iy + q)
        inside = (sx >= 0) & (sx < nx) & (sy >= 0) & (sy < ny)
        source = jnp.clip(sx, 0, nx - 1) * ny + jnp.clip(sy, 0, ny - 1)
        block = lax.dynamic_index_in_dim(incoming, source, 0, keepdims=False)
        pieces.append(jnp.where(inside, block[:nrows, : sizes[d]], 0.0))
    ghosts = jnp.concatenate(pieces, axis=1)
    if extra is None:
        return ghosts
    return (ghosts, jnp.max(incoming[:, nrows, 0]))


def pick_rows(array, index):
    runs = []
    for r in index:
        if runs and runs[-1][1] == r:
            runs[-1][1] = r + 1
        else:
            runs.append([r, r + 1])
    return jnp.concatenate([array[a:b] for a, b in runs], axis=0)


def extend(rows, extra):
    filler = jnp.zeros(
        (rows.shape[0], EXT_BLOCKS * TILE - rows.shape[1] - extra.shape[1]), jnp.float32
    )
    return jnp.concatenate([rows, extra, filler], axis=1)


def shards(
    positions,
    density,
    momentum,
    field,
    psi,
    ohmic,
    ambipolar,
    ghost_index,
    tile_i,
    tile_j,
    tile_count,
):
    nlocal = density.shape[0]
    nblocks = nlocal // TILE
    velocity = momentum / density
    speed = jnp.sqrt(1.0 + jnp.sum(field * field, axis=0) / density)
    fac = ambipolar / (density * jnp.sqrt(density))
    live = jnp.ones_like(density)
    core_rows = [positions, live[None], density[None], velocity, field, psi[None], speed[None]]
    payload = jnp.concatenate(core_rows + [ohmic[None], fac[None]], axis=0)
    qlocal = flux_rows(payload)
    ghosts, ch = spread_ghosts(payload, ghost_index, jnp.max(speed))
    dt = courant / ch
    ext = extend(payload, ghosts)
    pos_blocks = ext[0:3].reshape(3, EXT_BLOCKS, TILE)
    pos_local = positions.reshape(3, nblocks, TILE)
    qext = jnp.concatenate([qlocal, flux_rows(ext[:, nlocal:])], axis=1)
    nrow = qext.shape[0]
    twin = {}
    for d in range(3):
        twin[4 + 8 * d] = 46 + d
        twin[11 + 8 * d] = 49 + d
    keep = [r for r in range(nrow) if r not in twin]
    source = [keep.index(twin.get(r, r)) for r in range(nrow)]
    q_blocks = pick_rows(qext, keep).reshape(len(keep), EXT_BLOCKS, TILE)
    q_local_blocks = pick_rows(qlocal, keep).reshape(len(keep), nblocks, TILE)
    count = tile_count[0]
    tiles_total = tile_i.shape[0]
    batch = math.gcd(32, tiles_total)
    block_ids = jnp.arange(nblocks, dtype=jnp.int32)
    slots = jnp.arange(tiles_total, dtype=jnp.int32)
    key = jnp.where(slots < count, (tile_j >= nblocks).astype(jnp.int32), 2)
    first_n = jnp.sum((key == 0).astype(jnp.int32))
    second_n = jnp.sum((key == 1).astype(jnp.int32))
    rank = [jnp.cumsum((key == c).astype(jnp.int32)) - 1 for c in range(3)]
    dest = jnp.where(
        key == 0, rank[0], jnp.where(key == 1, first_n + rank[1], first_n + second_n + rank[2])
    )
    place = dest[None, :] == slots[:, None]
    pad = jnp.zeros((batch,), jnp.int32)
    list_i = jnp.concatenate([jnp.sum(jnp.where(place, tile_i[None, :], 0), axis=1), pad])
    list_j = jnp.concatenate([jnp.sum(jnp.where(place, tile_j[None, :], 0), axis=1), pad])
    split = first_n // batch * batch

    def batch_lists(offset, stop, clip):
        near_ids = lax.dynamic_slice_in_dim(list_i, offset, batch, 0)
        far_ids = lax.dynamic_slice_in_dim(list_j, offset, batch, 0)
        if clip:
            far_ids = jnp.minimum(far_ids, nblocks - 1)
        usable = offset + jnp.arange(batch, dtype=jnp.int32) < stop
        onehot = ((near_ids[None, :] == block_ids[:, None]) & usable[None, :]).astype(jnp.float32)
        return (near_ids, far_ids, onehot)

    def fold_batch(acc, blocks, weight, far_ids, onehot):
        qsel = jnp.take(blocks, far_ids, axis=1)
        part = jnp.einsum(
            "rtb,tab->rta",
            qsel,
            weight,
            precision=lax.Precision.HIGH,
            preferred_element_type=jnp.float32,
        )
        return acc + jnp.einsum(
            "pt,rta->rpa",
            onehot,
            part,
            precision=lax.Precision.HIGHEST,
            preferred_element_type=jnp.float32,
        )

    def hydro_pass(start, stop, pos_far, blocks, carry, clip):
        def step(turn, carry):
            acc, stored = carry
            offset = start + turn * batch
            near_ids, far_ids, onehot = batch_lists(offset, stop, clip)
            near = jnp.take(pos_local, near_ids, axis=1)
            far = jnp.take(pos_far, far_ids, axis=1)
            weight = kernel_tile(near, far)
            stored = lax.dynamic_update_slice_in_dim(stored, weight, offset, 0)
            return (fold_batch(acc, blocks, weight, far_ids, onehot), stored)

        return lax.fori_loop(0, (stop - start + batch - 1) // batch, step, carry)

    acc_start = jnp.zeros((len(keep), nblocks, TILE), jnp.float32)
    stored_start = jnp.zeros((tiles_total, TILE, TILE), jnp.float32)
    carry = hydro_pass(0, split, pos_local, q_local_blocks, (acc_start, stored_start), True)
    acc, stored = hydro_pass(split, count, pos_blocks, q_blocks, carry, False)
    acc = pick_rows(acc.reshape(len(keep), nlocal), source)
    rate, count_n = hydro_rate(acc, qlocal, ch)
    density_new = density + dt * rate[0]
    momentum_new = momentum + dt * rate[1:4]
    yzero = field + dt * rate[4:7]
    psi_new = (psi + dt * rate[7]) * jnp.exp(-damping * dt * ch)

    def diff_pass(start, stop, blocks, acc, clip):
        def step(turn, acc_diff):
            offset = start + turn * batch
            near_ids, far_ids, onehot = batch_lists(offset, stop, clip)
            weight = lax.dynamic_slice_in_dim(stored, offset, batch, 0)
            return fold_batch(acc_diff, blocks, weight, far_ids, onehot)

        return lax.fori_loop(0, (stop - start + batch - 1) // batch, step, acc)

    def operator(bfl):
        eta = ohmic + fac * jnp.sum(bfl * bfl, axis=0)
        q_near = jnp.concatenate([bfl, eta[None] * bfl, eta[None]], axis=0)
        acc_diff = diff_pass(
            0, split, q_near.reshape(7, nblocks, TILE), jnp.zeros((7, nblocks, TILE), jnp.float32), True
        )
        ghost_b = spread_ghosts(bfl, ghost_index)
        ghost_eta = ghosts[13] + ghosts[14] * jnp.sum(ghost_b * ghost_b, axis=0)
        b_ext = extend(bfl, ghost_b)
        eta_ext = extend(eta[None], ghost_eta[None])[0]
        qdiff = jnp.concatenate([b_ext, eta_ext[None] * b_ext, eta_ext[None]], axis=0)
        diff_blocks = qdiff.reshape(7, EXT_BLOCKS, TILE)
        acc_diff = diff_pass(split, count, diff_blocks, acc_diff, False)
        return diffusion_rate(acc_diff.reshape(7, nlocal), bfl, eta, count_n)

    first, rows = rkl_table(SECTIONS)
    lzero = operator(yzero)
    older = yzero
    prev = yzero + first * dt * lzero
    for mu_j, nu_j, mut_j, gam_j in rows:
        nxt = (
            mu_j * prev
            + nu_j * older
            + (1.0 - mu_j - nu_j) * yzero
            + mut_j * dt * operator(prev)
            + gam_j * dt * lzero
        )
        older = prev
        prev = nxt
    return (density_new, momentum_new, prev, psi_new)


def solution(mesh):
    placed = (
        P(None, ("gx", "gy")),
        P(("gx", "gy")),
        P(None, ("gx", "gy")),
        P(None, ("gx", "gy")),
        P(("gx", "gy")),
        P(("gx", "gy")),
        P(("gx", "gy")),
        P(("gx", "gy")),
        P(("gx", "gy")),
        P(("gx", "gy")),
        P(("gx", "gy")),
    )
    return jax.shard_map(
        shards,
        mesh=mesh,
        in_specs=placed,
        out_specs=(P(("gx", "gy")), P(None, ("gx", "gy")), P(None, ("gx", "gy")), P(("gx", "gy"))),
        check_vma=False,
    )
```

```python
import math

import jax
import jax.numpy as jnp
from jax import lax
from jax.sharding import PartitionSpec as P

TILE = 128
SECTIONS = 4
GHOST_X = 320
GHOST_Y = 160
GHOST_C = 32
EXT_BLOCKS = 25


DIRECTIONS = [(-1, -1), (-1, 0), (-1, 1), (0, -1), (0, 1), (1, -1), (1, 0), (1, 1)]
courant = 0.3
damping = 0.5


def extended(array, sides, width):
    for axis, dim in sides:
        size, length = (lax.axis_size(axis), array.shape[dim])
        up = [(i, (i + 1) % size) for i in range(size - 1)]
        down = [(j, i) for i, j in up]
        last = lax.slice_in_dim(array, length - width, length, axis=dim)
        leading = lax.slice_in_dim(array, 0, width, axis=dim)
        before = lax.ppermute(last, axis, up)
        after = lax.ppermute(leading, axis, down)
        array = jnp.concatenate([before, array, after], axis=dim)
    return array


def ghost_sizes():
    return [GHOST_C, GHOST_X, GHOST_C, GHOST_Y, GHOST_Y, GHOST_C, GHOST_X, GHOST_C]


def ghost_offsets():
    sizes = ghost_sizes()
    starts = [0]
    for value in sizes[:-1]:
        starts.append(starts[-1] + value)
    return starts


def rkl_table(sections):
    wfirst = 4.0 / (sections * sections + sections - 2)
    bvals = [1.0 / 3.0, 1.0 / 3.0, 1.0 / 3.0] + [
        (j * j + j - 2) / (2.0 * j * (j + 1)) for j in range(3, sections + 1)
    ]
    first = bvals[1] * wfirst
    rows = []
    for j in range(2, sections + 1):
        mu_j = (2.0 * j - 1.0) / j * bvals[j] / bvals[j - 1]
        nu_j = -(j - 1.0) / j * bvals[j] / bvals[j - 2]
        mut_j = mu_j * wfirst
        rows.append((mu_j, nu_j, mut_j, -(1.0 - bvals[j - 1]) * mut_j))
    return (first, rows)


def kernel_tile(near, far):
    dist = (near[0][..., :, None] - far[0][..., None, :]) ** 2
    dist = dist + (near[1][..., :, None] - far[1][..., None, :]) ** 2
    dist = dist + (near[2][..., :, None] - far[2][..., None, :]) ** 2
    base = jnp.maximum(1.0 - 4.0 * dist, 0.0)
    return base * base


def flux_rows(ext):
    posit = ext[0:3]
    live = ext[3]
    rho = ext[4]
    vel = ext[5:8]
    bfl = ext[8:11]
    cpsi = ext[11]
    speed = ext[12]
    mom = rho * vel
    ptot = rho + 0.5 * jnp.sum(bfl * bfl, axis=0)
    fluxes = []
    for d in range(3):
        rows_d = [mom[d]]
        for k in range(3):
            term = mom[k] * vel[d] - bfl[k] * bfl[d]
            rows_d.append(term + ptot if k == d else term)
        for k in range(3):
            term = vel[d] * bfl[k] - bfl[d] * vel[k]
            rows_d.append(term + cpsi if k == d else term)
        rows_d.append(bfl[d])
        fluxes.append(jnp.stack(rows_d))
    flux = jnp.stack(fluxes)
    state = jnp.concatenate([rho[None], mom, bfl, cpsi[None]], axis=0)
    gsum = posit[0] * flux[0] + posit[1] * flux[1] + posit[2] * flux[2]
    return jnp.concatenate(
        [live[None], posit, flux.reshape(24, -1), gsum, speed * state, speed[None], state], axis=0
    )


def hydro_rate(acc, local, ch):
    count_n = acc[0]
    num = acc.shape[1]
    wflux = acc[4:28].reshape(3, 8, num)
    flux = local[4:28].reshape(3, 8, num)
    posit = local[1:4]
    speed = local[44]
    state = local[45:53]
    central = acc[28:36]
    for d in range(3):
        central = central + flux[d] * (acc[1 + d] - posit[d] * count_n) - posit[d] * wflux[d]
    central = jnp.concatenate([central[:7], (ch * ch) * central[7:8]], axis=0)
    dissip = speed * (acc[45:53] - state * count_n) + acc[36:44] - state * acc[44]
    return ((0.5 * dissip - 0.5 * central) / (1.0 + count_n), count_n)


def diffusion_rate(acc, bloc, etaloc, count_n):
    return 0.5 * (etaloc * (acc[0:3] - bloc * count_n) + acc[3:6] - bloc * acc[6]) / (1.0 + count_n)


def spread_ghosts(rows, ghost_index, extra=None):
    sizes = ghost_sizes()
    starts = ghost_offsets()
    width = max(sizes)
    nx, ny = (lax.axis_size("gx"), lax.axis_size("gy"))
    ix, iy = (lax.axis_index("gx"), lax.axis_index("gy"))
    sent = jnp.take(rows, ghost_index, axis=1)
    segments = []
    for d in range(8):
        part = sent[:, starts[d] : starts[d] + sizes[d]]
        segments.append(jnp.pad(part, ((0, 0), (0, width - sizes[d]))))
    segments.append(jnp.zeros_like(segments[0]))
    segments = jnp.stack(segments)
    table = [8] * 9
    for d, (p, q) in enumerate(DIRECTIONS):
        table[(p + 1) * 3 + q + 1] = d
    peer = jnp.arange(nx * ny, dtype=jnp.int32)
    du = peer // ny - ix
    dv = peer % ny - iy
    near = (jnp.abs(du) <= 1) & (jnp.abs(dv) <= 1)
    code = jnp.clip((du + 1) * 3 + dv + 1, 0, 8)
    pick = jnp.where(near, jnp.array(table, jnp.int32)[code], 8)
    outgoing = jnp.take(segments, pick, axis=0)
    nrows = rows.shape[0]
    if extra is not None:
        tag = jnp.full((nx * ny, 1, width), extra, jnp.float32)
        outgoing = jnp.concatenate([outgoing, tag], axis=1)
    incoming = lax.all_to_all(outgoing, ("gx", "gy"), 0, 0, tiled=True)
    pieces = []
    for d, (p, q) in enumerate(DIRECTIONS):
        sx, sy = (ix + p, iy + q)
        inside = (sx >= 0) & (sx < nx) & (sy >= 0) & (sy < ny)
        source = jnp.clip(sx, 0, nx - 1) * ny + jnp.clip(sy, 0, ny - 1)
        block = lax.dynamic_index_in_dim(incoming, source, 0, keepdims=False)
        pieces.append(jnp.where(inside, block[:nrows, : sizes[d]], 0.0))
    ghosts = jnp.concatenate(pieces, axis=1)
    if extra is None:
        return ghosts
    return (ghosts, jnp.max(incoming[:, nrows, 0]))


def pick_rows(array, index):
    runs = []
    for r in index:
        if runs and runs[-1][1] == r:
            runs[-1][1] = r + 1
        else:
            runs.append([r, r + 1])
    return jnp.concatenate([array[a:b] for a, b in runs], axis=0)


def extend(rows, extra):
    filler = jnp.zeros(
        (rows.shape[0], EXT_BLOCKS * TILE - rows.shape[1] - extra.shape[1]), jnp.float32
    )
    return jnp.concatenate([rows, extra, filler], axis=1)


def shards(
    positions,
    density,
    momentum,
    field,
    psi,
    ohmic,
    ambipolar,
    ghost_index,
    tile_i,
    tile_j,
    tile_count,
):
    nlocal = density.shape[0]
    nblocks = nlocal // TILE
    velocity = momentum / density
    speed = jnp.sqrt(1.0 + jnp.sum(field * field, axis=0) / density)
    fac = ambipolar / (density * jnp.sqrt(density))
    live = jnp.ones_like(density)
    core_rows = [positions, live[None], density[None], velocity, field, psi[None], speed[None]]
    payload = jnp.concatenate(core_rows + [ohmic[None], fac[None]], axis=0)
    qlocal = flux_rows(payload)
    ghosts, ch = spread_ghosts(payload, ghost_index, jnp.max(speed))
    dt = courant / ch
    ext = extend(payload, ghosts)
    pos_blocks = ext[0:3].reshape(3, EXT_BLOCKS, TILE)
    pos_local = positions.reshape(3, nblocks, TILE)
    qext = jnp.concatenate([qlocal, flux_rows(ext[:, nlocal:])], axis=1)
    nrow = qext.shape[0]
    twin = {}
    for d in range(3):
        twin[4 + 8 * d] = 46 + d
        twin[11 + 8 * d] = 49 + d
    keep = [r for r in range(nrow) if r not in twin]
    source = [keep.index(twin.get(r, r)) for r in range(nrow)]
    q_blocks = pick_rows(qext, keep).reshape(len(keep), EXT_BLOCKS, TILE)
    q_local_blocks = pick_rows(qlocal, keep).reshape(len(keep), nblocks, TILE)
    count = tile_count[0]
    tiles_total = tile_i.shape[0]
    batch = math.gcd(32, tiles_total)
    block_ids = jnp.arange(nblocks, dtype=jnp.int32)
    slots = jnp.arange(tiles_total, dtype=jnp.int32)
    key = jnp.where(slots < count, (tile_j >= nblocks).astype(jnp.int32), 2)
    first_n = jnp.sum((key == 0).astype(jnp.int32))
    second_n = jnp.sum((key == 1).astype(jnp.int32))
    rank = [jnp.cumsum((key == c).astype(jnp.int32)) - 1 for c in range(3)]
    dest = jnp.where(
        key == 0, rank[0], jnp.where(key == 1, first_n + rank[1], first_n + second_n + rank[2])
    )
    place = dest[None, :] == slots[:, None]
    pad = jnp.zeros((batch,), jnp.int32)
    list_i = jnp.concatenate([jnp.sum(jnp.where(place, tile_i[None, :], 0), axis=1), pad])
    list_j = jnp.concatenate([jnp.sum(jnp.where(place, tile_j[None, :], 0), axis=1), pad])
    split = first_n // batch * batch

    spots = jnp.arange(tiles_total + batch, dtype=jnp.int32)
    owner = list_i[None, :] == block_ids[:, None]
    onehots = {
        stop: (owner & (spots < bound)[None, :]).astype(jnp.float32)
        for stop, bound in (("split", split), ("count", count))
    }

    def batch_lists(offset, stop, clip):
        near_ids = lax.dynamic_slice_in_dim(list_i, offset, batch, 0)
        far_ids = lax.dynamic_slice_in_dim(list_j, offset, batch, 0)
        if clip:
            far_ids = jnp.minimum(far_ids, nblocks - 1)
        onehot = lax.dynamic_slice_in_dim(onehots[stop], offset, batch, 1)
        return (near_ids, far_ids, onehot)

    def fold_batch(acc, blocks, weight, far_ids, onehot):
        qsel = jnp.take(blocks, far_ids, axis=1)
        part = jnp.einsum(
            "rtb,tab->rta",
            qsel,
            weight,
            precision=lax.Precision.HIGH,
            preferred_element_type=jnp.float32,
        )
        return acc + jnp.einsum(
            "pt,rta->rpa",
            onehot,
            part,
            precision=lax.Precision.HIGHEST,
            preferred_element_type=jnp.float32,
        )

    bounds = {0: 0, "split": split, "count": count}

    def hydro_pass(first, stop, pos_far, blocks, carry, clip):
        start = bounds[first]

        def step(turn, carry):
            acc, stored = carry
            offset = start + turn * batch
            near_ids, far_ids, onehot = batch_lists(offset, stop, clip)
            near = jnp.take(pos_local, near_ids, axis=1)
            far = jnp.take(pos_far, far_ids, axis=1)
            weight = kernel_tile(near, far)
            stored = lax.dynamic_update_slice_in_dim(stored, weight, offset, 0)
            return (fold_batch(acc, blocks, weight, far_ids, onehot), stored)

        return lax.fori_loop(0, (bounds[stop] - start + batch - 1) // batch, step, carry)

    acc_start = jnp.zeros((len(keep), nblocks, TILE), jnp.float32)
    stored_start = jnp.zeros((tiles_total, TILE, TILE), jnp.float32)
    carry = hydro_pass(0, "split", pos_local, q_local_blocks, (acc_start, stored_start), True)
    acc, stored = hydro_pass("split", "count", pos_blocks, q_blocks, carry, False)
    acc = pick_rows(acc.reshape(len(keep), nlocal), source)
    rate, count_n = hydro_rate(acc, qlocal, ch)
    density_new = density + dt * rate[0]
    momentum_new = momentum + dt * rate[1:4]
    yzero = field + dt * rate[4:7]
    psi_new = (psi + dt * rate[7]) * jnp.exp(-damping * dt * ch)

    def diff_pass(first, stop, blocks, acc, clip):
        start = bounds[first]

        def step(turn, acc_diff):
            offset = start + turn * batch
            near_ids, far_ids, onehot = batch_lists(offset, stop, clip)
            weight = lax.dynamic_slice_in_dim(stored, offset, batch, 0)
            return fold_batch(acc_diff, blocks, weight, far_ids, onehot)

        return lax.fori_loop(0, (bounds[stop] - start + batch - 1) // batch, step, acc)

    def operator(bfl):
        eta = ohmic + fac * jnp.sum(bfl * bfl, axis=0)
        q_near = jnp.concatenate([bfl, eta[None] * bfl, eta[None]], axis=0)
        acc_diff = diff_pass(
            0, "split", q_near.reshape(7, nblocks, TILE), jnp.zeros((7, nblocks, TILE), jnp.float32), True
        )
        ghost_b = spread_ghosts(bfl, ghost_index)
        ghost_eta = ghosts[13] + ghosts[14] * jnp.sum(ghost_b * ghost_b, axis=0)
        b_ext = extend(bfl, ghost_b)
        eta_ext = extend(eta[None], ghost_eta[None])[0]
        qdiff = jnp.concatenate([b_ext, eta_ext[None] * b_ext, eta_ext[None]], axis=0)
        diff_blocks = qdiff.reshape(7, EXT_BLOCKS, TILE)
        acc_diff = diff_pass("split", "count", diff_blocks, acc_diff, False)
        return diffusion_rate(acc_diff.reshape(7, nlocal), bfl, eta, count_n)

    first, rows = rkl_table(SECTIONS)
    lzero = operator(yzero)
    older = yzero
    prev = yzero + first * dt * lzero
    for mu_j, nu_j, mut_j, gam_j in rows:
        nxt = (
            mu_j * prev
            + nu_j * older
            + (1.0 - mu_j - nu_j) * yzero
            + mut_j * dt * operator(prev)
            + gam_j * dt * lzero
        )
        older = prev
        prev = nxt
    return (density_new, momentum_new, prev, psi_new)


def solution(mesh):
    placed = (
        P(None, ("gx", "gy")),
        P(("gx", "gy")),
        P(None, ("gx", "gy")),
        P(None, ("gx", "gy")),
        P(("gx", "gy")),
        P(("gx", "gy")),
        P(("gx", "gy")),
        P(("gx", "gy")),
        P(("gx", "gy")),
        P(("gx", "gy")),
        P(("gx", "gy")),
    )
    return jax.shard_map(
        shards,
        mesh=mesh,
        in_specs=placed,
        out_specs=(P(("gx", "gy")), P(None, ("gx", "gy")), P(None, ("gx", "gy")), P(("gx", "gy"))),
        check_vma=False,
    )
```

```python
import math

import jax
import jax.numpy as jnp
from jax import lax
from jax.sharding import PartitionSpec as P

TILE = 128
SECTIONS = 4
GHOST_X = 320
GHOST_Y = 160
GHOST_C = 32
EXT_BLOCKS = 25


DIRECTIONS = [(-1, -1), (-1, 0), (-1, 1), (0, -1), (0, 1), (1, -1), (1, 0), (1, 1)]
courant = 0.3
damping = 0.5


def extended(array, sides, width):
    for axis, dim in sides:
        size, length = (lax.axis_size(axis), array.shape[dim])
        up = [(i, (i + 1) % size) for i in range(size - 1)]
        down = [(j, i) for i, j in up]
        last = lax.slice_in_dim(array, length - width, length, axis=dim)
        leading = lax.slice_in_dim(array, 0, width, axis=dim)
        before = lax.ppermute(last, axis, up)
        after = lax.ppermute(leading, axis, down)
        array = jnp.concatenate([before, array, after], axis=dim)
    return array


def ghost_sizes():
    return [GHOST_C, GHOST_X, GHOST_C, GHOST_Y, GHOST_Y, GHOST_C, GHOST_X, GHOST_C]


def ghost_offsets():
    sizes = ghost_sizes()
    starts = [0]
    for value in sizes[:-1]:
        starts.append(starts[-1] + value)
    return starts


def rkl_table(sections):
    wfirst = 4.0 / (sections * sections + sections - 2)
    bvals = [1.0 / 3.0, 1.0 / 3.0, 1.0 / 3.0] + [
        (j * j + j - 2) / (2.0 * j * (j + 1)) for j in range(3, sections + 1)
    ]
    first = bvals[1] * wfirst
    rows = []
    for j in range(2, sections + 1):
        mu_j = (2.0 * j - 1.0) / j * bvals[j] / bvals[j - 1]
        nu_j = -(j - 1.0) / j * bvals[j] / bvals[j - 2]
        mut_j = mu_j * wfirst
        rows.append((mu_j, nu_j, mut_j, -(1.0 - bvals[j - 1]) * mut_j))
    return (first, rows)


def kernel_tile(near, far):
    dist = (near[0][..., :, None] - far[0][..., None, :]) ** 2
    dist = dist + (near[1][..., :, None] - far[1][..., None, :]) ** 2
    dist = dist + (near[2][..., :, None] - far[2][..., None, :]) ** 2
    base = jnp.maximum(1.0 - 4.0 * dist, 0.0)
    return base * base


def flux_rows(ext):
    posit = ext[0:3]
    live = ext[3]
    rho = ext[4]
    vel = ext[5:8]
    bfl = ext[8:11]
    cpsi = ext[11]
    speed = ext[12]
    mom = rho * vel
    ptot = rho + 0.5 * jnp.sum(bfl * bfl, axis=0)
    fluxes = []
    for d in range(3):
        rows_d = [mom[d]]
        for k in range(3):
            term = mom[k] * vel[d] - bfl[k] * bfl[d]
            rows_d.append(term + ptot if k == d else term)
        for k in range(3):
            term = vel[d] * bfl[k] - bfl[d] * vel[k]
            rows_d.append(term + cpsi if k == d else term)
        rows_d.append(bfl[d])
        fluxes.append(jnp.stack(rows_d))
    flux = jnp.stack(fluxes)
    state = jnp.concatenate([rho[None], mom, bfl, cpsi[None]], axis=0)
    gsum = posit[0] * flux[0] + posit[1] * flux[1] + posit[2] * flux[2]
    return jnp.concatenate(
        [live[None], posit, flux.reshape(24, -1), gsum, speed * state, speed[None], state], axis=0
    )


def hydro_rate(acc, local, ch):
    count_n = acc[0]
    num = acc.shape[1]
    wflux = acc[4:28].reshape(3, 8, num)
    flux = local[4:28].reshape(3, 8, num)
    posit = local[1:4]
    speed = local[44]
    state = local[45:53]
    central = acc[28:36]
    for d in range(3):
        central = central + flux[d] * (acc[1 + d] - posit[d] * count_n) - posit[d] * wflux[d]
    central = jnp.concatenate([central[:7], (ch * ch) * central[7:8]], axis=0)
    dissip = speed * (acc[45:53] - state * count_n) + acc[36:44] - state * acc[44]
    return ((0.5 * dissip - 0.5 * central) / (1.0 + count_n), count_n)


def diffusion_rate(acc, bloc, etaloc, count_n):
    return 0.5 * (etaloc * (acc[0:3] - bloc * count_n) + acc[3:6] - bloc * acc[6]) / (1.0 + count_n)


def spread_ghosts(rows, ghost_index, extra=None):
    sizes = ghost_sizes()
    starts = ghost_offsets()
    width = max(sizes)
    nx, ny = (lax.axis_size("gx"), lax.axis_size("gy"))
    ix, iy = (lax.axis_index("gx"), lax.axis_index("gy"))
    sent = jnp.take(rows.T, ghost_index, axis=0).T
    segments = []
    for d in range(8):
        part = sent[:, starts[d] : starts[d] + sizes[d]]
        segments.append(jnp.pad(part, ((0, 0), (0, width - sizes[d]))))
    segments.append(jnp.zeros_like(segments[0]))
    segments = jnp.stack(segments)
    table = [8] * 9
    for d, (p, q) in enumerate(DIRECTIONS):
        table[(p + 1) * 3 + q + 1] = d
    peer = jnp.arange(nx * ny, dtype=jnp.int32)
    du = peer // ny - ix
    dv = peer % ny - iy
    near = (jnp.abs(du) <= 1) & (jnp.abs(dv) <= 1)
    code = jnp.clip((du + 1) * 3 + dv + 1, 0, 8)
    pick = jnp.where(near, jnp.array(table, jnp.int32)[code], 8)
    outgoing = jnp.take(segments, pick, axis=0)
    nrows = rows.shape[0]
    if extra is not None:
        tag = jnp.full((nx * ny, 1, width), extra, jnp.float32)
        outgoing = jnp.concatenate([outgoing, tag], axis=1)
    incoming = lax.all_to_all(outgoing, ("gx", "gy"), 0, 0, tiled=True)
    pieces = []
    for d, (p, q) in enumerate(DIRECTIONS):
        sx, sy = (ix + p, iy + q)
        inside = (sx >= 0) & (sx < nx) & (sy >= 0) & (sy < ny)
        source = jnp.clip(sx, 0, nx - 1) * ny + jnp.clip(sy, 0, ny - 1)
        block = lax.dynamic_index_in_dim(incoming, source, 0, keepdims=False)
        pieces.append(jnp.where(inside, block[:nrows, : sizes[d]], 0.0))
    ghosts = jnp.concatenate(pieces, axis=1)
    if extra is None:
        return ghosts
    return (ghosts, jnp.max(incoming[:, nrows, 0]))


def pick_rows(array, index):
    runs = []
    for r in index:
        if runs and runs[-1][1] == r:
            runs[-1][1] = r + 1
        else:
            runs.append([r, r + 1])
    return jnp.concatenate([array[a:b] for a, b in runs], axis=0)


def extend(rows, extra):
    filler = jnp.zeros(
        (rows.shape[0], EXT_BLOCKS * TILE - rows.shape[1] - extra.shape[1]), jnp.float32
    )
    return jnp.concatenate([rows, extra, filler], axis=1)


def shards(
    positions,
    density,
    momentum,
    field,
    psi,
    ohmic,
    ambipolar,
    ghost_index,
    tile_i,
    tile_j,
    tile_count,
):
    nlocal = density.shape[0]
    nblocks = nlocal // TILE
    velocity = momentum / density
    speed = jnp.sqrt(1.0 + jnp.sum(field * field, axis=0) / density)
    fac = ambipolar / (density * jnp.sqrt(density))
    live = jnp.ones_like(density)
    core_rows = [positions, live[None], density[None], velocity, field, psi[None], speed[None]]
    payload = jnp.concatenate(core_rows + [ohmic[None], fac[None]], axis=0)
    qlocal = flux_rows(payload)
    ghosts, ch = spread_ghosts(payload, ghost_index, jnp.max(speed))
    dt = courant / ch
    ext = extend(payload, ghosts)
    pos_blocks = ext[0:3].reshape(3, EXT_BLOCKS, TILE)
    pos_local = positions.reshape(3, nblocks, TILE)
    qext = jnp.concatenate([qlocal, flux_rows(ext[:, nlocal:])], axis=1)
    nrow = qext.shape[0]
    twin = {}
    for d in range(3):
        twin[4 + 8 * d] = 46 + d
        twin[11 + 8 * d] = 49 + d
    keep = [r for r in range(nrow) if r not in twin]
    source = [keep.index(twin.get(r, r)) for r in range(nrow)]
    q_blocks = pick_rows(qext, keep).reshape(len(keep), EXT_BLOCKS, TILE)
    q_local_blocks = pick_rows(qlocal, keep).reshape(len(keep), nblocks, TILE)
    count = tile_count[0]
    tiles_total = tile_i.shape[0]
    batch = math.gcd(32, tiles_total)
    block_ids = jnp.arange(nblocks, dtype=jnp.int32)
    slots = jnp.arange(tiles_total, dtype=jnp.int32)
    key = jnp.where(slots < count, (tile_j >= nblocks).astype(jnp.int32), 2)
    first_n = jnp.sum((key == 0).astype(jnp.int32))
    second_n = jnp.sum((key == 1).astype(jnp.int32))
    rank = [jnp.cumsum((key == c).astype(jnp.int32)) - 1 for c in range(3)]
    dest = jnp.where(
        key == 0, rank[0], jnp.where(key == 1, first_n + rank[1], first_n + second_n + rank[2])
    )
    place = dest[None, :] == slots[:, None]
    pad = jnp.zeros((batch,), jnp.int32)
    list_i = jnp.concatenate([jnp.sum(jnp.where(place, tile_i[None, :], 0), axis=1), pad])
    list_j = jnp.concatenate([jnp.sum(jnp.where(place, tile_j[None, :], 0), axis=1), pad])
    split = first_n // batch * batch

    spots = jnp.arange(tiles_total + batch, dtype=jnp.int32)
    owner = list_i[None, :] == block_ids[:, None]
    onehots = {
        stop: (owner & (spots < bound)[None, :]).astype(jnp.float32)
        for stop, bound in (("split", split), ("count", count))
    }

    def batch_lists(offset, stop, clip):
        near_ids = lax.dynamic_slice_in_dim(list_i, offset, batch, 0)
        far_ids = lax.dynamic_slice_in_dim(list_j, offset, batch, 0)
        if clip:
            far_ids = jnp.minimum(far_ids, nblocks - 1)
        onehot = lax.dynamic_slice_in_dim(onehots[stop], offset, batch, 1)
        return (near_ids, far_ids, onehot)

    def fold_batch(acc, blocks, weight, far_ids, onehot):
        qsel = jnp.take(blocks, far_ids, axis=1)
        part = jnp.einsum(
            "rtb,tab->rta",
            qsel,
            weight,
            precision=lax.Precision.HIGH,
            preferred_element_type=jnp.float32,
        )
        return acc + jnp.einsum(
            "pt,rta->rpa",
            onehot,
            part,
            precision=lax.Precision.HIGHEST,
            preferred_element_type=jnp.float32,
        )

    bounds = {0: 0, "split": split, "count": count}

    def hydro_pass(first, stop, pos_far, blocks, carry, clip):
        start = bounds[first]

        def step(turn, carry):
            acc, stored = carry
            offset = start + turn * batch
            near_ids, far_ids, onehot = batch_lists(offset, stop, clip)
            near = jnp.take(pos_local, near_ids, axis=1)
            far = jnp.take(pos_far, far_ids, axis=1)
            weight = kernel_tile(near, far)
            stored = lax.dynamic_update_slice_in_dim(stored, weight, offset, 0)
            return (fold_batch(acc, blocks, weight, far_ids, onehot), stored)

        return lax.fori_loop(0, (bounds[stop] - start + batch - 1) // batch, step, carry)

    acc_start = jnp.zeros((len(keep), nblocks, TILE), jnp.float32)
    stored_start = jnp.zeros((tiles_total, TILE, TILE), jnp.float32)
    carry = hydro_pass(0, "split", pos_local, q_local_blocks, (acc_start, stored_start), True)
    acc, stored = hydro_pass("split", "count", pos_blocks, q_blocks, carry, False)
    acc = pick_rows(acc.reshape(len(keep), nlocal), source)
    rate, count_n = hydro_rate(acc, qlocal, ch)
    density_new = density + dt * rate[0]
    momentum_new = momentum + dt * rate[1:4]
    yzero = field + dt * rate[4:7]
    psi_new = (psi + dt * rate[7]) * jnp.exp(-damping * dt * ch)

    def diff_pass(first, stop, blocks, acc, clip):
        start = bounds[first]

        def step(turn, acc_diff):
            offset = start + turn * batch
            near_ids, far_ids, onehot = batch_lists(offset, stop, clip)
            weight = lax.dynamic_slice_in_dim(stored, offset, batch, 0)
            return fold_batch(acc_diff, blocks, weight, far_ids, onehot)

        return lax.fori_loop(0, (bounds[stop] - start + batch - 1) // batch, step, acc)

    def operator(bfl):
        eta = ohmic + fac * jnp.sum(bfl * bfl, axis=0)
        q_near = jnp.concatenate([bfl, eta[None] * bfl, eta[None]], axis=0)
        acc_diff = diff_pass(
            0, "split", q_near.reshape(7, nblocks, TILE), jnp.zeros((7, nblocks, TILE), jnp.float32), True
        )
        ghost_b = spread_ghosts(bfl, ghost_index)
        ghost_eta = ghosts[13] + ghosts[14] * jnp.sum(ghost_b * ghost_b, axis=0)
        b_ext = extend(bfl, ghost_b)
        eta_ext = extend(eta[None], ghost_eta[None])[0]
        qdiff = jnp.concatenate([b_ext, eta_ext[None] * b_ext, eta_ext[None]], axis=0)
        diff_blocks = qdiff.reshape(7, EXT_BLOCKS, TILE)
        acc_diff = diff_pass("split", "count", diff_blocks, acc_diff, False)
        return diffusion_rate(acc_diff.reshape(7, nlocal), bfl, eta, count_n)

    first, rows = rkl_table(SECTIONS)
    lzero = operator(yzero)
    older = yzero
    prev = yzero + first * dt * lzero
    for mu_j, nu_j, mut_j, gam_j in rows:
        nxt = (
            mu_j * prev
            + nu_j * older
            + (1.0 - mu_j - nu_j) * yzero
            + mut_j * dt * operator(prev)
            + gam_j * dt * lzero
        )
        older = prev
        prev = nxt
    return (density_new, momentum_new, prev, psi_new)


def solution(mesh):
    placed = (
        P(None, ("gx", "gy")),
        P(("gx", "gy")),
        P(None, ("gx", "gy")),
        P(None, ("gx", "gy")),
        P(("gx", "gy")),
        P(("gx", "gy")),
        P(("gx", "gy")),
        P(("gx", "gy")),
        P(("gx", "gy")),
        P(("gx", "gy")),
        P(("gx", "gy")),
    )
    return jax.shard_map(
        shards,
        mesh=mesh,
        in_specs=placed,
        out_specs=(P(("gx", "gy")), P(None, ("gx", "gy")), P(None, ("gx", "gy")), P(("gx", "gy"))),
        check_vma=False,
    )
```

```python
import math

import jax
import jax.numpy as jnp
from jax import lax
from jax.sharding import PartitionSpec as P

TILE = 128
SECTIONS = 4
GHOST_X = 320
GHOST_Y = 160
GHOST_C = 32
EXT_BLOCKS = 25


DIRECTIONS = [(-1, -1), (-1, 0), (-1, 1), (0, -1), (0, 1), (1, -1), (1, 0), (1, 1)]
courant = 0.3
damping = 0.5


def extended(array, sides, width):
    for axis, dim in sides:
        size, length = (lax.axis_size(axis), array.shape[dim])
        up = [(i, (i + 1) % size) for i in range(size - 1)]
        down = [(j, i) for i, j in up]
        last = lax.slice_in_dim(array, length - width, length, axis=dim)
        leading = lax.slice_in_dim(array, 0, width, axis=dim)
        before = lax.ppermute(last, axis, up)
        after = lax.ppermute(leading, axis, down)
        array = jnp.concatenate([before, array, after], axis=dim)
    return array


def ghost_sizes():
    return [GHOST_C, GHOST_X, GHOST_C, GHOST_Y, GHOST_Y, GHOST_C, GHOST_X, GHOST_C]


def ghost_offsets():
    sizes = ghost_sizes()
    starts = [0]
    for value in sizes[:-1]:
        starts.append(starts[-1] + value)
    return starts


def rkl_table(sections):
    wfirst = 4.0 / (sections * sections + sections - 2)
    bvals = [1.0 / 3.0, 1.0 / 3.0, 1.0 / 3.0] + [
        (j * j + j - 2) / (2.0 * j * (j + 1)) for j in range(3, sections + 1)
    ]
    first = bvals[1] * wfirst
    rows = []
    for j in range(2, sections + 1):
        mu_j = (2.0 * j - 1.0) / j * bvals[j] / bvals[j - 1]
        nu_j = -(j - 1.0) / j * bvals[j] / bvals[j - 2]
        mut_j = mu_j * wfirst
        rows.append((mu_j, nu_j, mut_j, -(1.0 - bvals[j - 1]) * mut_j))
    return (first, rows)


def kernel_tile(near, far):
    dist = (near[0][..., :, None] - far[0][..., None, :]) ** 2
    dist = dist + (near[1][..., :, None] - far[1][..., None, :]) ** 2
    dist = dist + (near[2][..., :, None] - far[2][..., None, :]) ** 2
    base = jnp.maximum(1.0 - 4.0 * dist, 0.0)
    return base * base


def flux_rows(ext):
    posit = ext[0:3]
    live = ext[3]
    rho = ext[4]
    vel = ext[5:8]
    bfl = ext[8:11]
    cpsi = ext[11]
    speed = ext[12]
    mom = rho * vel
    ptot = rho + 0.5 * jnp.sum(bfl * bfl, axis=0)
    fluxes = []
    for d in range(3):
        rows_d = [mom[d]]
        for k in range(3):
            term = mom[k] * vel[d] - bfl[k] * bfl[d]
            rows_d.append(term + ptot if k == d else term)
        for k in range(3):
            term = vel[d] * bfl[k] - bfl[d] * vel[k]
            rows_d.append(term + cpsi if k == d else term)
        rows_d.append(bfl[d])
        fluxes.append(jnp.stack(rows_d))
    flux = jnp.stack(fluxes)
    state = jnp.concatenate([rho[None], mom, bfl, cpsi[None]], axis=0)
    gsum = posit[0] * flux[0] + posit[1] * flux[1] + posit[2] * flux[2]
    return jnp.concatenate(
        [live[None], posit, flux.reshape(24, -1), gsum, speed * state, speed[None], state], axis=0
    )


def hydro_rate(acc, local, ch):
    count_n = acc[0]
    num = acc.shape[1]
    wflux = acc[4:28].reshape(3, 8, num)
    flux = local[4:28].reshape(3, 8, num)
    posit = local[1:4]
    speed = local[44]
    state = local[45:53]
    central = acc[28:36]
    for d in range(3):
        central = central + flux[d] * (acc[1 + d] - posit[d] * count_n) - posit[d] * wflux[d]
    central = jnp.concatenate([central[:7], (ch * ch) * central[7:8]], axis=0)
    dissip = speed * (acc[45:53] - state * count_n) + acc[36:44] - state * acc[44]
    return ((0.5 * dissip - 0.5 * central) / (1.0 + count_n), count_n)


def diffusion_rate(acc, bloc, etaloc, count_n):
    return 0.5 * (etaloc * (acc[0:3] - bloc * count_n) + acc[3:6] - bloc * acc[6]) / (1.0 + count_n)


def spread_ghosts(rows, ghost_index, extra=None):
    sizes = ghost_sizes()
    starts = ghost_offsets()
    width = max(sizes)
    nx, ny = (lax.axis_size("gx"), lax.axis_size("gy"))
    ix, iy = (lax.axis_index("gx"), lax.axis_index("gy"))
    sent = jnp.take(rows.T, ghost_index, axis=0).T
    segments = []
    for d in range(8):
        part = sent[:, starts[d] : starts[d] + sizes[d]]
        segments.append(jnp.pad(part, ((0, 0), (0, width - sizes[d]))))
    segments.append(jnp.zeros_like(segments[0]))
    segments = jnp.stack(segments)
    table = [8] * 9
    for d, (p, q) in enumerate(DIRECTIONS):
        table[(p + 1) * 3 + q + 1] = d
    peer = jnp.arange(nx * ny, dtype=jnp.int32)
    du = peer // ny - ix
    dv = peer % ny - iy
    near = (jnp.abs(du) <= 1) & (jnp.abs(dv) <= 1)
    code = jnp.clip((du + 1) * 3 + dv + 1, 0, 8)
    pick = jnp.where(near, jnp.array(table, jnp.int32)[code], 8)
    outgoing = jnp.take(segments, pick, axis=0)
    nrows = rows.shape[0]
    if extra is not None:
        tag = jnp.full((nx * ny, 1, width), extra, jnp.float32)
        outgoing = jnp.concatenate([outgoing, tag], axis=1)
    incoming = lax.all_to_all(outgoing, ("gx", "gy"), 0, 0, tiled=True)
    pieces = []
    for d, (p, q) in enumerate(DIRECTIONS):
        sx, sy = (ix + p, iy + q)
        inside = (sx >= 0) & (sx < nx) & (sy >= 0) & (sy < ny)
        source = jnp.clip(sx, 0, nx - 1) * ny + jnp.clip(sy, 0, ny - 1)
        block = lax.dynamic_index_in_dim(incoming, source, 0, keepdims=False)
        pieces.append(jnp.where(inside, block[:nrows, : sizes[d]], 0.0))
    ghosts = jnp.concatenate(pieces, axis=1)
    if extra is None:
        return ghosts
    return (ghosts, jnp.max(incoming[:, nrows, 0]))


def pick_rows(array, index):
    runs = []
    for r in index:
        if runs and runs[-1][1] == r:
            runs[-1][1] = r + 1
        else:
            runs.append([r, r + 1])
    return jnp.concatenate([array[a:b] for a, b in runs], axis=0)


def extend(rows, extra):
    filler = jnp.zeros(
        (rows.shape[0], EXT_BLOCKS * TILE - rows.shape[1] - extra.shape[1]), jnp.float32
    )
    return jnp.concatenate([rows, extra, filler], axis=1)


def shards(
    positions,
    density,
    momentum,
    field,
    psi,
    ohmic,
    ambipolar,
    ghost_index,
    tile_i,
    tile_j,
    tile_count,
):
    nlocal = density.shape[0]
    nblocks = nlocal // TILE
    velocity = momentum / density
    speed = jnp.sqrt(1.0 + jnp.sum(field * field, axis=0) / density)
    fac = ambipolar / (density * jnp.sqrt(density))
    live = jnp.ones_like(density)
    core_rows = [positions, live[None], density[None], velocity, field, psi[None], speed[None]]
    payload = jnp.concatenate(core_rows + [ohmic[None], fac[None]], axis=0)
    qlocal = flux_rows(payload)
    ghosts, ch = spread_ghosts(payload, ghost_index, jnp.max(speed))
    dt = courant / ch
    ext = extend(payload, ghosts)
    pos_blocks = ext[0:3].reshape(3, EXT_BLOCKS, TILE)
    pos_local = positions.reshape(3, nblocks, TILE)
    qext = jnp.concatenate([qlocal, flux_rows(ext[:, nlocal:])], axis=1)
    nrow = qext.shape[0]
    twin = {}
    for d in range(3):
        twin[4 + 8 * d] = 46 + d
        twin[11 + 8 * d] = 49 + d
    keep = [r for r in range(nrow) if r not in twin]
    source = [keep.index(twin.get(r, r)) for r in range(nrow)]
    q_blocks = pick_rows(qext, keep).reshape(len(keep), EXT_BLOCKS, TILE)
    q_local_blocks = pick_rows(qlocal, keep).reshape(len(keep), nblocks, TILE)
    count = tile_count[0]
    tiles_total = tile_i.shape[0]
    batch = math.gcd(32, tiles_total)
    block_ids = jnp.arange(nblocks, dtype=jnp.int32)
    slots = jnp.arange(tiles_total, dtype=jnp.int32)
    key = jnp.where(slots < count, (tile_j >= nblocks).astype(jnp.int32), 2)
    first_n = jnp.sum((key == 0).astype(jnp.int32))
    second_n = jnp.sum((key == 1).astype(jnp.int32))
    rank = [jnp.cumsum((key == c).astype(jnp.int32)) - 1 for c in range(3)]
    dest = jnp.where(
        key == 0, rank[0], jnp.where(key == 1, first_n + rank[1], first_n + second_n + rank[2])
    )
    place = dest[None, :] == slots[:, None]
    pad = jnp.zeros((batch,), jnp.int32)
    list_i = jnp.concatenate([jnp.sum(jnp.where(place, tile_i[None, :], 0), axis=1), pad])
    list_j = jnp.concatenate([jnp.sum(jnp.where(place, tile_j[None, :], 0), axis=1), pad])
    split = first_n // batch * batch

    spots = jnp.arange(tiles_total + batch, dtype=jnp.int32)
    owner = list_i[None, :] == block_ids[:, None]
    onehots = {
        stop: (owner & (spots < bound)[None, :]).astype(jnp.float32)
        for stop, bound in (("split", split), ("count", count))
    }

    def batch_lists(offset, stop, clip):
        near_ids = lax.dynamic_slice_in_dim(list_i, offset, batch, 0)
        far_ids = lax.dynamic_slice_in_dim(list_j, offset, batch, 0)
        if clip:
            far_ids = jnp.minimum(far_ids, nblocks - 1)
        onehot = lax.dynamic_slice_in_dim(onehots[stop], offset, batch, 1)
        return (near_ids, far_ids, onehot)

    def fold_batch(acc, blocks, weight, far_ids, onehot):
        qsel = jnp.take(blocks, far_ids, axis=1)
        part = jnp.einsum(
            "rtb,tab->rta",
            qsel,
            weight,
            precision=lax.Precision.HIGH,
            preferred_element_type=jnp.float32,
        )
        return acc + jnp.einsum(
            "pt,rta->rpa",
            onehot,
            part,
            precision=lax.Precision.HIGH,
            preferred_element_type=jnp.float32,
        )

    bounds = {0: 0, "split": split, "count": count}

    def hydro_pass(first, stop, pos_far, blocks, carry, clip):
        start = bounds[first]

        def step(turn, carry):
            acc, stored = carry
            offset = start + turn * batch
            near_ids, far_ids, onehot = batch_lists(offset, stop, clip)
            near = jnp.take(pos_local, near_ids, axis=1)
            far = jnp.take(pos_far, far_ids, axis=1)
            weight = kernel_tile(near, far)
            stored = lax.dynamic_update_slice_in_dim(stored, weight, offset, 0)
            return (fold_batch(acc, blocks, weight, far_ids, onehot), stored)

        return lax.fori_loop(0, (bounds[stop] - start + batch - 1) // batch, step, carry)

    acc_start = jnp.zeros((len(keep), nblocks, TILE), jnp.float32)
    stored_start = jnp.zeros((tiles_total, TILE, TILE), jnp.float32)
    carry = hydro_pass(0, "split", pos_local, q_local_blocks, (acc_start, stored_start), True)
    acc, stored = hydro_pass("split", "count", pos_blocks, q_blocks, carry, False)
    acc = pick_rows(acc.reshape(len(keep), nlocal), source)
    rate, count_n = hydro_rate(acc, qlocal, ch)
    density_new = density + dt * rate[0]
    momentum_new = momentum + dt * rate[1:4]
    yzero = field + dt * rate[4:7]
    psi_new = (psi + dt * rate[7]) * jnp.exp(-damping * dt * ch)

    def diff_pass(first, stop, blocks, acc, clip):
        start = bounds[first]

        def step(turn, acc_diff):
            offset = start + turn * batch
            near_ids, far_ids, onehot = batch_lists(offset, stop, clip)
            weight = lax.dynamic_slice_in_dim(stored, offset, batch, 0)
            return fold_batch(acc_diff, blocks, weight, far_ids, onehot)

        return lax.fori_loop(0, (bounds[stop] - start + batch - 1) // batch, step, acc)

    def operator(bfl):
        eta = ohmic + fac * jnp.sum(bfl * bfl, axis=0)
        q_near = jnp.concatenate([bfl, eta[None] * bfl, eta[None]], axis=0)
        acc_diff = diff_pass(
            0, "split", q_near.reshape(7, nblocks, TILE), jnp.zeros((7, nblocks, TILE), jnp.float32), True
        )
        ghost_b = spread_ghosts(bfl, ghost_index)
        ghost_eta = ghosts[13] + ghosts[14] * jnp.sum(ghost_b * ghost_b, axis=0)
        b_ext = extend(bfl, ghost_b)
        eta_ext = extend(eta[None], ghost_eta[None])[0]
        qdiff = jnp.concatenate([b_ext, eta_ext[None] * b_ext, eta_ext[None]], axis=0)
        diff_blocks = qdiff.reshape(7, EXT_BLOCKS, TILE)
        acc_diff = diff_pass("split", "count", diff_blocks, acc_diff, False)
        return diffusion_rate(acc_diff.reshape(7, nlocal), bfl, eta, count_n)

    first, rows = rkl_table(SECTIONS)
    lzero = operator(yzero)
    older = yzero
    prev = yzero + first * dt * lzero
    for mu_j, nu_j, mut_j, gam_j in rows:
        nxt = (
            mu_j * prev
            + nu_j * older
            + (1.0 - mu_j - nu_j) * yzero
            + mut_j * dt * operator(prev)
            + gam_j * dt * lzero
        )
        older = prev
        prev = nxt
    return (density_new, momentum_new, prev, psi_new)


def solution(mesh):
    placed = (
        P(None, ("gx", "gy")),
        P(("gx", "gy")),
        P(None, ("gx", "gy")),
        P(None, ("gx", "gy")),
        P(("gx", "gy")),
        P(("gx", "gy")),
        P(("gx", "gy")),
        P(("gx", "gy")),
        P(("gx", "gy")),
        P(("gx", "gy")),
        P(("gx", "gy")),
    )
    return jax.shard_map(
        shards,
        mesh=mesh,
        in_specs=placed,
        out_specs=(P(("gx", "gy")), P(None, ("gx", "gy")), P(None, ("gx", "gy")), P(("gx", "gy"))),
        check_vma=False,
    )
```

```python
import math

import jax
import jax.numpy as jnp
from jax import lax
from jax.sharding import PartitionSpec as P

TILE = 128
SECTIONS = 4
GHOST_X = 320
GHOST_Y = 160
GHOST_C = 32
EXT_BLOCKS = 25


DIRECTIONS = [(-1, -1), (-1, 0), (-1, 1), (0, -1), (0, 1), (1, -1), (1, 0), (1, 1)]
courant = 0.3
damping = 0.5


def extended(array, sides, width):
    for axis, dim in sides:
        size, length = (lax.axis_size(axis), array.shape[dim])
        up = [(i, (i + 1) % size) for i in range(size - 1)]
        down = [(j, i) for i, j in up]
        last = lax.slice_in_dim(array, length - width, length, axis=dim)
        leading = lax.slice_in_dim(array, 0, width, axis=dim)
        before = lax.ppermute(last, axis, up)
        after = lax.ppermute(leading, axis, down)
        array = jnp.concatenate([before, array, after], axis=dim)
    return array


def ghost_sizes():
    return [GHOST_C, GHOST_X, GHOST_C, GHOST_Y, GHOST_Y, GHOST_C, GHOST_X, GHOST_C]


def ghost_offsets():
    sizes = ghost_sizes()
    starts = [0]
    for value in sizes[:-1]:
        starts.append(starts[-1] + value)
    return starts


def rkl_table(sections):
    wfirst = 4.0 / (sections * sections + sections - 2)
    bvals = [1.0 / 3.0, 1.0 / 3.0, 1.0 / 3.0] + [
        (j * j + j - 2) / (2.0 * j * (j + 1)) for j in range(3, sections + 1)
    ]
    first = bvals[1] * wfirst
    rows = []
    for j in range(2, sections + 1):
        mu_j = (2.0 * j - 1.0) / j * bvals[j] / bvals[j - 1]
        nu_j = -(j - 1.0) / j * bvals[j] / bvals[j - 2]
        mut_j = mu_j * wfirst
        rows.append((mu_j, nu_j, mut_j, -(1.0 - bvals[j - 1]) * mut_j))
    return (first, rows)


def kernel_tile(near, far):
    dist = (near[0][..., :, None] - far[0][..., None, :]) ** 2
    dist = dist + (near[1][..., :, None] - far[1][..., None, :]) ** 2
    dist = dist + (near[2][..., :, None] - far[2][..., None, :]) ** 2
    base = jnp.maximum(1.0 - 4.0 * dist, 0.0)
    return base * base


def flux_rows(ext):
    posit = ext[0:3]
    live = ext[3]
    rho = ext[4]
    vel = ext[5:8]
    bfl = ext[8:11]
    cpsi = ext[11]
    speed = ext[12]
    mom = rho * vel
    ptot = rho + 0.5 * jnp.sum(bfl * bfl, axis=0)
    fluxes = []
    for d in range(3):
        rows_d = [mom[d]]
        for k in range(3):
            term = mom[k] * vel[d] - bfl[k] * bfl[d]
            rows_d.append(term + ptot if k == d else term)
        for k in range(3):
            term = vel[d] * bfl[k] - bfl[d] * vel[k]
            rows_d.append(term + cpsi if k == d else term)
        rows_d.append(bfl[d])
        fluxes.append(jnp.stack(rows_d))
    flux = jnp.stack(fluxes)
    state = jnp.concatenate([rho[None], mom, bfl, cpsi[None]], axis=0)
    gsum = posit[0] * flux[0] + posit[1] * flux[1] + posit[2] * flux[2]
    return jnp.concatenate(
        [live[None], posit, flux.reshape(24, -1), gsum, speed * state, speed[None], state], axis=0
    )


def hydro_rate(acc, local, ch):
    count_n = acc[0]
    num = acc.shape[1]
    wflux = acc[4:28].reshape(3, 8, num)
    flux = local[4:28].reshape(3, 8, num)
    posit = local[1:4]
    speed = local[44]
    state = local[45:53]
    central = acc[28:36]
    for d in range(3):
        central = central + flux[d] * (acc[1 + d] - posit[d] * count_n) - posit[d] * wflux[d]
    central = jnp.concatenate([central[:7], (ch * ch) * central[7:8]], axis=0)
    dissip = speed * (acc[45:53] - state * count_n) + acc[36:44] - state * acc[44]
    return ((0.5 * dissip - 0.5 * central) / (1.0 + count_n), count_n)


def diffusion_rate(acc, bloc, etaloc, count_n):
    return 0.5 * (etaloc * (acc[0:3] - bloc * count_n) + acc[3:6] - bloc * acc[6]) / (1.0 + count_n)


def spread_ghosts(rows, ghost_index, extra=None):
    sizes = ghost_sizes()
    starts = ghost_offsets()
    width = max(sizes)
    nx, ny = (lax.axis_size("gx"), lax.axis_size("gy"))
    ix, iy = (lax.axis_index("gx"), lax.axis_index("gy"))
    sent = jnp.take(rows.T, ghost_index, axis=0).T
    segments = []
    for d in range(8):
        part = sent[:, starts[d] : starts[d] + sizes[d]]
        segments.append(jnp.pad(part, ((0, 0), (0, width - sizes[d]))))
    segments.append(jnp.zeros_like(segments[0]))
    segments = jnp.stack(segments)
    table = [8] * 9
    for d, (p, q) in enumerate(DIRECTIONS):
        table[(p + 1) * 3 + q + 1] = d
    peer = jnp.arange(nx * ny, dtype=jnp.int32)
    du = peer // ny - ix
    dv = peer % ny - iy
    near = (jnp.abs(du) <= 1) & (jnp.abs(dv) <= 1)
    code = jnp.clip((du + 1) * 3 + dv + 1, 0, 8)
    pick = jnp.where(near, jnp.array(table, jnp.int32)[code], 8)
    outgoing = jnp.take(segments, pick, axis=0)
    nrows = rows.shape[0]
    if extra is not None:
        tag = jnp.full((nx * ny, 1, width), extra, jnp.float32)
        outgoing = jnp.concatenate([outgoing, tag], axis=1)
    incoming = lax.all_to_all(outgoing, ("gx", "gy"), 0, 0, tiled=True)
    pieces = []
    for d, (p, q) in enumerate(DIRECTIONS):
        sx, sy = (ix + p, iy + q)
        inside = (sx >= 0) & (sx < nx) & (sy >= 0) & (sy < ny)
        source = jnp.clip(sx, 0, nx - 1) * ny + jnp.clip(sy, 0, ny - 1)
        block = lax.dynamic_index_in_dim(incoming, source, 0, keepdims=False)
        pieces.append(jnp.where(inside, block[:nrows, : sizes[d]], 0.0))
    ghosts = jnp.concatenate(pieces, axis=1)
    if extra is None:
        return ghosts
    return (ghosts, jnp.max(incoming[:, nrows, 0]))


def pick_rows(array, index):
    runs = []
    for r in index:
        if runs and runs[-1][1] == r:
            runs[-1][1] = r + 1
        else:
            runs.append([r, r + 1])
    return jnp.concatenate([array[a:b] for a, b in runs], axis=0)


def extend(rows, extra):
    filler = jnp.zeros(
        (rows.shape[0], EXT_BLOCKS * TILE - rows.shape[1] - extra.shape[1]), jnp.float32
    )
    return jnp.concatenate([rows, extra, filler], axis=1)


def shards(
    positions,
    density,
    momentum,
    field,
    psi,
    ohmic,
    ambipolar,
    ghost_index,
    tile_i,
    tile_j,
    tile_count,
):
    nlocal = density.shape[0]
    nblocks = nlocal // TILE
    velocity = momentum / density
    speed = jnp.sqrt(1.0 + jnp.sum(field * field, axis=0) / density)
    fac = ambipolar / (density * jnp.sqrt(density))
    live = jnp.ones_like(density)
    core_rows = [positions, live[None], density[None], velocity, field, psi[None], speed[None]]
    payload = jnp.concatenate(core_rows + [ohmic[None], fac[None]], axis=0)
    qlocal = flux_rows(payload)
    sendable = jnp.concatenate([payload[0:3], payload[4:12], payload[13:15]], axis=0)
    got, ch = spread_ghosts(sendable, ghost_index, jnp.max(speed))
    real = got[3] > 0.0
    safe_rho = jnp.where(real, got[3], 1.0)
    ghost_speed = jnp.where(real, jnp.sqrt(1.0 + jnp.sum(got[7:10] * got[7:10], axis=0) / safe_rho), 0.0)
    ghosts = jnp.concatenate(
        [got[0:3], real.astype(jnp.float32)[None], got[3:11], ghost_speed[None], got[11:13]], axis=0
    )
    dt = courant / ch
    ext = extend(payload, ghosts)
    pos_blocks = ext[0:3].reshape(3, EXT_BLOCKS, TILE)
    pos_local = positions.reshape(3, nblocks, TILE)
    qext = jnp.concatenate([qlocal, flux_rows(ext[:, nlocal:])], axis=1)
    nrow = qext.shape[0]
    twin = {}
    for d in range(3):
        twin[4 + 8 * d] = 46 + d
        twin[11 + 8 * d] = 49 + d
    keep = [r for r in range(nrow) if r not in twin]
    source = [keep.index(twin.get(r, r)) for r in range(nrow)]
    q_blocks = pick_rows(qext, keep).reshape(len(keep), EXT_BLOCKS, TILE)
    q_local_blocks = pick_rows(qlocal, keep).reshape(len(keep), nblocks, TILE)
    count = tile_count[0]
    tiles_total = tile_i.shape[0]
    batch = math.gcd(32, tiles_total)
    block_ids = jnp.arange(nblocks, dtype=jnp.int32)
    slots = jnp.arange(tiles_total, dtype=jnp.int32)
    key = jnp.where(slots < count, (tile_j >= nblocks).astype(jnp.int32), 2)
    first_n = jnp.sum((key == 0).astype(jnp.int32))
    second_n = jnp.sum((key == 1).astype(jnp.int32))
    rank = [jnp.cumsum((key == c).astype(jnp.int32)) - 1 for c in range(3)]
    dest = jnp.where(
        key == 0, rank[0], jnp.where(key == 1, first_n + rank[1], first_n + second_n + rank[2])
    )
    place = dest[None, :] == slots[:, None]
    pad = jnp.zeros((batch,), jnp.int32)
    list_i = jnp.concatenate([jnp.sum(jnp.where(place, tile_i[None, :], 0), axis=1), pad])
    list_j = jnp.concatenate([jnp.sum(jnp.where(place, tile_j[None, :], 0), axis=1), pad])
    split = first_n // batch * batch

    spots = jnp.arange(tiles_total + batch, dtype=jnp.int32)
    owner = list_i[None, :] == block_ids[:, None]
    onehots = {
        stop: (owner & (spots < bound)[None, :]).astype(jnp.float32)
        for stop, bound in (("split", split), ("count", count))
    }

    def batch_lists(offset, stop, clip):
        near_ids = lax.dynamic_slice_in_dim(list_i, offset, batch, 0)
        far_ids = lax.dynamic_slice_in_dim(list_j, offset, batch, 0)
        if clip:
            far_ids = jnp.minimum(far_ids, nblocks - 1)
        onehot = lax.dynamic_slice_in_dim(onehots[stop], offset, batch, 1)
        return (near_ids, far_ids, onehot)

    def fold_batch(acc, blocks, weight, far_ids, onehot):
        qsel = jnp.take(blocks, far_ids, axis=1)
        part = jnp.einsum(
            "rtb,tab->rta",
            qsel,
            weight,
            precision=lax.Precision.HIGH,
            preferred_element_type=jnp.float32,
        )
        return acc + jnp.einsum(
            "pt,rta->rpa",
            onehot,
            part,
            precision=lax.Precision.HIGHEST,
            preferred_element_type=jnp.float32,
        )

    bounds = {0: 0, "split": split, "count": count}

    def hydro_pass(first, stop, pos_far, blocks, carry, clip):
        start = bounds[first]

        def step(turn, carry):
            acc, stored = carry
            offset = start + turn * batch
            near_ids, far_ids, onehot = batch_lists(offset, stop, clip)
            near = jnp.take(pos_local, near_ids, axis=1)
            far = jnp.take(pos_far, far_ids, axis=1)
            weight = kernel_tile(near, far)
            stored = lax.dynamic_update_slice_in_dim(stored, weight, offset, 0)
            return (fold_batch(acc, blocks, weight, far_ids, onehot), stored)

        return lax.fori_loop(0, (bounds[stop] - start + batch - 1) // batch, step, carry)

    acc_start = jnp.zeros((len(keep), nblocks, TILE), jnp.float32)
    stored_start = jnp.zeros((tiles_total, TILE, TILE), jnp.float32)
    carry = hydro_pass(0, "split", pos_local, q_local_blocks, (acc_start, stored_start), True)
    acc, stored = hydro_pass("split", "count", pos_blocks, q_blocks, carry, False)
    acc = pick_rows(acc.reshape(len(keep), nlocal), source)
    rate, count_n = hydro_rate(acc, qlocal, ch)
    density_new = density + dt * rate[0]
    momentum_new = momentum + dt * rate[1:4]
    yzero = field + dt * rate[4:7]
    psi_new = (psi + dt * rate[7]) * jnp.exp(-damping * dt * ch)

    def diff_pass(first, stop, blocks, acc, clip):
        start = bounds[first]

        def step(turn, acc_diff):
            offset = start + turn * batch
            near_ids, far_ids, onehot = batch_lists(offset, stop, clip)
            weight = lax.dynamic_slice_in_dim(stored, offset, batch, 0)
            return fold_batch(acc_diff, blocks, weight, far_ids, onehot)

        return lax.fori_loop(0, (bounds[stop] - start + batch - 1) // batch, step, acc)

    def operator(bfl):
        eta = ohmic + fac * jnp.sum(bfl * bfl, axis=0)
        q_near = jnp.concatenate([bfl, eta[None] * bfl, eta[None]], axis=0)
        acc_diff = diff_pass(
            0, "split", q_near.reshape(7, nblocks, TILE), jnp.zeros((7, nblocks, TILE), jnp.float32), True
        )
        ghost_b = spread_ghosts(bfl, ghost_index)
        ghost_eta = ghosts[13] + ghosts[14] * jnp.sum(ghost_b * ghost_b, axis=0)
        b_ext = extend(bfl, ghost_b)
        eta_ext = extend(eta[None], ghost_eta[None])[0]
        qdiff = jnp.concatenate([b_ext, eta_ext[None] * b_ext, eta_ext[None]], axis=0)
        diff_blocks = qdiff.reshape(7, EXT_BLOCKS, TILE)
        acc_diff = diff_pass("split", "count", diff_blocks, acc_diff, False)
        return diffusion_rate(acc_diff.reshape(7, nlocal), bfl, eta, count_n)

    first, rows = rkl_table(SECTIONS)
    lzero = operator(yzero)
    older = yzero
    prev = yzero + first * dt * lzero
    for mu_j, nu_j, mut_j, gam_j in rows:
        nxt = (
            mu_j * prev
            + nu_j * older
            + (1.0 - mu_j - nu_j) * yzero
            + mut_j * dt * operator(prev)
            + gam_j * dt * lzero
        )
        older = prev
        prev = nxt
    return (density_new, momentum_new, prev, psi_new)


def solution(mesh):
    placed = (
        P(None, ("gx", "gy")),
        P(("gx", "gy")),
        P(None, ("gx", "gy")),
        P(None, ("gx", "gy")),
        P(("gx", "gy")),
        P(("gx", "gy")),
        P(("gx", "gy")),
        P(("gx", "gy")),
        P(("gx", "gy")),
        P(("gx", "gy")),
        P(("gx", "gy")),
    )
    return jax.shard_map(
        shards,
        mesh=mesh,
        in_specs=placed,
        out_specs=(P(("gx", "gy")), P(None, ("gx", "gy")), P(None, ("gx", "gy")), P(("gx", "gy"))),
        check_vma=False,
    )
```
